32 devices in a mesh: fsdp: 8 (over z, y), rows: 4 (over x, core).
Axes of the slice: x: 2, y: 2, z: 4, core: 2. Of those that a mesh axis runs over, the one named last changes fastest.
Arguments:
- frames: bfloat16 [8, 12, 16, 1536], P('fsdp', 'rows'), may hold values from -6 to 6
- kernel: float32 [7, 7, 1536], replicated, may hold values from -0.875 to 0.875
- kernel_bias: float32 [1536], replicated, may hold values from -3 to 3
- layer_norm_weight: float32 [1536], replicated, may hold values from 0.25 to 1.75
- layer_norm_bias: float32 [1536], replicated, may hold values from -3 to 3
- up_weight: bfloat16 [1536, 6144], P('fsdp', 'rows'), may hold values from -1 to 1, as said below
- up_bias: float32 [6144], P('rows'), may hold values from -3 to 3
- grn_gamma: float32 [6144], P('rows'), may hold values from 0.2 to 1
- grn_beta: float32 [6144], P('rows'), may hold values from -3 to 3
- grad_out: bfloat16 [8, 12, 16, 6144], P('fsdp', None, None, 'rows'), may hold values from -8 to 8, as said below
Outputs:
- activation: bfloat16 [8, 12, 16, 6144], P('fsdp', None, None, 'rows')
- frames_grad: bfloat16 [8, 12, 16, 1536], P('fsdp', 'rows')
- up_weight_grad: float32 [1536, 6144], P('fsdp', 'rows')
- kernel_grad: float32 [7, 7, 1536], replicated
The draws below stay inside these ranges and needn't reach their ends.
Inputs may be any that keep to these rules, and one draw needn't show every extreme that they name: `up_weight`: entries lie within the bounds. `grad_out`: entries lie within the bounds.
All inputs are finite; a program needn't handle non-finite values.
Results may differ from the reference program's by a relative error of at most 0.014.
Values may be sent and summed in bfloat16 or wider, within the bound.
No kernel may reach another device: no remote copies, remote signals or barrier semaphores. Data moves between devices by JAX's collectives and lax.ppermute only.
A program may use at most 64 MiB of HBM per device.

```python
import math
import jax
import jax.numpy as jnp
from jax import lax

C = 1536
FF = 6144
KS = 7
WIDTH = 16
HEIGHT = 12
FRAMES = 8
N_ROWS = 4


def draw_up_weight(key, part):
    key_base, key_scale = jax.random.split(jax.random.fold_in(key, 11))
    position = jnp.arange(FF, dtype=jnp.float32) / FF
    spread = jnp.exp(jax.random.uniform(key_scale, (FF,), jnp.float32, math.log(0.5), math.log(2.0)))
    base = jnp.clip(jax.random.normal(key_base, (C, FF), jnp.float32), -4.0, 4.0)
    rising = jnp.power(3.0, position) / 1.82
    values = base * spread * rising / math.sqrt(C)
    return jnp.clip(values, -1.0, 1.0).astype(jnp.bfloat16)


def draw_grad_out(key, part):
    key_noise, key_mean = jax.random.split(jax.random.fold_in(key, 23), 2)
    position = jnp.arange(FF, dtype=jnp.float32) / FF
    jitter = jax.random.uniform(key_mean, (FF,), jnp.float32, 0.6, 1.4)
    noise = jnp.clip(jax.random.normal(key_noise, (FRAMES, HEIGHT, WIDTH, FF), jnp.float32), -5.0, 5.0)
    level = 0.06 * jnp.power(6.0, position) * jitter
    values = noise + level
    return jnp.clip(values, -8.0, 8.0).astype(jnp.bfloat16)


def shard_levels(rng, dims, cuts, smallest, high):
    def one(dim, blocks):
        draws = jax.random.uniform(jax.random.fold_in(jax.random.fold_in(rng, 6), dim), (blocks,), jnp.float32, smallest / len(cuts), high / len(cuts))
        return jnp.repeat(jnp.exp(draws), dims[dim] // blocks).reshape((-1,) + (1,) * (len(dims) - dim - 1))

    level = one(*cuts[0])
    for cut in cuts[1:]:
        level = level * one(*cut)
    return level


def bell_draw(key, dims, deviation, reach, cuts=(), kind=jnp.bfloat16):
    values = jax.random.normal(key, dims, jnp.float32) * deviation
    if len(cuts) > 0:
        values = shard_levels(key, dims, cuts, -0.22, 0.18) * values
    return jnp.clip(values, min=-reach, max=reach).astype(kind)


def setup_inputs(seed: int = 0) -> dict:
    keys = jax.random.split(jax.random.key(seed), 11)
    return {
        "frames": bell_draw(keys[0], (FRAMES, HEIGHT, WIDTH, C), 1.0, 6.0, ((0, 8), (1, 4))),
        "kernel": bell_draw(keys[1], (KS, KS, C), (KS * KS) ** -0.5, 0.875, (), jnp.float32),
        "kernel_bias": bell_draw(keys[2], (C,), 0.5, 3.0, (), jnp.float32),
        "layer_norm_weight": jnp.clip(1.0 + 0.15 * jax.random.normal(keys[3], (C,), jnp.float32), 0.25, 1.75),
        "layer_norm_bias": bell_draw(keys[4], (C,), 0.5, 3.0, (), jnp.float32),
        "up_weight": draw_up_weight(jax.random.fold_in(keys[10], 71), 0),
        "up_bias": bell_draw(keys[6], (FF,), 0.5, 3.0, ((0, 4),), jnp.float32),
        "grn_gamma": jnp.clip(jnp.exp(math.log(1.0) - 1.609438 * jax.random.uniform(keys[7], (FF,), jnp.float32) ** shard_levels(keys[7], (FF,), ((0, 4),), -0.2, 0.2)), 0.2, 1.0),
        "grn_beta": bell_draw(keys[8], (FF,), 0.5, 3.0, ((0, 4),), jnp.float32),
        "grad_out": draw_grad_out(jax.random.fold_in(keys[10], 71), 0),
    }


def conv_rows(framed, kern, kbias):
    rows = framed.shape[0] - 6
    cols = framed.shape[1]
    wide = jnp.pad(framed, ((0, 0), (3, 3), (0, 0)))
    total = jnp.zeros((rows, cols, framed.shape[2]), jnp.float32) + kbias
    for i in range(kern.shape[0]):
        for j in range(kern.shape[1]):
            total = total + wide[i:i + rows, j:j + cols].astype(jnp.float32) * kern[i, j]
    return total

def back_conv(grad_pad, kern):
    rows = grad_pad.shape[0] - 6
    cols = grad_pad.shape[1]
    wide = jnp.pad(grad_pad, ((0, 0), (3, 3), (0, 0)))
    total = jnp.zeros((rows, cols, grad_pad.shape[2]), jnp.float32)
    for i in range(kern.shape[0]):
        for j in range(kern.shape[1]):
            total = total + wide[6 - i:6 - i + rows, 6 - j:6 - j + cols].astype(jnp.float32) * kern[i, j]
    return total

def kern_grad(framed, grad_rows):
    rows = grad_rows.shape[0]
    cols = grad_rows.shape[1]
    wide = jnp.pad(framed, ((0, 0), (3, 3), (0, 0)))
    grad_f = grad_rows.astype(jnp.float32)
    parts = []
    for i in range(7):
        for j in range(7):
            parts.append(lax.optimization_barrier(jnp.sum(wide[i:i + rows, j:j + cols].astype(jnp.float32) * grad_f, axis=(0, 1))))
    return jnp.stack(parts).reshape(7, 7, grad_rows.shape[2])

def apply_layer_norm(activation_rows, scale_factor, offset_bias):
    centered_input = activation_rows - lax.optimization_barrier(jnp.mean(activation_rows, axis=-1, keepdims=True))
    inverse_deviation = lax.rsqrt(lax.optimization_barrier(jnp.mean(centered_input * centered_input, axis=-1, keepdims=True)) + 1e-06)
    standardized_input = centered_input * inverse_deviation
    return ((standardized_input * scale_factor + offset_bias).astype(jnp.bfloat16), standardized_input, inverse_deviation)

def gelu_grad(value):
    return 0.5 * (1.0 + jax.scipy.special.erf(value * 0.7071067811865476)) + value * jnp.exp(-0.5 * value * value) * 0.3989422804014327

def reference(frames, kernel, kernel_bias, layer_norm_weight, layer_norm_bias, up_weight, up_bias, grn_gamma, grn_beta, grad_out):
    chans = frames.shape[3]
    weight_groups = up_weight.reshape(chans, N_ROWS, -1).astype(jnp.float32)

    def one_frame(carry, item):
        w_acc, k_acc = carry
        slab, cot = item
        rim = jnp.zeros((3,) + slab.shape[1:], slab.dtype)
        framed = jnp.concatenate([rim, slab, rim], 0)
        activation_rows = conv_rows(framed, kernel, kernel_bias)
        normed_output, standardized_input, inverse_deviation = apply_layer_norm(activation_rows, layer_norm_weight, layer_norm_bias)
        flat = normed_output.reshape(-1, chans)
        pre = jnp.dot(flat, up_weight, preferred_element_type=jnp.float32) + up_bias
        post = jax.nn.gelu(pre, approximate=False)
        norms = jnp.sqrt(lax.optimization_barrier(jnp.sum(post * post, axis=0)) + 1e-06)
        denom = jnp.sum(norms) / FF + 1e-06
        ratio = norms / denom
        output = (grn_gamma * (post * ratio) + grn_beta + post).astype(jnp.bfloat16)
        cot_f = cot.reshape(-1, FF).astype(jnp.float32)
        dnorm = grn_gamma * lax.optimization_barrier(jnp.sum(cot_f * post, axis=0))
        cross = jnp.sum(dnorm * norms)
        dnorms = dnorm / denom - cross / (denom * denom) / FF
        dpost = cot_f * (1.0 + grn_gamma * ratio) + post * (dnorms / norms)
        dpre = (dpost * gelu_grad(pre)).astype(jnp.bfloat16)
        w_term = lax.dot_general(flat, dpre, (((0,), (0,)), ((), ())), preferred_element_type=jnp.float32).astype(jnp.bfloat16)
        w_acc = w_acc + lax.optimization_barrier(w_term).astype(jnp.float32)
        groups = jnp.einsum('tns,cns->ntc', dpre.reshape(flat.shape[0], N_ROWS, -1).astype(jnp.float32), weight_groups).astype(jnp.bfloat16)
        normed_input_gradient = lax.optimization_barrier(jnp.sum(lax.optimization_barrier(groups).astype(jnp.float32), axis=0)).reshape(activation_rows.shape)
        scaled_output = normed_input_gradient * layer_norm_weight
        activation_gradient = (inverse_deviation * (scaled_output - lax.optimization_barrier(jnp.mean(scaled_output, axis=-1, keepdims=True)) - standardized_input * lax.optimization_barrier(jnp.mean(scaled_output * standardized_input, axis=-1, keepdims=True)))).astype(jnp.bfloat16)
        grad_rim = jnp.zeros((3,) + activation_gradient.shape[1:], activation_gradient.dtype)
        grad_pad = jnp.concatenate([grad_rim, activation_gradient, grad_rim], 0)
        dframe = back_conv(grad_pad, kernel).astype(jnp.bfloat16)
        k_acc = k_acc + kern_grad(framed, activation_gradient)
        return ((w_acc, k_acc), (output.reshape(slab.shape[0], slab.shape[1], FF), dframe))
    init = (jnp.zeros((chans, FF), jnp.float32), jnp.zeros(kernel.shape, jnp.float32))
    (w_acc, k_acc), (outputs, dframes) = lax.scan(one_frame, init, (frames, grad_out))
    return (outputs, dframes, w_acc, k_acc)
```

```python
import jax
import jax.numpy as jnp
from jax import lax
from jax.sharding import PartitionSpec as P

FF = 6144


def extended(block, sides, width):
    for axis, dim in sides:
        count = lax.axis_size(axis)
        forward = [(i, i + 1) for i in range(count - 1)]
        backward = [(target, source) for source, target in forward]
        low = lax.ppermute(
            lax.slice_in_dim(block, block.shape[dim] - width, None, axis=dim), axis, forward
        )
        high = lax.ppermute(lax.slice_in_dim(block, 0, width, axis=dim), axis, backward)
        block = jnp.concatenate([low, block, high], axis=dim)
    return block


def _bit_steps(axes):
    steps = []
    for axis in axes:
        size = lax.axis_size(axis)
        assert size & (size - 1) == 0
        mask = 1
        while mask < size:
            steps.append((axis, mask, size))
            mask *= 2
    return steps


def tree_allreduce(value, axes):
    shape = value.shape
    flat = value.reshape(-1)
    steps = _bit_steps(axes)
    assert flat.shape[0] % (1 << len(steps)) == 0
    bits = []
    for axis, mask, size in steps:
        bit = (lax.axis_index(axis) // mask) % 2
        bits.append(bit)
        halves = flat.reshape(2, -1)
        keep = lax.dynamic_index_in_dim(halves, bit, keepdims=False)
        give = lax.dynamic_index_in_dim(halves, 1 - bit, keepdims=False)
        perm = [(j, j ^ mask) for j in range(size)]
        flat = keep + lax.ppermute(give, axis, perm)
    for (axis, mask, size), bit in reversed(list(zip(steps, bits))):
        perm = [(j, j ^ mask) for j in range(size)]
        other = lax.ppermute(flat, axis, perm)
        flat = jnp.where(bit == 0, jnp.concatenate([flat, other]), jnp.concatenate([other, flat]))
    return flat.reshape(shape)


def conv_rows(framed, kern, kbias):
    rows = framed.shape[0] - 6
    cols = framed.shape[1]
    wide = jnp.pad(framed, ((0, 0), (3, 3), (0, 0)))
    total = jnp.zeros((rows, cols, framed.shape[2]), jnp.float32) + kbias
    for i in range(kern.shape[0]):
        for j in range(kern.shape[1]):
            total = total + wide[i : i + rows, j : j + cols].astype(jnp.float32) * kern[i, j]
    return total


def back_conv(grad_pad, kern):
    rows = grad_pad.shape[0] - 6
    cols = grad_pad.shape[1]
    wide = jnp.pad(grad_pad, ((0, 0), (3, 3), (0, 0)))
    total = jnp.zeros((rows, cols, grad_pad.shape[2]), jnp.float32)
    for i in range(kern.shape[0]):
        for j in range(kern.shape[1]):
            total = (
                total
                + wide[6 - i : 6 - i + rows, 6 - j : 6 - j + cols].astype(jnp.float32) * kern[i, j]
            )
    return total


def kern_grad(framed, grad_rows):
    rows = grad_rows.shape[0]
    cols = grad_rows.shape[1]
    wide = jnp.pad(framed, ((0, 0), (3, 3), (0, 0)))
    grad_f = grad_rows.astype(jnp.float32)
    parts = []
    for i in range(7):
        for j in range(7):
            parts.append(
                jnp.sum(wide[i : i + rows, j : j + cols].astype(jnp.float32) * grad_f, axis=(0, 1))
            )
    return jnp.stack(parts).reshape(7, 7, grad_rows.shape[2])


def apply_layer_norm(activation_rows, scale_factor, offset_bias):
    centered_input = activation_rows - jnp.mean(activation_rows, axis=-1, keepdims=True)
    inverse_deviation = lax.rsqrt(
        jnp.mean(centered_input * centered_input, axis=-1, keepdims=True) + 1e-06
    )
    standardized_input = centered_input * inverse_deviation
    return (
        (standardized_input * scale_factor + offset_bias).astype(jnp.bfloat16),
        standardized_input,
        inverse_deviation,
    )


def gelu_grad(value):
    return (
        0.5 * (1.0 + jax.scipy.special.erf(value * 0.7071067811865476))
        + value * jnp.exp(-0.5 * value * value) * 0.3989422804014327
    )


def layer_norm_backward(normed_input_gradient, scale_factor, standardized_input, inverse_deviation):
    scaled_output = normed_input_gradient * scale_factor
    return (
        inverse_deviation
        * (
            scaled_output
            - jnp.mean(scaled_output, axis=-1, keepdims=True)
            - standardized_input
            * jnp.mean(scaled_output * standardized_input, axis=-1, keepdims=True)
        )
    ).astype(jnp.bfloat16)


def body(
    frames,
    kernel,
    kernel_bias,
    layer_norm_weight,
    layer_norm_bias,
    up_weight,
    up_bias,
    grn_gamma,
    grn_beta,
    grad_out,
):
    slab = frames[0]
    chans = slab.shape[2]
    columns = lax.all_gather(up_weight, "fsdp", axis=0, tiled=True)
    padded = extended(slab, (("rows", 0),), 3)
    activation_rows = conv_rows(padded, kernel, kernel_bias)
    normed_output, standardized_input, inverse_deviation = apply_layer_norm(
        activation_rows, layer_norm_weight, layer_norm_bias
    )
    whole = lax.all_gather(normed_output, "rows", axis=0, tiled=True)
    height = whole.shape[0]
    cols = whole.shape[1]
    flat = whole.reshape(-1, chans)
    pre = jnp.dot(flat, columns, preferred_element_type=jnp.float32) + up_bias
    post = jax.nn.gelu(pre, approximate=False)
    norms = jnp.sqrt(jnp.sum(post * post, axis=0) + 1e-06)
    cot_f = grad_out[0].reshape(flat.shape[0], -1).astype(jnp.float32)
    dnorm = grn_gamma * jnp.sum(cot_f * post, axis=0)
    norm_total = lax.psum(jnp.sum(norms), "rows")
    denom = norm_total / FF + 1e-06
    ratio = norms / denom
    output = (grn_gamma * (post * ratio) + grn_beta + post).astype(jnp.bfloat16)
    cross = lax.psum(jnp.sum(dnorm * norms), "rows")
    dnorms = dnorm / denom - cross / (denom * denom) / FF
    dpost = cot_f * (1.0 + grn_gamma * ratio) + post * (dnorms / norms)
    dpre = (dpost * gelu_grad(pre)).astype(jnp.bfloat16)
    w_term = lax.dot_general(
        flat, dpre, (((0,), (0,)), ((), ())), preferred_element_type=jnp.float32
    )
    up_grad = lax.psum_scatter(
        w_term.astype(jnp.bfloat16), "fsdp", scatter_dimension=0, tiled=True
    ).astype(jnp.float32)
    dpre_rows = dpre.reshape(height, cols, -1)
    normed_input_gradient = lax.psum_scatter(
        jnp.einsum("hwf,cf->hwc", dpre_rows, columns, preferred_element_type=jnp.float32).astype(
            jnp.bfloat16
        ),
        "rows",
        scatter_dimension=0,
        tiled=True,
    ).astype(jnp.float32)
    activation_gradient = layer_norm_backward(
        normed_input_gradient, layer_norm_weight, standardized_input, inverse_deviation
    )
    grad_pad = extended(activation_gradient, (("rows", 0),), 3)
    dframe = back_conv(grad_pad, kernel).astype(jnp.bfloat16)
    kernel_local = kern_grad(padded, activation_gradient)
    kernel_total = tree_allreduce(kernel_local, ("rows", "fsdp"))
    activation = output.reshape(1, height, cols, -1)
    return (activation, dframe.reshape((1,) + dframe.shape), up_grad, kernel_total)


def solution(mesh):
    placed = (
        P("fsdp", "rows", None, None),
        P(),
        P(),
        P(),
        P(),
        P("fsdp", "rows"),
        P("rows"),
        P("rows"),
        P("rows"),
        P("fsdp", None, None, "rows"),
    )
    return jax.shard_map(
        body,
        mesh=mesh,
        in_specs=placed,
        out_specs=(
            P("fsdp", None, None, "rows"),
            P("fsdp", "rows", None, None),
            P("fsdp", "rows"),
            P(),
        ),
        check_vma=False,
    )
```

```python
import jax
import jax.numpy as jnp
from jax import lax
from jax.sharding import PartitionSpec as P

FF = 6144


def extended(block, sides, width):
    for axis, dim in sides:
        count = lax.axis_size(axis)
        forward = [(i, i + 1) for i in range(count - 1)]
        backward = [(target, source) for source, target in forward]
        low = lax.ppermute(
            lax.slice_in_dim(block, block.shape[dim] - width, None, axis=dim), axis, forward
        )
        high = lax.ppermute(lax.slice_in_dim(block, 0, width, axis=dim), axis, backward)
        block = jnp.concatenate([low, block, high], axis=dim)
    return block


def _bit_steps(axes):
    steps = []
    for axis in axes:
        size = lax.axis_size(axis)
        assert size & (size - 1) == 0
        mask = 1
        while mask < size:
            steps.append((axis, mask, size))
            mask *= 2
    return steps


def tree_allreduce(value, axes):
    shape = value.shape
    flat = value.reshape(-1)
    steps = _bit_steps(axes)
    assert flat.shape[0] % (1 << len(steps)) == 0
    bits = []
    for axis, mask, size in steps:
        bit = (lax.axis_index(axis) // mask) % 2
        bits.append(bit)
        halves = flat.reshape(2, -1)
        keep = lax.dynamic_index_in_dim(halves, bit, keepdims=False)
        give = lax.dynamic_index_in_dim(halves, 1 - bit, keepdims=False)
        perm = [(j, j ^ mask) for j in range(size)]
        flat = keep + lax.ppermute(give, axis, perm)
    for (axis, mask, size), bit in reversed(list(zip(steps, bits))):
        perm = [(j, j ^ mask) for j in range(size)]
        other = lax.ppermute(flat, axis, perm)
        flat = jnp.where(bit == 0, jnp.concatenate([flat, other]), jnp.concatenate([other, flat]))
    return flat.reshape(shape)


def tree_reduce_scatter(chunks, axis):
    size = lax.axis_size(axis)
    assert chunks.shape[0] == size and size & (size - 1) == 0
    me = lax.axis_index(axis)
    data = chunks
    mask = 1
    while mask < size:
        bit = (me // mask) % 2
        pairs = data.reshape((data.shape[0] // 2, 2) + data.shape[1:])
        keep = lax.dynamic_index_in_dim(pairs, bit, axis=1, keepdims=False)
        give = lax.dynamic_index_in_dim(pairs, 1 - bit, axis=1, keepdims=False)
        perm = [(j, j ^ mask) for j in range(size)]
        data = keep.astype(jnp.float32) + lax.ppermute(give, axis, perm).astype(jnp.float32)
        mask *= 2
    return data[0]


def conv_rows(framed, kern, kbias):
    rows = framed.shape[0] - 6
    cols = framed.shape[1]
    wide = jnp.pad(framed, ((0, 0), (3, 3), (0, 0)))
    total = jnp.zeros((rows, cols, framed.shape[2]), jnp.float32) + kbias
    for i in range(kern.shape[0]):
        for j in range(kern.shape[1]):
            total = total + wide[i : i + rows, j : j + cols].astype(jnp.float32) * kern[i, j]
    return total


def back_conv(grad_pad, kern):
    rows = grad_pad.shape[0] - 6
    cols = grad_pad.shape[1]
    wide = jnp.pad(grad_pad, ((0, 0), (3, 3), (0, 0)))
    total = jnp.zeros((rows, cols, grad_pad.shape[2]), jnp.float32)
    for i in range(kern.shape[0]):
        for j in range(kern.shape[1]):
            total = (
                total
                + wide[6 - i : 6 - i + rows, 6 - j : 6 - j + cols].astype(jnp.float32) * kern[i, j]
            )
    return total


def kern_grad(framed, grad_rows):
    rows = grad_rows.shape[0]
    cols = grad_rows.shape[1]
    wide = jnp.pad(framed, ((0, 0), (3, 3), (0, 0)))
    grad_f = grad_rows.astype(jnp.float32)
    parts = []
    for i in range(7):
        for j in range(7):
            parts.append(
                jnp.sum(wide[i : i + rows, j : j + cols].astype(jnp.float32) * grad_f, axis=(0, 1))
            )
    return jnp.stack(parts).reshape(7, 7, grad_rows.shape[2])


def apply_layer_norm(activation_rows, scale_factor, offset_bias):
    centered_input = activation_rows - jnp.mean(activation_rows, axis=-1, keepdims=True)
    inverse_deviation = lax.rsqrt(
        jnp.mean(centered_input * centered_input, axis=-1, keepdims=True) + 1e-06
    )
    standardized_input = centered_input * inverse_deviation
    return (
        (standardized_input * scale_factor + offset_bias).astype(jnp.bfloat16),
        standardized_input,
        inverse_deviation,
    )


def gelu_grad(value):
    return (
        0.5 * (1.0 + jax.scipy.special.erf(value * 0.7071067811865476))
        + value * jnp.exp(-0.5 * value * value) * 0.3989422804014327
    )


def layer_norm_backward(normed_input_gradient, scale_factor, standardized_input, inverse_deviation):
    scaled_output = normed_input_gradient * scale_factor
    return (
        inverse_deviation
        * (
            scaled_output
            - jnp.mean(scaled_output, axis=-1, keepdims=True)
            - standardized_input
            * jnp.mean(scaled_output * standardized_input, axis=-1, keepdims=True)
        )
    ).astype(jnp.bfloat16)


def body(
    frames,
    kernel,
    kernel_bias,
    layer_norm_weight,
    layer_norm_bias,
    up_weight,
    up_bias,
    grn_gamma,
    grn_beta,
    grad_out,
):
    slab = frames[0]
    chans = slab.shape[2]
    columns = lax.all_gather(up_weight, "fsdp", axis=0, tiled=True)
    padded = extended(slab, (("rows", 0),), 3)
    activation_rows = conv_rows(padded, kernel, kernel_bias)
    normed_output, standardized_input, inverse_deviation = apply_layer_norm(
        activation_rows, layer_norm_weight, layer_norm_bias
    )
    whole = lax.all_gather(normed_output, "rows", axis=0, tiled=True)
    height = whole.shape[0]
    cols = whole.shape[1]
    flat = whole.reshape(-1, chans)
    pre = jnp.dot(flat, columns, preferred_element_type=jnp.float32) + up_bias
    post = jax.nn.gelu(pre, approximate=False)
    norms = jnp.sqrt(jnp.sum(post * post, axis=0) + 1e-06)
    cot_f = grad_out[0].reshape(flat.shape[0], -1).astype(jnp.float32)
    dnorm = grn_gamma * jnp.sum(cot_f * post, axis=0)
    norm_total = lax.psum(jnp.sum(norms), "rows")
    denom = norm_total / FF + 1e-06
    ratio = norms / denom
    output = (grn_gamma * (post * ratio) + grn_beta + post).astype(jnp.bfloat16)
    cross = lax.psum(jnp.sum(dnorm * norms), "rows")
    dnorms = dnorm / denom - cross / (denom * denom) / FF
    dpost = cot_f * (1.0 + grn_gamma * ratio) + post * (dnorms / norms)
    dpre = (dpost * gelu_grad(pre)).astype(jnp.bfloat16)
    w_term = lax.dot_general(
        flat, dpre, (((0,), (0,)), ((), ())), preferred_element_type=jnp.float32
    )
    up_grad = lax.psum_scatter(
        w_term.astype(jnp.bfloat16), "fsdp", scatter_dimension=0, tiled=True
    ).astype(jnp.float32)
    dpre_rows = dpre.reshape(height, cols, -1)
    group_terms = jnp.einsum(
        "hwf,cf->hwc", dpre_rows, columns, preferred_element_type=jnp.float32
    ).astype(jnp.bfloat16)
    n_rows = lax.axis_size("rows")
    normed_input_gradient = tree_reduce_scatter(
        group_terms.reshape((n_rows, height // n_rows) + group_terms.shape[1:]), "rows"
    )
    activation_gradient = layer_norm_backward(
        normed_input_gradient, layer_norm_weight, standardized_input, inverse_deviation
    )
    grad_pad = extended(activation_gradient, (("rows", 0),), 3)
    dframe = back_conv(grad_pad, kernel).astype(jnp.bfloat16)
    kernel_local = kern_grad(padded, activation_gradient)
    kernel_total = tree_allreduce(kernel_local, ("rows", "fsdp"))
    activation = output.reshape(1, height, cols, -1)
    return (activation, dframe.reshape((1,) + dframe.shape), up_grad, kernel_total)


def solution(mesh):
    placed = (
        P("fsdp", "rows", None, None),
        P(),
        P(),
        P(),
        P(),
        P("fsdp", "rows"),
        P("rows"),
        P("rows"),
        P("rows"),
        P("fsdp", None, None, "rows"),
    )
    return jax.shard_map(
        body,
        mesh=mesh,
        in_specs=placed,
        out_specs=(
            P("fsdp", None, None, "rows"),
            P("fsdp", "rows", None, None),
            P("fsdp", "rows"),
            P(),
        ),
        check_vma=False,
    )
```

```python
import functools

import jax
import jax.numpy as jnp
from jax import lax
from jax.sharding import PartitionSpec as P

FF = 6144


def extended(block, sides, width):
    for axis, dim in sides:
        count = lax.axis_size(axis)
        forward = [(i, i + 1) for i in range(count - 1)]
        backward = [(target, source) for source, target in forward]
        low = lax.ppermute(
            lax.slice_in_dim(block, block.shape[dim] - width, None, axis=dim), axis, forward
        )
        high = lax.ppermute(lax.slice_in_dim(block, 0, width, axis=dim), axis, backward)
        block = jnp.concatenate([low, block, high], axis=dim)
    return block


def _bit_steps(axes):
    steps = []
    for axis in axes:
        size = lax.axis_size(axis)
        assert size & (size - 1) == 0
        mask = 1
        while mask < size:
            steps.append((axis, mask, size))
            mask *= 2
    return steps


def tree_allreduce(value, axes):
    shape = value.shape
    flat = value.reshape(-1)
    steps = _bit_steps(axes)
    assert flat.shape[0] % (1 << len(steps)) == 0
    bits = []
    for axis, mask, size in steps:
        bit = (lax.axis_index(axis) // mask) % 2
        bits.append(bit)
        halves = flat.reshape(2, -1)
        keep = lax.dynamic_index_in_dim(halves, bit, keepdims=False)
        give = lax.dynamic_index_in_dim(halves, 1 - bit, keepdims=False)
        perm = [(j, j ^ mask) for j in range(size)]
        flat = keep + lax.ppermute(give, axis, perm)
    for (axis, mask, size), bit in reversed(list(zip(steps, bits))):
        perm = [(j, j ^ mask) for j in range(size)]
        other = lax.ppermute(flat, axis, perm)
        flat = jnp.where(bit == 0, jnp.concatenate([flat, other]), jnp.concatenate([other, flat]))
    return flat.reshape(shape)


def tree_reduce_scatter(chunks, axis):
    size = lax.axis_size(axis)
    assert chunks.shape[0] == size and size & (size - 1) == 0
    me = lax.axis_index(axis)
    data = chunks
    mask = 1
    while mask < size:
        bit = (me // mask) % 2
        pairs = data.reshape((data.shape[0] // 2, 2) + data.shape[1:])
        keep = lax.dynamic_index_in_dim(pairs, bit, axis=1, keepdims=False)
        give = lax.dynamic_index_in_dim(pairs, 1 - bit, axis=1, keepdims=False)
        perm = [(j, j ^ mask) for j in range(size)]
        data = keep.astype(jnp.float32) + lax.ppermute(give, axis, perm).astype(jnp.float32)
        mask *= 2
    return data[0]


def fsdp_ring(mesh):
    count = mesh.shape["fsdp"]
    try:
        members = [mesh.devices[j, 0] for j in range(count)]
        spots = [(d.coords[2], d.coords[1]) for d in members]
        zs = sorted({z for z, _ in spots})
        ys = sorted({y for _, y in spots})
        rows_a, cols_b = len(zs), len(ys)
        where = {(zs.index(z), ys.index(y)): j for j, (z, y) in enumerate(spots)}
        assert len(where) == count == rows_a * cols_b and rows_a % 2 == 0 and cols_b >= 2
        cells = [(a, 0) for a in range(rows_a)]
        for k, a in enumerate(range(rows_a - 1, -1, -1)):
            span = range(1, cols_b) if k % 2 == 0 else range(cols_b - 1, 0, -1)
            cells += [(a, b) for b in span]
        ring = [where[c] for c in cells]
        assert sorted(ring) == list(range(count))
    except Exception:
        ring = list(range(count))
    return ring


def ring_all_gather(block, axis, ring):
    count = len(ring)
    place = [0] * count
    for k, j in enumerate(ring):
        place[j] = k
    ring_arr = jnp.array(ring, jnp.int32)
    me = lax.axis_index(axis)
    spot = jnp.array(place, jnp.int32)[me]
    forward = [(ring[k], ring[(k + 1) % count]) for k in range(count)]
    backward = [(ring[k], ring[(k - 1) % count]) for k in range(count)]
    ahead = count // 2
    behind = count - 1 - ahead
    gathered = jnp.zeros((count,) + block.shape, block.dtype)
    gathered = lax.dynamic_update_index_in_dim(gathered, block, me, 0)
    cw = block
    ccw = block
    for s in range(1, ahead + 1):
        cw = lax.ppermute(cw, axis, forward)
        if s <= behind:
            ccw = lax.ppermute(ccw, axis, backward)
        gathered = lax.dynamic_update_index_in_dim(gathered, cw, ring_arr[(spot - s) % count], 0)
        if s <= behind:
            gathered = lax.dynamic_update_index_in_dim(
                gathered, ccw, ring_arr[(spot + s) % count], 0
            )
    return gathered.reshape((count * block.shape[0],) + block.shape[1:])


def conv_rows(framed, kern, kbias):
    rows = framed.shape[0] - 6
    cols = framed.shape[1]
    wide = jnp.pad(framed, ((0, 0), (3, 3), (0, 0)))
    total = jnp.zeros((rows, cols, framed.shape[2]), jnp.float32) + kbias
    for i in range(kern.shape[0]):
        for j in range(kern.shape[1]):
            total = total + wide[i : i + rows, j : j + cols].astype(jnp.float32) * kern[i, j]
    return total


def back_conv(grad_pad, kern):
    rows = grad_pad.shape[0] - 6
    cols = grad_pad.shape[1]
    wide = jnp.pad(grad_pad, ((0, 0), (3, 3), (0, 0)))
    total = jnp.zeros((rows, cols, grad_pad.shape[2]), jnp.float32)
    for i in range(kern.shape[0]):
        for j in range(kern.shape[1]):
            total = (
                total
                + wide[6 - i : 6 - i + rows, 6 - j : 6 - j + cols].astype(jnp.float32) * kern[i, j]
            )
    return total


def kern_grad(framed, grad_rows):
    rows = grad_rows.shape[0]
    cols = grad_rows.shape[1]
    wide = jnp.pad(framed, ((0, 0), (3, 3), (0, 0)))
    grad_f = grad_rows.astype(jnp.float32)
    parts = []
    for i in range(7):
        for j in range(7):
            parts.append(
                jnp.sum(wide[i : i + rows, j : j + cols].astype(jnp.float32) * grad_f, axis=(0, 1))
            )
    return jnp.stack(parts).reshape(7, 7, grad_rows.shape[2])


def apply_layer_norm(activation_rows, scale_factor, offset_bias):
    centered_input = activation_rows - jnp.mean(activation_rows, axis=-1, keepdims=True)
    inverse_deviation = lax.rsqrt(
        jnp.mean(centered_input * centered_input, axis=-1, keepdims=True) + 1e-06
    )
    standardized_input = centered_input * inverse_deviation
    return (
        (standardized_input * scale_factor + offset_bias).astype(jnp.bfloat16),
        standardized_input,
        inverse_deviation,
    )


def gelu_grad(value):
    return (
        0.5 * (1.0 + jax.scipy.special.erf(value * 0.7071067811865476))
        + value * jnp.exp(-0.5 * value * value) * 0.3989422804014327
    )


def layer_norm_backward(normed_input_gradient, scale_factor, standardized_input, inverse_deviation):
    scaled_output = normed_input_gradient * scale_factor
    return (
        inverse_deviation
        * (
            scaled_output
            - jnp.mean(scaled_output, axis=-1, keepdims=True)
            - standardized_input
            * jnp.mean(scaled_output * standardized_input, axis=-1, keepdims=True)
        )
    ).astype(jnp.bfloat16)


def body(
    ring,
    frames,
    kernel,
    kernel_bias,
    layer_norm_weight,
    layer_norm_bias,
    up_weight,
    up_bias,
    grn_gamma,
    grn_beta,
    grad_out,
):
    slab = frames[0]
    chans = slab.shape[2]
    columns = ring_all_gather(up_weight, "fsdp", ring)
    padded = extended(slab, (("rows", 0),), 3)
    activation_rows = conv_rows(padded, kernel, kernel_bias)
    normed_output, standardized_input, inverse_deviation = apply_layer_norm(
        activation_rows, layer_norm_weight, layer_norm_bias
    )
    whole = lax.all_gather(normed_output, "rows", axis=0, tiled=True)
    height = whole.shape[0]
    cols = whole.shape[1]
    flat = whole.reshape(-1, chans)
    pre = jnp.dot(flat, columns, preferred_element_type=jnp.float32) + up_bias
    post = jax.nn.gelu(pre, approximate=False)
    norms = jnp.sqrt(jnp.sum(post * post, axis=0) + 1e-06)
    cot_f = grad_out[0].reshape(flat.shape[0], -1).astype(jnp.float32)
    dnorm = grn_gamma * jnp.sum(cot_f * post, axis=0)
    norm_total = lax.psum(jnp.sum(norms), "rows")
    denom = norm_total / FF + 1e-06
    ratio = norms / denom
    output = (grn_gamma * (post * ratio) + grn_beta + post).astype(jnp.bfloat16)
    cross = lax.psum(jnp.sum(dnorm * norms), "rows")
    dnorms = dnorm / denom - cross / (denom * denom) / FF
    dpost = cot_f * (1.0 + grn_gamma * ratio) + post * (dnorms / norms)
    dpre = (dpost * gelu_grad(pre)).astype(jnp.bfloat16)
    w_term = lax.dot_general(
        flat, dpre, (((0,), (0,)), ((), ())), preferred_element_type=jnp.float32
    )
    up_grad = lax.psum_scatter(
        w_term.astype(jnp.bfloat16), "fsdp", scatter_dimension=0, tiled=True
    ).astype(jnp.float32)
    dpre_rows = dpre.reshape(height, cols, -1)
    group_terms = jnp.einsum(
        "hwf,cf->hwc", dpre_rows, columns, preferred_element_type=jnp.float32
    ).astype(jnp.bfloat16)
    n_rows = lax.axis_size("rows")
    normed_input_gradient = tree_reduce_scatter(
        group_terms.reshape((n_rows, height // n_rows) + group_terms.shape[1:]), "rows"
    )
    activation_gradient = layer_norm_backward(
        normed_input_gradient, layer_norm_weight, standardized_input, inverse_deviation
    )
    grad_pad = extended(activation_gradient, (("rows", 0),), 3)
    dframe = back_conv(grad_pad, kernel).astype(jnp.bfloat16)
    kernel_local = kern_grad(padded, activation_gradient)
    kernel_total = tree_allreduce(kernel_local, ("rows", "fsdp"))
    activation = output.reshape(1, height, cols, -1)
    return (activation, dframe.reshape((1,) + dframe.shape), up_grad, kernel_total)


def solution(mesh):
    placed = (
        P("fsdp", "rows", None, None),
        P(),
        P(),
        P(),
        P(),
        P("fsdp", "rows"),
        P("rows"),
        P("rows"),
        P("rows"),
        P("fsdp", None, None, "rows"),
    )
    return jax.shard_map(
        functools.partial(body, fsdp_ring(mesh)),
        mesh=mesh,
        in_specs=placed,
        out_specs=(
            P("fsdp", None, None, "rows"),
            P("fsdp", "rows", None, None),
            P("fsdp", "rows"),
            P(),
        ),
        check_vma=False,
    )
```

```python
import functools

import jax
import jax.numpy as jnp
from jax import lax
from jax.sharding import PartitionSpec as P

FF = 6144


def extended(block, sides, width):
    for axis, dim in sides:
        count = lax.axis_size(axis)
        forward = [(i, i + 1) for i in range(count - 1)]
        backward = [(target, source) for source, target in forward]
        low = lax.ppermute(
            lax.slice_in_dim(block, block.shape[dim] - width, None, axis=dim), axis, forward
        )
        high = lax.ppermute(lax.slice_in_dim(block, 0, width, axis=dim), axis, backward)
        block = jnp.concatenate([low, block, high], axis=dim)
    return block


def _bit_steps(axes):
    steps = []
    for axis in axes:
        size = lax.axis_size(axis)
        assert size & (size - 1) == 0
        mask = 1
        while mask < size:
            steps.append((axis, mask, size))
            mask *= 2
    return steps


def tree_allreduce(value, axes):
    shape = value.shape
    flat = value.reshape(-1)
    steps = _bit_steps(axes)
    assert flat.shape[0] % (1 << len(steps)) == 0
    bits = []
    for axis, mask, size in steps:
        bit = (lax.axis_index(axis) // mask) % 2
        bits.append(bit)
        halves = flat.reshape(2, -1)
        keep = lax.dynamic_index_in_dim(halves, bit, keepdims=False)
        give = lax.dynamic_index_in_dim(halves, 1 - bit, keepdims=False)
        perm = [(j, j ^ mask) for j in range(size)]
        flat = keep + lax.ppermute(give, axis, perm)
    for (axis, mask, size), bit in reversed(list(zip(steps, bits))):
        perm = [(j, j ^ mask) for j in range(size)]
        other = lax.ppermute(flat, axis, perm)
        flat = jnp.where(bit == 0, jnp.concatenate([flat, other]), jnp.concatenate([other, flat]))
    return flat.reshape(shape)


def tree_reduce_scatter(chunks, axis):
    size = lax.axis_size(axis)
    assert chunks.shape[0] == size and size & (size - 1) == 0
    me = lax.axis_index(axis)
    data = chunks
    mask = 1
    while mask < size:
        bit = (me // mask) % 2
        pairs = data.reshape((data.shape[0] // 2, 2) + data.shape[1:])
        keep = lax.dynamic_index_in_dim(pairs, bit, axis=1, keepdims=False)
        give = lax.dynamic_index_in_dim(pairs, 1 - bit, axis=1, keepdims=False)
        perm = [(j, j ^ mask) for j in range(size)]
        data = keep.astype(jnp.float32) + lax.ppermute(give, axis, perm).astype(jnp.float32)
        mask *= 2
    return data[0]


def fsdp_ring(mesh):
    count = mesh.shape["fsdp"]
    try:
        members = [mesh.devices[j, 0] for j in range(count)]
        spots = [(d.coords[2], d.coords[1]) for d in members]
        zs = sorted({z for z, _ in spots})
        ys = sorted({y for _, y in spots})
        rows_a, cols_b = len(zs), len(ys)
        where = {(zs.index(z), ys.index(y)): j for j, (z, y) in enumerate(spots)}
        assert len(where) == count == rows_a * cols_b and rows_a % 2 == 0 and cols_b >= 2
        cells = [(a, 0) for a in range(rows_a)]
        for k, a in enumerate(range(rows_a - 1, -1, -1)):
            span = range(1, cols_b) if k % 2 == 0 else range(cols_b - 1, 0, -1)
            cells += [(a, b) for b in span]
        ring = [where[c] for c in cells]
        assert sorted(ring) == list(range(count))
    except Exception:
        ring = list(range(count))
    return ring


def ring_all_gather(block, axis, ring):
    count = len(ring)
    place = [0] * count
    for k, j in enumerate(ring):
        place[j] = k
    ring_arr = jnp.array(ring, jnp.int32)
    me = lax.axis_index(axis)
    spot = jnp.array(place, jnp.int32)[me]
    forward = [(ring[k], ring[(k + 1) % count]) for k in range(count)]
    backward = [(ring[k], ring[(k - 1) % count]) for k in range(count)]
    ahead = count // 2
    behind = count - 1 - ahead
    gathered = jnp.zeros((count,) + block.shape, block.dtype)
    gathered = lax.dynamic_update_index_in_dim(gathered, block, me, 0)
    cw = block
    ccw = block
    for s in range(1, ahead + 1):
        cw = lax.ppermute(cw, axis, forward)
        if s <= behind:
            ccw = lax.ppermute(ccw, axis, backward)
        gathered = lax.dynamic_update_index_in_dim(gathered, cw, ring_arr[(spot - s) % count], 0)
        if s <= behind:
            gathered = lax.dynamic_update_index_in_dim(
                gathered, ccw, ring_arr[(spot + s) % count], 0
            )
    return gathered.reshape((count * block.shape[0],) + block.shape[1:])


def ring_reduce_scatter(terms, axis, ring):
    count = len(ring)
    place = [0] * count
    for k, j in enumerate(ring):
        place[j] = k
    ring_arr = jnp.array(ring, jnp.int32)
    me = lax.axis_index(axis)
    spot = jnp.array(place, jnp.int32)[me]
    forward = [(ring[k], ring[(k + 1) % count]) for k in range(count)]
    backward = [(ring[k], ring[(k - 1) % count]) for k in range(count)]
    ahead = count // 2
    behind = count - 1 - ahead

    def term(offset):
        return lax.dynamic_index_in_dim(terms, ring_arr[(spot + offset) % count], 0, keepdims=False)

    total = term(0).astype(jnp.float32)
    cw = term(ahead)
    ccw = term(-behind) if behind else None
    for s in range(1, ahead + 1):
        cw = lax.ppermute(cw, axis, forward)
        if s <= behind:
            ccw = lax.ppermute(ccw, axis, backward)
        if s < ahead:
            cw = (cw.astype(jnp.float32) + term(ahead - s).astype(jnp.float32)).astype(terms.dtype)
        else:
            total = total + cw.astype(jnp.float32)
        if s < behind:
            ccw = (ccw.astype(jnp.float32) + term(s - behind).astype(jnp.float32)).astype(terms.dtype)
        elif s == behind:
            total = total + ccw.astype(jnp.float32)
    return total


def conv_rows(framed, kern, kbias):
    rows = framed.shape[0] - 6
    cols = framed.shape[1]
    wide = jnp.pad(framed, ((0, 0), (3, 3), (0, 0)))
    total = jnp.zeros((rows, cols, framed.shape[2]), jnp.float32) + kbias
    for i in range(kern.shape[0]):
        for j in range(kern.shape[1]):
            total = total + wide[i : i + rows, j : j + cols].astype(jnp.float32) * kern[i, j]
    return total


def back_conv(grad_pad, kern):
    rows = grad_pad.shape[0] - 6
    cols = grad_pad.shape[1]
    wide = jnp.pad(grad_pad, ((0, 0), (3, 3), (0, 0)))
    total = jnp.zeros((rows, cols, grad_pad.shape[2]), jnp.float32)
    for i in range(kern.shape[0]):
        for j in range(kern.shape[1]):
            total = (
                total
                + wide[6 - i : 6 - i + rows, 6 - j : 6 - j + cols].astype(jnp.float32) * kern[i, j]
            )
    return total


def kern_grad(framed, grad_rows):
    rows = grad_rows.shape[0]
    cols = grad_rows.shape[1]
    wide = jnp.pad(framed, ((0, 0), (3, 3), (0, 0)))
    grad_f = grad_rows.astype(jnp.float32)
    parts = []
    for i in range(7):
        for j in range(7):
            parts.append(
                jnp.sum(wide[i : i + rows, j : j + cols].astype(jnp.float32) * grad_f, axis=(0, 1))
            )
    return jnp.stack(parts).reshape(7, 7, grad_rows.shape[2])


def apply_layer_norm(activation_rows, scale_factor, offset_bias):
    centered_input = activation_rows - jnp.mean(activation_rows, axis=-1, keepdims=True)
    inverse_deviation = lax.rsqrt(
        jnp.mean(centered_input * centered_input, axis=-1, keepdims=True) + 1e-06
    )
    standardized_input = centered_input * inverse_deviation
    return (
        (standardized_input * scale_factor + offset_bias).astype(jnp.bfloat16),
        standardized_input,
        inverse_deviation,
    )


def gelu_grad(value):
    return (
        0.5 * (1.0 + jax.scipy.special.erf(value * 0.7071067811865476))
        + value * jnp.exp(-0.5 * value * value) * 0.3989422804014327
    )


def layer_norm_backward(normed_input_gradient, scale_factor, standardized_input, inverse_deviation):
    scaled_output = normed_input_gradient * scale_factor
    return (
        inverse_deviation
        * (
            scaled_output
            - jnp.mean(scaled_output, axis=-1, keepdims=True)
            - standardized_input
            * jnp.mean(scaled_output * standardized_input, axis=-1, keepdims=True)
        )
    ).astype(jnp.bfloat16)


def body(
    ring,
    frames,
    kernel,
    kernel_bias,
    layer_norm_weight,
    layer_norm_bias,
    up_weight,
    up_bias,
    grn_gamma,
    grn_beta,
    grad_out,
):
    slab = frames[0]
    chans = slab.shape[2]
    columns = lax.all_gather(up_weight, "fsdp", axis=0, tiled=True)
    padded = extended(slab, (("rows", 0),), 3)
    activation_rows = conv_rows(padded, kernel, kernel_bias)
    normed_output, standardized_input, inverse_deviation = apply_layer_norm(
        activation_rows, layer_norm_weight, layer_norm_bias
    )
    whole = lax.all_gather(normed_output, "rows", axis=0, tiled=True)
    height = whole.shape[0]
    cols = whole.shape[1]
    flat = whole.reshape(-1, chans)
    pre = jnp.dot(flat, columns, preferred_element_type=jnp.float32) + up_bias
    post = jax.nn.gelu(pre, approximate=False)
    norms = jnp.sqrt(jnp.sum(post * post, axis=0) + 1e-06)
    cot_f = grad_out[0].reshape(flat.shape[0], -1).astype(jnp.float32)
    dnorm = grn_gamma * jnp.sum(cot_f * post, axis=0)
    norm_total = lax.psum(jnp.sum(norms), "rows")
    denom = norm_total / FF + 1e-06
    ratio = norms / denom
    output = (grn_gamma * (post * ratio) + grn_beta + post).astype(jnp.bfloat16)
    cross = lax.psum(jnp.sum(dnorm * norms), "rows")
    dnorms = dnorm / denom - cross / (denom * denom) / FF
    dpost = cot_f * (1.0 + grn_gamma * ratio) + post * (dnorms / norms)
    dpre = (dpost * gelu_grad(pre)).astype(jnp.bfloat16)
    w_term = lax.dot_general(
        flat, dpre, (((0,), (0,)), ((), ())), preferred_element_type=jnp.float32
    )
    n_fsdp = lax.axis_size("fsdp")
    up_grad = ring_reduce_scatter(
        w_term.astype(jnp.bfloat16).reshape((n_fsdp, chans // n_fsdp, -1)), "fsdp", ring
    )
    dpre_rows = dpre.reshape(height, cols, -1)
    group_terms = jnp.einsum(
        "hwf,cf->hwc", dpre_rows, columns, preferred_element_type=jnp.float32
    ).astype(jnp.bfloat16)
    n_rows = lax.axis_size("rows")
    normed_input_gradient = tree_reduce_scatter(
        group_terms.reshape((n_rows, height // n_rows) + group_terms.shape[1:]), "rows"
    )
    activation_gradient = layer_norm_backward(
        normed_input_gradient, layer_norm_weight, standardized_input, inverse_deviation
    )
    grad_pad = extended(activation_gradient, (("rows", 0),), 3)
    dframe = back_conv(grad_pad, kernel).astype(jnp.bfloat16)
    kernel_local = kern_grad(padded, activation_gradient)
    kernel_total = tree_allreduce(kernel_local, ("rows", "fsdp"))
    activation = output.reshape(1, height, cols, -1)
    return (activation, dframe.reshape((1,) + dframe.shape), up_grad, kernel_total)


def solution(mesh):
    placed = (
        P("fsdp", "rows", None, None),
        P(),
        P(),
        P(),
        P(),
        P("fsdp", "rows"),
        P("rows"),
        P("rows"),
        P("rows"),
        P("fsdp", None, None, "rows"),
    )
    return jax.shard_map(
        functools.partial(body, fsdp_ring(mesh)),
        mesh=mesh,
        in_specs=placed,
        out_specs=(
            P("fsdp", None, None, "rows"),
            P("fsdp", "rows", None, None),
            P("fsdp", "rows"),
            P(),
        ),
        check_vma=False,
    )
```

```python
import functools

import jax
import jax.numpy as jnp
from jax import lax
from jax.sharding import PartitionSpec as P

FF = 6144


def extended(block, sides, width):
    for axis, dim in sides:
        count = lax.axis_size(axis)
        forward = [(i, i + 1) for i in range(count - 1)]
        backward = [(target, source) for source, target in forward]
        low = lax.ppermute(
            lax.slice_in_dim(block, block.shape[dim] - width, None, axis=dim), axis, forward
        )
        high = lax.ppermute(lax.slice_in_dim(block, 0, width, axis=dim), axis, backward)
        block = jnp.concatenate([low, block, high], axis=dim)
    return block


def _bit_steps(axes):
    steps = []
    for axis in axes:
        size = lax.axis_size(axis)
        assert size & (size - 1) == 0
        mask = 1
        while mask < size:
            steps.append((axis, mask, size))
            mask *= 2
    return steps


def tree_allreduce(value, axes):
    shape = value.shape
    flat = value.reshape(-1)
    steps = _bit_steps(axes)
    assert flat.shape[0] % (1 << len(steps)) == 0
    bits = []
    for axis, mask, size in steps:
        bit = (lax.axis_index(axis) // mask) % 2
        bits.append(bit)
        halves = flat.reshape(2, -1)
        keep = lax.dynamic_index_in_dim(halves, bit, keepdims=False)
        give = lax.dynamic_index_in_dim(halves, 1 - bit, keepdims=False)
        perm = [(j, j ^ mask) for j in range(size)]
        flat = keep + lax.ppermute(give, axis, perm)
    for (axis, mask, size), bit in reversed(list(zip(steps, bits))):
        perm = [(j, j ^ mask) for j in range(size)]
        other = lax.ppermute(flat, axis, perm)
        flat = jnp.where(bit == 0, jnp.concatenate([flat, other]), jnp.concatenate([other, flat]))
    return flat.reshape(shape)


def tree_reduce_scatter(chunks, axis):
    size = lax.axis_size(axis)
    assert chunks.shape[0] == size and size & (size - 1) == 0
    me = lax.axis_index(axis)
    data = chunks
    mask = 1
    while mask < size:
        bit = (me // mask) % 2
        pairs = data.reshape((data.shape[0] // 2, 2) + data.shape[1:])
        keep = lax.dynamic_index_in_dim(pairs, bit, axis=1, keepdims=False)
        give = lax.dynamic_index_in_dim(pairs, 1 - bit, axis=1, keepdims=False)
        perm = [(j, j ^ mask) for j in range(size)]
        data = keep.astype(jnp.float32) + lax.ppermute(give, axis, perm).astype(jnp.float32)
        mask *= 2
    return data[0]


def fsdp_ring(mesh):
    count = mesh.shape["fsdp"]
    try:
        members = [mesh.devices[j, 0] for j in range(count)]
        spots = [(d.coords[2], d.coords[1]) for d in members]
        zs = sorted({z for z, _ in spots})
        ys = sorted({y for _, y in spots})
        rows_a, cols_b = len(zs), len(ys)
        where = {(zs.index(z), ys.index(y)): j for j, (z, y) in enumerate(spots)}
        assert len(where) == count == rows_a * cols_b and rows_a % 2 == 0 and cols_b >= 2
        cells = [(a, 0) for a in range(rows_a)]
        for k, a in enumerate(range(rows_a - 1, -1, -1)):
            span = range(1, cols_b) if k % 2 == 0 else range(cols_b - 1, 0, -1)
            cells += [(a, b) for b in span]
        ring = [where[c] for c in cells]
        assert sorted(ring) == list(range(count))
    except Exception:
        ring = list(range(count))
    return ring


def ring_all_gather(block, axis, ring):
    count = len(ring)
    place = [0] * count
    for k, j in enumerate(ring):
        place[j] = k
    ring_arr = jnp.array(ring, jnp.int32)
    me = lax.axis_index(axis)
    spot = jnp.array(place, jnp.int32)[me]
    forward = [(ring[k], ring[(k + 1) % count]) for k in range(count)]
    backward = [(ring[k], ring[(k - 1) % count]) for k in range(count)]
    ahead = count // 2
    behind = count - 1 - ahead
    gathered = jnp.zeros((count,) + block.shape, block.dtype)
    gathered = lax.dynamic_update_index_in_dim(gathered, block, me, 0)
    cw = block
    ccw = block
    for s in range(1, ahead + 1):
        cw = lax.ppermute(cw, axis, forward)
        if s <= behind:
            ccw = lax.ppermute(ccw, axis, backward)
        gathered = lax.dynamic_update_index_in_dim(gathered, cw, ring_arr[(spot - s) % count], 0)
        if s <= behind:
            gathered = lax.dynamic_update_index_in_dim(
                gathered, ccw, ring_arr[(spot + s) % count], 0
            )
    return gathered.reshape((count * block.shape[0],) + block.shape[1:])


def ring_reduce_scatter(terms, axis, ring):
    count = len(ring)
    place = [0] * count
    for k, j in enumerate(ring):
        place[j] = k
    ring_arr = jnp.array(ring, jnp.int32)
    me = lax.axis_index(axis)
    spot = jnp.array(place, jnp.int32)[me]
    forward = [(ring[k], ring[(k + 1) % count]) for k in range(count)]
    backward = [(ring[k], ring[(k - 1) % count]) for k in range(count)]
    ahead = count // 2
    behind = count - 1 - ahead

    def term(offset):
        return lax.dynamic_index_in_dim(terms, ring_arr[(spot + offset) % count], 0, keepdims=False)

    total = term(0).astype(jnp.float32)
    cw = term(ahead)
    ccw = term(-behind) if behind else None
    for s in range(1, ahead + 1):
        cw = lax.ppermute(cw, axis, forward)
        if s <= behind:
            ccw = lax.ppermute(ccw, axis, backward)
        if s < ahead:
            cw = (cw.astype(jnp.float32) + term(ahead - s).astype(jnp.float32)).astype(terms.dtype)
        else:
            total = total + cw.astype(jnp.float32)
        if s < behind:
            ccw = (ccw.astype(jnp.float32) + term(s - behind).astype(jnp.float32)).astype(terms.dtype)
        elif s == behind:
            total = total + ccw.astype(jnp.float32)
    return total


def conv_rows(framed, kern, kbias):
    rows = framed.shape[0] - 6
    cols = framed.shape[1]
    wide = jnp.pad(framed, ((0, 0), (3, 3), (0, 0)))
    total = jnp.zeros((rows, cols, framed.shape[2]), jnp.float32) + kbias
    for i in range(kern.shape[0]):
        for j in range(kern.shape[1]):
            total = total + wide[i : i + rows, j : j + cols].astype(jnp.float32) * kern[i, j]
    return total


def back_conv(grad_pad, kern):
    rows = grad_pad.shape[0] - 6
    cols = grad_pad.shape[1]
    wide = jnp.pad(grad_pad, ((0, 0), (3, 3), (0, 0)))
    total = jnp.zeros((rows, cols, grad_pad.shape[2]), jnp.float32)
    for i in range(kern.shape[0]):
        for j in range(kern.shape[1]):
            total = (
                total
                + wide[6 - i : 6 - i + rows, 6 - j : 6 - j + cols].astype(jnp.float32) * kern[i, j]
            )
    return total


def kern_grad(framed, grad_rows):
    rows = grad_rows.shape[0]
    cols = grad_rows.shape[1]
    wide = jnp.pad(framed, ((0, 0), (3, 3), (0, 0)))
    grad_f = grad_rows.astype(jnp.float32)
    parts = []
    for i in range(7):
        for j in range(7):
            parts.append(
                jnp.sum(wide[i : i + rows, j : j + cols].astype(jnp.float32) * grad_f, axis=(0, 1))
            )
    return jnp.stack(parts).reshape(7, 7, grad_rows.shape[2])


def apply_layer_norm(activation_rows, scale_factor, offset_bias):
    centered_input = activation_rows - jnp.mean(activation_rows, axis=-1, keepdims=True)
    inverse_deviation = lax.rsqrt(
        jnp.mean(centered_input * centered_input, axis=-1, keepdims=True) + 1e-06
    )
    standardized_input = centered_input * inverse_deviation
    return (
        (standardized_input * scale_factor + offset_bias).astype(jnp.bfloat16),
        standardized_input,
        inverse_deviation,
    )


def gelu_grad(value):
    return (
        0.5 * (1.0 + jax.scipy.special.erf(value * 0.7071067811865476))
        + value * jnp.exp(-0.5 * value * value) * 0.3989422804014327
    )


def layer_norm_backward(normed_input_gradient, scale_factor, standardized_input, inverse_deviation):
    scaled_output = normed_input_gradient * scale_factor
    return (
        inverse_deviation
        * (
            scaled_output
            - jnp.mean(scaled_output, axis=-1, keepdims=True)
            - standardized_input
            * jnp.mean(scaled_output * standardized_input, axis=-1, keepdims=True)
        )
    ).astype(jnp.bfloat16)


def body(
    ring,
    frames,
    kernel,
    kernel_bias,
    layer_norm_weight,
    layer_norm_bias,
    up_weight,
    up_bias,
    grn_gamma,
    grn_beta,
    grad_out,
):
    slab = frames[0]
    chans = slab.shape[2]
    split = up_weight.shape[1] // 2
    columns = jnp.concatenate(
        [
            lax.all_gather(up_weight[:, :split], "fsdp", axis=0, tiled=True),
            ring_all_gather(up_weight[:, split:], "fsdp", ring),
        ],
        axis=1,
    )
    padded = extended(slab, (("rows", 0),), 3)
    activation_rows = conv_rows(padded, kernel, kernel_bias)
    normed_output, standardized_input, inverse_deviation = apply_layer_norm(
        activation_rows, layer_norm_weight, layer_norm_bias
    )
    whole = lax.all_gather(normed_output, "rows", axis=0, tiled=True)
    height = whole.shape[0]
    cols = whole.shape[1]
    flat = whole.reshape(-1, chans)
    pre = jnp.dot(flat, columns, preferred_element_type=jnp.float32) + up_bias
    post = jax.nn.gelu(pre, approximate=False)
    norms = jnp.sqrt(jnp.sum(post * post, axis=0) + 1e-06)
    cot_f = grad_out[0].reshape(flat.shape[0], -1).astype(jnp.float32)
    dnorm = grn_gamma * jnp.sum(cot_f * post, axis=0)
    norm_total = lax.psum(jnp.sum(norms), "rows")
    denom = norm_total / FF + 1e-06
    ratio = norms / denom
    output = (grn_gamma * (post * ratio) + grn_beta + post).astype(jnp.bfloat16)
    cross = lax.psum(jnp.sum(dnorm * norms), "rows")
    dnorms = dnorm / denom - cross / (denom * denom) / FF
    dpost = cot_f * (1.0 + grn_gamma * ratio) + post * (dnorms / norms)
    dpre = (dpost * gelu_grad(pre)).astype(jnp.bfloat16)
    w_term = lax.dot_general(
        flat, dpre, (((0,), (0,)), ((), ())), preferred_element_type=jnp.float32
    )
    up_grad = lax.psum_scatter(
        w_term.astype(jnp.bfloat16), "fsdp", scatter_dimension=0, tiled=True
    ).astype(jnp.float32)
    dpre_rows = dpre.reshape(height, cols, -1)
    group_terms = jnp.einsum(
        "hwf,cf->hwc", dpre_rows, columns, preferred_element_type=jnp.float32
    ).astype(jnp.bfloat16)
    n_rows = lax.axis_size("rows")
    normed_input_gradient = tree_reduce_scatter(
        group_terms.reshape((n_rows, height // n_rows) + group_terms.shape[1:]), "rows"
    )
    activation_gradient = layer_norm_backward(
        normed_input_gradient, layer_norm_weight, standardized_input, inverse_deviation
    )
    grad_pad = extended(activation_gradient, (("rows", 0),), 3)
    dframe = back_conv(grad_pad, kernel).astype(jnp.bfloat16)
    kernel_local = kern_grad(padded, activation_gradient)
    kernel_total = tree_allreduce(kernel_local, ("rows", "fsdp"))
    activation = output.reshape(1, height, cols, -1)
    return (activation, dframe.reshape((1,) + dframe.shape), up_grad, kernel_total)


def solution(mesh):
    placed = (
        P("fsdp", "rows", None, None),
        P(),
        P(),
        P(),
        P(),
        P("fsdp", "rows"),
        P("rows"),
        P("rows"),
        P("rows"),
        P("fsdp", None, None, "rows"),
    )
    return jax.shard_map(
        functools.partial(body, fsdp_ring(mesh)),
        mesh=mesh,
        in_specs=placed,
        out_specs=(
            P("fsdp", None, None, "rows"),
            P("fsdp", "rows", None, None),
            P("fsdp", "rows"),
            P(),
        ),
        check_vma=False,
    )
```

```python
import functools

import jax
import jax.numpy as jnp
from jax import lax
from jax.sharding import PartitionSpec as P

FF = 6144


def extended(block, sides, width):
    for axis, dim in sides:
        count = lax.axis_size(axis)
        forward = [(i, i + 1) for i in range(count - 1)]
        backward = [(target, source) for source, target in forward]
        low = lax.ppermute(
            lax.slice_in_dim(block, block.shape[dim] - width, None, axis=dim), axis, forward
        )
        high = lax.ppermute(lax.slice_in_dim(block, 0, width, axis=dim), axis, backward)
        block = jnp.concatenate([low, block, high], axis=dim)
    return block


def _bit_steps(axes):
    steps = []
    for axis in axes:
        size = lax.axis_size(axis)
        assert size & (size - 1) == 0
        mask = 1
        while mask < size:
            steps.append((axis, mask, size))
            mask *= 2
    return steps


def tree_allreduce(value, axes):
    shape = value.shape
    flat = value.reshape(-1)
    steps = _bit_steps(axes)
    assert flat.shape[0] % (1 << len(steps)) == 0
    bits = []
    for axis, mask, size in steps:
        bit = (lax.axis_index(axis) // mask) % 2
        bits.append(bit)
        halves = flat.reshape(2, -1)
        keep = lax.dynamic_index_in_dim(halves, bit, keepdims=False)
        give = lax.dynamic_index_in_dim(halves, 1 - bit, keepdims=False)
        perm = [(j, j ^ mask) for j in range(size)]
        flat = keep + lax.ppermute(give, axis, perm)
    for (axis, mask, size), bit in reversed(list(zip(steps, bits))):
        perm = [(j, j ^ mask) for j in range(size)]
        other = lax.ppermute(flat, axis, perm)
        flat = jnp.where(bit == 0, jnp.concatenate([flat, other]), jnp.concatenate([other, flat]))
    return flat.reshape(shape)


def tree_reduce_scatter(chunks, axis):
    size = lax.axis_size(axis)
    assert chunks.shape[0] == size and size & (size - 1) == 0
    me = lax.axis_index(axis)
    data = chunks
    mask = 1
    while mask < size:
        bit = (me // mask) % 2
        pairs = data.reshape((data.shape[0] // 2, 2) + data.shape[1:])
        keep = lax.dynamic_index_in_dim(pairs, bit, axis=1, keepdims=False)
        give = lax.dynamic_index_in_dim(pairs, 1 - bit, axis=1, keepdims=False)
        perm = [(j, j ^ mask) for j in range(size)]
        data = keep.astype(jnp.float32) + lax.ppermute(give, axis, perm).astype(jnp.float32)
        mask *= 2
    return data[0]


def fsdp_ring(mesh):
    count = mesh.shape["fsdp"]
    try:
        members = [mesh.devices[j, 0] for j in range(count)]
        spots = [(d.coords[2], d.coords[1]) for d in members]
        zs = sorted({z for z, _ in spots})
        ys = sorted({y for _, y in spots})
        rows_a, cols_b = len(zs), len(ys)
        where = {(zs.index(z), ys.index(y)): j for j, (z, y) in enumerate(spots)}
        assert len(where) == count == rows_a * cols_b and rows_a % 2 == 0 and cols_b >= 2
        cells = [(a, 0) for a in range(rows_a)]
        for k, a in enumerate(range(rows_a - 1, -1, -1)):
            span = range(1, cols_b) if k % 2 == 0 else range(cols_b - 1, 0, -1)
            cells += [(a, b) for b in span]
        ring = [where[c] for c in cells]
        assert sorted(ring) == list(range(count))
    except Exception:
        ring = list(range(count))
    return ring


def ring_all_gather(block, axis, ring):
    count = len(ring)
    place = [0] * count
    for k, j in enumerate(ring):
        place[j] = k
    ring_arr = jnp.array(ring, jnp.int32)
    me = lax.axis_index(axis)
    spot = jnp.array(place, jnp.int32)[me]
    forward = [(ring[k], ring[(k + 1) % count]) for k in range(count)]
    backward = [(ring[k], ring[(k - 1) % count]) for k in range(count)]
    ahead = count // 2
    behind = count - 1 - ahead
    gathered = jnp.zeros((count,) + block.shape, block.dtype)
    gathered = lax.dynamic_update_index_in_dim(gathered, block, me, 0)
    cw = block
    ccw = block
    for s in range(1, ahead + 1):
        cw = lax.ppermute(cw, axis, forward)
        if s <= behind:
            ccw = lax.ppermute(ccw, axis, backward)
        gathered = lax.dynamic_update_index_in_dim(gathered, cw, ring_arr[(spot - s) % count], 0)
        if s <= behind:
            gathered = lax.dynamic_update_index_in_dim(
                gathered, ccw, ring_arr[(spot + s) % count], 0
            )
    return gathered.reshape((count * block.shape[0],) + block.shape[1:])


def ring_reduce_scatter(terms, axis, ring):
    count = len(ring)
    place = [0] * count
    for k, j in enumerate(ring):
        place[j] = k
    ring_arr = jnp.array(ring, jnp.int32)
    me = lax.axis_index(axis)
    spot = jnp.array(place, jnp.int32)[me]
    forward = [(ring[k], ring[(k + 1) % count]) for k in range(count)]
    backward = [(ring[k], ring[(k - 1) % count]) for k in range(count)]
    ahead = count // 2
    behind = count - 1 - ahead

    def term(offset):
        return lax.dynamic_index_in_dim(terms, ring_arr[(spot + offset) % count], 0, keepdims=False)

    total = term(0).astype(jnp.float32)
    cw = term(ahead)
    ccw = term(-behind) if behind else None
    for s in range(1, ahead + 1):
        cw = lax.ppermute(cw, axis, forward)
        if s <= behind:
            ccw = lax.ppermute(ccw, axis, backward)
        if s < ahead:
            cw = (cw.astype(jnp.float32) + term(ahead - s).astype(jnp.float32)).astype(terms.dtype)
        else:
            total = total + cw.astype(jnp.float32)
        if s < behind:
            ccw = (ccw.astype(jnp.float32) + term(s - behind).astype(jnp.float32)).astype(terms.dtype)
        elif s == behind:
            total = total + ccw.astype(jnp.float32)
    return total


def tree_all_gather(block, axis):
    size = lax.axis_size(axis)
    assert size & (size - 1) == 0
    me = lax.axis_index(axis)
    data = block[None]
    mask = 1
    while mask < size:
        bit = (me // mask) % 2
        perm = [(j, j ^ mask) for j in range(size)]
        other = lax.ppermute(data, axis, perm)
        data = jnp.where(bit == 0, jnp.concatenate([data, other]), jnp.concatenate([other, data]))
        mask *= 2
    return data.reshape((size * block.shape[0],) + block.shape[1:])


def conv_rows(framed, kern, kbias):
    rows = framed.shape[0] - 6
    cols = framed.shape[1]
    wide = jnp.pad(framed, ((0, 0), (3, 3), (0, 0)))
    total = jnp.zeros((rows, cols, framed.shape[2]), jnp.float32) + kbias
    for i in range(kern.shape[0]):
        for j in range(kern.shape[1]):
            total = total + wide[i : i + rows, j : j + cols].astype(jnp.float32) * kern[i, j]
    return total


def back_conv(grad_pad, kern):
    rows = grad_pad.shape[0] - 6
    cols = grad_pad.shape[1]
    wide = jnp.pad(grad_pad, ((0, 0), (3, 3), (0, 0)))
    total = jnp.zeros((rows, cols, grad_pad.shape[2]), jnp.float32)
    for i in range(kern.shape[0]):
        for j in range(kern.shape[1]):
            total = (
                total
                + wide[6 - i : 6 - i + rows, 6 - j : 6 - j + cols].astype(jnp.float32) * kern[i, j]
            )
    return total


def kern_grad(framed, grad_rows):
    rows = grad_rows.shape[0]
    cols = grad_rows.shape[1]
    wide = jnp.pad(framed, ((0, 0), (3, 3), (0, 0)))
    grad_f = grad_rows.astype(jnp.float32)
    parts = []
    for i in range(7):
        for j in range(7):
            parts.append(
                jnp.sum(wide[i : i + rows, j : j + cols].astype(jnp.float32) * grad_f, axis=(0, 1))
            )
    return jnp.stack(parts).reshape(7, 7, grad_rows.shape[2])


def apply_layer_norm(activation_rows, scale_factor, offset_bias):
    centered_input = activation_rows - jnp.mean(activation_rows, axis=-1, keepdims=True)
    inverse_deviation = lax.rsqrt(
        jnp.mean(centered_input * centered_input, axis=-1, keepdims=True) + 1e-06
    )
    standardized_input = centered_input * inverse_deviation
    return (
        (standardized_input * scale_factor + offset_bias).astype(jnp.bfloat16),
        standardized_input,
        inverse_deviation,
    )


def gelu_grad(value):
    return (
        0.5 * (1.0 + jax.scipy.special.erf(value * 0.7071067811865476))
        + value * jnp.exp(-0.5 * value * value) * 0.3989422804014327
    )


def layer_norm_backward(normed_input_gradient, scale_factor, standardized_input, inverse_deviation):
    scaled_output = normed_input_gradient * scale_factor
    return (
        inverse_deviation
        * (
            scaled_output
            - jnp.mean(scaled_output, axis=-1, keepdims=True)
            - standardized_input
            * jnp.mean(scaled_output * standardized_input, axis=-1, keepdims=True)
        )
    ).astype(jnp.bfloat16)


def body(
    ring,
    frames,
    kernel,
    kernel_bias,
    layer_norm_weight,
    layer_norm_bias,
    up_weight,
    up_bias,
    grn_gamma,
    grn_beta,
    grad_out,
):
    slab = frames[0]
    chans = slab.shape[2]
    padded = extended(slab, (("rows", 0),), 3)
    own_block, padded = lax.optimization_barrier((up_weight, padded))
    columns = ring_all_gather(own_block, "fsdp", ring)
    activation_rows = conv_rows(padded, kernel, kernel_bias)
    normed_output, standardized_input, inverse_deviation = apply_layer_norm(
        activation_rows, layer_norm_weight, layer_norm_bias
    )
    whole = tree_all_gather(normed_output, "rows")
    height = whole.shape[0]
    cols = whole.shape[1]
    flat = whole.reshape(-1, chans)
    pre = jnp.dot(flat, columns, preferred_element_type=jnp.float32) + up_bias
    post = jax.nn.gelu(pre, approximate=False)
    norms = jnp.sqrt(jnp.sum(post * post, axis=0) + 1e-06)
    cot_f = grad_out[0].reshape(flat.shape[0], -1).astype(jnp.float32)
    dnorm = grn_gamma * jnp.sum(cot_f * post, axis=0)
    norm_total = lax.psum(jnp.sum(norms), "rows")
    denom = norm_total / FF + 1e-06
    ratio = norms / denom
    output = (grn_gamma * (post * ratio) + grn_beta + post).astype(jnp.bfloat16)
    cross = lax.psum(jnp.sum(dnorm * norms), "rows")
    dnorms = dnorm / denom - cross / (denom * denom) / FF
    dpost = cot_f * (1.0 + grn_gamma * ratio) + post * (dnorms / norms)
    dpre = (dpost * gelu_grad(pre)).astype(jnp.bfloat16)
    w_term = lax.dot_general(
        flat, dpre, (((0,), (0,)), ((), ())), preferred_element_type=jnp.float32
    )
    up_grad = lax.psum_scatter(
        w_term.astype(jnp.bfloat16), "fsdp", scatter_dimension=0, tiled=True
    ).astype(jnp.float32)
    dpre_rows = dpre.reshape(height, cols, -1)
    group_terms = jnp.einsum(
        "hwf,cf->hwc", dpre_rows, columns, preferred_element_type=jnp.float32
    ).astype(jnp.bfloat16)
    n_rows = lax.axis_size("rows")
    normed_input_gradient = tree_reduce_scatter(
        group_terms.reshape((n_rows, height // n_rows) + group_terms.shape[1:]), "rows"
    )
    activation_gradient = layer_norm_backward(
        normed_input_gradient, layer_norm_weight, standardized_input, inverse_deviation
    )
    grad_pad = extended(activation_gradient, (("rows", 0),), 3)
    dframe = back_conv(grad_pad, kernel).astype(jnp.bfloat16)
    kernel_local = kern_grad(padded, activation_gradient)
    kernel_total = tree_allreduce(kernel_local, ("rows", "fsdp"))
    activation = output.reshape(1, height, cols, -1)
    return (activation, dframe.reshape((1,) + dframe.shape), up_grad, kernel_total)


def solution(mesh):
    placed = (
        P("fsdp", "rows", None, None),
        P(),
        P(),
        P(),
        P(),
        P("fsdp", "rows"),
        P("rows"),
        P("rows"),
        P("rows"),
        P("fsdp", None, None, "rows"),
    )
    return jax.shard_map(
        functools.partial(body, fsdp_ring(mesh)),
        mesh=mesh,
        in_specs=placed,
        out_specs=(
            P("fsdp", None, None, "rows"),
            P("fsdp", "rows", None, None),
            P("fsdp", "rows"),
            P(),
        ),
        check_vma=False,
    )
```

```python
import functools

import jax
import jax.numpy as jnp
from jax import lax
from jax.sharding import PartitionSpec as P

FF = 6144


def extended(block, sides, width):
    for axis, dim in sides:
        count = lax.axis_size(axis)
        forward = [(i, i + 1) for i in range(count - 1)]
        backward = [(target, source) for source, target in forward]
        low = lax.ppermute(
            lax.slice_in_dim(block, block.shape[dim] - width, None, axis=dim), axis, forward
        )
        high = lax.ppermute(lax.slice_in_dim(block, 0, width, axis=dim), axis, backward)
        block = jnp.concatenate([low, block, high], axis=dim)
    return block


def _bit_steps(axes):
    steps = []
    for axis in axes:
        size = lax.axis_size(axis)
        assert size & (size - 1) == 0
        mask = 1
        while mask < size:
            steps.append((axis, mask, size))
            mask *= 2
    return steps


def tree_allreduce(value, axes):
    shape = value.shape
    flat = value.reshape(-1)
    steps = _bit_steps(axes)
    assert flat.shape[0] % (1 << len(steps)) == 0
    bits = []
    for axis, mask, size in steps:
        bit = (lax.axis_index(axis) // mask) % 2
        bits.append(bit)
        halves = flat.reshape(2, -1)
        keep = lax.dynamic_index_in_dim(halves, bit, keepdims=False)
        give = lax.dynamic_index_in_dim(halves, 1 - bit, keepdims=False)
        perm = [(j, j ^ mask) for j in range(size)]
        flat = keep + lax.ppermute(give, axis, perm)
    for (axis, mask, size), bit in reversed(list(zip(steps, bits))):
        perm = [(j, j ^ mask) for j in range(size)]
        other = lax.ppermute(flat, axis, perm)
        flat = jnp.where(bit == 0, jnp.concatenate([flat, other]), jnp.concatenate([other, flat]))
    return flat.reshape(shape)


def tree_reduce_scatter(chunks, axis):
    size = lax.axis_size(axis)
    assert chunks.shape[0] == size and size & (size - 1) == 0
    me = lax.axis_index(axis)
    data = chunks
    mask = 1
    while mask < size:
        bit = (me // mask) % 2
        pairs = data.reshape((data.shape[0] // 2, 2) + data.shape[1:])
        keep = lax.dynamic_index_in_dim(pairs, bit, axis=1, keepdims=False)
        give = lax.dynamic_index_in_dim(pairs, 1 - bit, axis=1, keepdims=False)
        perm = [(j, j ^ mask) for j in range(size)]
        data = keep.astype(jnp.float32) + lax.ppermute(give, axis, perm).astype(jnp.float32)
        mask *= 2
    return data[0]


def fsdp_ring(mesh):
    count = mesh.shape["fsdp"]
    try:
        members = [mesh.devices[j, 0] for j in range(count)]
        spots = [(d.coords[2], d.coords[1]) for d in members]
        zs = sorted({z for z, _ in spots})
        ys = sorted({y for _, y in spots})
        rows_a, cols_b = len(zs), len(ys)
        where = {(zs.index(z), ys.index(y)): j for j, (z, y) in enumerate(spots)}
        assert len(where) == count == rows_a * cols_b and rows_a % 2 == 0 and cols_b >= 2
        cells = [(a, 0) for a in range(rows_a)]
        for k, a in enumerate(range(rows_a - 1, -1, -1)):
            span = range(1, cols_b) if k % 2 == 0 else range(cols_b - 1, 0, -1)
            cells += [(a, b) for b in span]
        ring = [where[c] for c in cells]
        assert sorted(ring) == list(range(count))
    except Exception:
        ring = list(range(count))
    return ring


def ring_all_gather(block, axis, ring, held=None):
    count = len(ring)
    place = [0] * count
    for k, j in enumerate(ring):
        place[j] = k
    ring_arr = jnp.array(ring, jnp.int32)
    me = lax.axis_index(axis)
    spot = jnp.array(place, jnp.int32)[me]
    forward = [(ring[k], ring[(k + 1) % count]) for k in range(count)]
    backward = [(ring[k], ring[(k - 1) % count]) for k in range(count)]
    ahead = count // 2
    behind = count - 1 - ahead
    gathered = jnp.zeros((count,) + block.shape, block.dtype)
    gathered = lax.dynamic_update_index_in_dim(gathered, block, me, 0)
    cw = block
    ccw = block
    for s in range(1, ahead + 1):
        cw = lax.ppermute(cw, axis, forward)
        if s <= behind:
            ccw = lax.ppermute(ccw, axis, backward)
        if s == 1 and held is not None:
            cw, ccw, held = lax.optimization_barrier((cw, ccw, held))
        gathered = lax.dynamic_update_index_in_dim(gathered, cw, ring_arr[(spot - s) % count], 0)
        if s <= behind:
            gathered = lax.dynamic_update_index_in_dim(
                gathered, ccw, ring_arr[(spot + s) % count], 0
            )
    return gathered.reshape((count * block.shape[0],) + block.shape[1:]), held


def ring_reduce_scatter(terms, axis, ring):
    count = len(ring)
    place = [0] * count
    for k, j in enumerate(ring):
        place[j] = k
    ring_arr = jnp.array(ring, jnp.int32)
    me = lax.axis_index(axis)
    spot = jnp.array(place, jnp.int32)[me]
    forward = [(ring[k], ring[(k + 1) % count]) for k in range(count)]
    backward = [(ring[k], ring[(k - 1) % count]) for k in range(count)]
    ahead = count // 2
    behind = count - 1 - ahead

    def term(offset):
        return lax.dynamic_index_in_dim(terms, ring_arr[(spot + offset) % count], 0, keepdims=False)

    total = term(0).astype(jnp.float32)
    cw = term(ahead)
    ccw = term(-behind) if behind else None
    for s in range(1, ahead + 1):
        cw = lax.ppermute(cw, axis, forward)
        if s <= behind:
            ccw = lax.ppermute(ccw, axis, backward)
        if s < ahead:
            cw = (cw.astype(jnp.float32) + term(ahead - s).astype(jnp.float32)).astype(terms.dtype)
        else:
            total = total + cw.astype(jnp.float32)
        if s < behind:
            ccw = (ccw.astype(jnp.float32) + term(s - behind).astype(jnp.float32)).astype(terms.dtype)
        elif s == behind:
            total = total + ccw.astype(jnp.float32)
    return total


def tree_all_gather(block, axis):
    size = lax.axis_size(axis)
    assert size & (size - 1) == 0
    me = lax.axis_index(axis)
    data = block[None]
    mask = 1
    while mask < size:
        bit = (me // mask) % 2
        perm = [(j, j ^ mask) for j in range(size)]
        other = lax.ppermute(data, axis, perm)
        data = jnp.where(bit == 0, jnp.concatenate([data, other]), jnp.concatenate([other, data]))
        mask *= 2
    return data.reshape((size * block.shape[0],) + block.shape[1:])


def conv_rows(framed, kern, kbias):
    rows = framed.shape[0] - 6
    cols = framed.shape[1]
    wide = jnp.pad(framed, ((0, 0), (3, 3), (0, 0)))
    total = jnp.zeros((rows, cols, framed.shape[2]), jnp.float32) + kbias
    for i in range(kern.shape[0]):
        for j in range(kern.shape[1]):
            total = total + wide[i : i + rows, j : j + cols].astype(jnp.float32) * kern[i, j]
    return total


def back_conv(grad_pad, kern):
    rows = grad_pad.shape[0] - 6
    cols = grad_pad.shape[1]
    wide = jnp.pad(grad_pad, ((0, 0), (3, 3), (0, 0)))
    total = jnp.zeros((rows, cols, grad_pad.shape[2]), jnp.float32)
    for i in range(kern.shape[0]):
        for j in range(kern.shape[1]):
            total = (
                total
                + wide[6 - i : 6 - i + rows, 6 - j : 6 - j + cols].astype(jnp.float32) * kern[i, j]
            )
    return total


def kern_grad(framed, grad_rows):
    rows = grad_rows.shape[0]
    cols = grad_rows.shape[1]
    wide = jnp.pad(framed, ((0, 0), (3, 3), (0, 0)))
    grad_f = grad_rows.astype(jnp.float32)
    parts = []
    for i in range(7):
        for j in range(7):
            parts.append(
                jnp.sum(wide[i : i + rows, j : j + cols].astype(jnp.float32) * grad_f, axis=(0, 1))
            )
    return jnp.stack(parts).reshape(7, 7, grad_rows.shape[2])


def apply_layer_norm(activation_rows, scale_factor, offset_bias):
    centered_input = activation_rows - jnp.mean(activation_rows, axis=-1, keepdims=True)
    inverse_deviation = lax.rsqrt(
        jnp.mean(centered_input * centered_input, axis=-1, keepdims=True) + 1e-06
    )
    standardized_input = centered_input * inverse_deviation
    return (
        (standardized_input * scale_factor + offset_bias).astype(jnp.bfloat16),
        standardized_input,
        inverse_deviation,
    )


def gelu_grad(value):
    return (
        0.5 * (1.0 + jax.scipy.special.erf(value * 0.7071067811865476))
        + value * jnp.exp(-0.5 * value * value) * 0.3989422804014327
    )


def layer_norm_backward(normed_input_gradient, scale_factor, standardized_input, inverse_deviation):
    scaled_output = normed_input_gradient * scale_factor
    return (
        inverse_deviation
        * (
            scaled_output
            - jnp.mean(scaled_output, axis=-1, keepdims=True)
            - standardized_input
            * jnp.mean(scaled_output * standardized_input, axis=-1, keepdims=True)
        )
    ).astype(jnp.bfloat16)


def body(
    ring,
    frames,
    kernel,
    kernel_bias,
    layer_norm_weight,
    layer_norm_bias,
    up_weight,
    up_bias,
    grn_gamma,
    grn_beta,
    grad_out,
):
    slab = frames[0]
    chans = slab.shape[2]
    columns, slab = ring_all_gather(up_weight, "fsdp", ring, slab)
    padded = extended(slab, (("rows", 0),), 3)
    activation_rows = conv_rows(padded, kernel, kernel_bias)
    normed_output, standardized_input, inverse_deviation = apply_layer_norm(
        activation_rows, layer_norm_weight, layer_norm_bias
    )
    whole = tree_all_gather(normed_output, "rows")
    height = whole.shape[0]
    cols = whole.shape[1]
    flat = whole.reshape(-1, chans)
    pre = jnp.dot(flat, columns, preferred_element_type=jnp.float32) + up_bias
    post = jax.nn.gelu(pre, approximate=False)
    norms = jnp.sqrt(jnp.sum(post * post, axis=0) + 1e-06)
    cot_f = grad_out[0].reshape(flat.shape[0], -1).astype(jnp.float32)
    dnorm = grn_gamma * jnp.sum(cot_f * post, axis=0)
    norm_total = lax.psum(jnp.sum(norms), "rows")
    denom = norm_total / FF + 1e-06
    ratio = norms / denom
    output = (grn_gamma * (post * ratio) + grn_beta + post).astype(jnp.bfloat16)
    cross = lax.psum(jnp.sum(dnorm * norms), "rows")
    dnorms = dnorm / denom - cross / (denom * denom) / FF
    dpost = cot_f * (1.0 + grn_gamma * ratio) + post * (dnorms / norms)
    dpre = (dpost * gelu_grad(pre)).astype(jnp.bfloat16)
    w_term = lax.dot_general(
        flat, dpre, (((0,), (0,)), ((), ())), preferred_element_type=jnp.float32
    )
    up_grad = lax.psum_scatter(
        w_term.astype(jnp.bfloat16), "fsdp", scatter_dimension=0, tiled=True
    ).astype(jnp.float32)
    dpre_rows = dpre.reshape(height, cols, -1)
    group_terms = jnp.einsum(
        "hwf,cf->hwc", dpre_rows, columns, preferred_element_type=jnp.float32
    ).astype(jnp.bfloat16)
    n_rows = lax.axis_size("rows")
    normed_input_gradient = tree_reduce_scatter(
        group_terms.reshape((n_rows, height // n_rows) + group_terms.shape[1:]), "rows"
    )
    activation_gradient = layer_norm_backward(
        normed_input_gradient, layer_norm_weight, standardized_input, inverse_deviation
    )
    grad_pad = extended(activation_gradient, (("rows", 0),), 3)
    dframe = back_conv(grad_pad, kernel).astype(jnp.bfloat16)
    kernel_local = kern_grad(padded, activation_gradient)
    kernel_total = tree_allreduce(kernel_local, ("rows", "fsdp"))
    activation = output.reshape(1, height, cols, -1)
    return (activation, dframe.reshape((1,) + dframe.shape), up_grad, kernel_total)


def solution(mesh):
    placed = (
        P("fsdp", "rows", None, None),
        P(),
        P(),
        P(),
        P(),
        P("fsdp", "rows"),
        P("rows"),
        P("rows"),
        P("rows"),
        P("fsdp", None, None, "rows"),
    )
    return jax.shard_map(
        functools.partial(body, fsdp_ring(mesh)),
        mesh=mesh,
        in_specs=placed,
        out_specs=(
            P("fsdp", None, None, "rows"),
            P("fsdp", "rows", None, None),
            P("fsdp", "rows"),
            P(),
        ),
        check_vma=False,
    )
```

```python
import functools

import jax
import jax.numpy as jnp
from jax import lax
from jax.sharding import PartitionSpec as P

FF = 6144


def extended(block, sides, width):
    for axis, dim in sides:
        count = lax.axis_size(axis)
        forward = [(i, i + 1) for i in range(count - 1)]
        backward = [(target, source) for source, target in forward]
        low = lax.ppermute(
            lax.slice_in_dim(block, block.shape[dim] - width, None, axis=dim), axis, forward
        )
        high = lax.ppermute(lax.slice_in_dim(block, 0, width, axis=dim), axis, backward)
        block = jnp.concatenate([low, block, high], axis=dim)
    return block


def _bit_steps(axes):
    steps = []
    for axis in axes:
        size = lax.axis_size(axis)
        assert size & (size - 1) == 0
        mask = 1
        while mask < size:
            steps.append((axis, mask, size))
            mask *= 2
    return steps


def tree_allreduce(value, axes):
    shape = value.shape
    flat = value.reshape(-1)
    steps = _bit_steps(axes)
    assert flat.shape[0] % (1 << len(steps)) == 0
    bits = []
    for axis, mask, size in steps:
        bit = (lax.axis_index(axis) // mask) % 2
        bits.append(bit)
        halves = flat.reshape(2, -1)
        keep = lax.dynamic_index_in_dim(halves, bit, keepdims=False)
        give = lax.dynamic_index_in_dim(halves, 1 - bit, keepdims=False)
        perm = [(j, j ^ mask) for j in range(size)]
        flat = keep + lax.ppermute(give, axis, perm)
    for (axis, mask, size), bit in reversed(list(zip(steps, bits))):
        perm = [(j, j ^ mask) for j in range(size)]
        other = lax.ppermute(flat, axis, perm)
        flat = jnp.where(bit == 0, jnp.concatenate([flat, other]), jnp.concatenate([other, flat]))
    return flat.reshape(shape)


def tree_reduce_scatter(chunks, axis):
    size = lax.axis_size(axis)
    assert chunks.shape[0] == size and size & (size - 1) == 0
    me = lax.axis_index(axis)
    data = chunks
    mask = 1
    while mask < size:
        bit = (me // mask) % 2
        pairs = data.reshape((data.shape[0] // 2, 2) + data.shape[1:])
        keep = lax.dynamic_index_in_dim(pairs, bit, axis=1, keepdims=False)
        give = lax.dynamic_index_in_dim(pairs, 1 - bit, axis=1, keepdims=False)
        perm = [(j, j ^ mask) for j in range(size)]
        data = keep.astype(jnp.float32) + lax.ppermute(give, axis, perm).astype(jnp.float32)
        mask *= 2
    return data[0]


def fsdp_ring(mesh):
    count = mesh.shape["fsdp"]
    try:
        members = [mesh.devices[j, 0] for j in range(count)]
        spots = [(d.coords[2], d.coords[1]) for d in members]
        zs = sorted({z for z, _ in spots})
        ys = sorted({y for _, y in spots})
        rows_a, cols_b = len(zs), len(ys)
        where = {(zs.index(z), ys.index(y)): j for j, (z, y) in enumerate(spots)}
        assert len(where) == count == rows_a * cols_b and rows_a % 2 == 0 and cols_b >= 2
        cells = [(a, 0) for a in range(rows_a)]
        for k, a in enumerate(range(rows_a - 1, -1, -1)):
            span = range(1, cols_b) if k % 2 == 0 else range(cols_b - 1, 0, -1)
            cells += [(a, b) for b in span]
        ring = [where[c] for c in cells]
        assert sorted(ring) == list(range(count))
    except Exception:
        ring = list(range(count))
    return ring


def ring_all_gather(block, axis, ring, held=None):
    count = len(ring)
    place = [0] * count
    for k, j in enumerate(ring):
        place[j] = k
    ring_arr = jnp.array(ring, jnp.int32)
    me = lax.axis_index(axis)
    spot = jnp.array(place, jnp.int32)[me]
    forward = [(ring[k], ring[(k + 1) % count]) for k in range(count)]
    backward = [(ring[k], ring[(k - 1) % count]) for k in range(count)]
    ahead = count // 2
    behind = count - 1 - ahead
    gathered = jnp.zeros((count,) + block.shape, block.dtype)
    gathered = lax.dynamic_update_index_in_dim(gathered, block, me, 0)
    cw = block
    ccw = block
    for s in range(1, ahead + 1):
        cw = lax.ppermute(cw, axis, forward)
        if s <= behind:
            ccw = lax.ppermute(ccw, axis, backward)
        if s == 1 and held is not None:
            cw, ccw, held = lax.optimization_barrier((cw, ccw, held))
        gathered = lax.dynamic_update_index_in_dim(gathered, cw, ring_arr[(spot - s) % count], 0)
        if s <= behind:
            gathered = lax.dynamic_update_index_in_dim(
                gathered, ccw, ring_arr[(spot + s) % count], 0
            )
    return gathered.reshape((count * block.shape[0],) + block.shape[1:]), held


def ring_reduce_scatter(terms, axis, ring):
    count = len(ring)
    place = [0] * count
    for k, j in enumerate(ring):
        place[j] = k
    ring_arr = jnp.array(ring, jnp.int32)
    me = lax.axis_index(axis)
    spot = jnp.array(place, jnp.int32)[me]
    forward = [(ring[k], ring[(k + 1) % count]) for k in range(count)]
    backward = [(ring[k], ring[(k - 1) % count]) for k in range(count)]
    ahead = count // 2
    behind = count - 1 - ahead

    def term(offset):
        return lax.dynamic_index_in_dim(terms, ring_arr[(spot + offset) % count], 0, keepdims=False)

    total = term(0).astype(jnp.float32)
    cw = term(ahead)
    ccw = term(-behind) if behind else None
    for s in range(1, ahead + 1):
        cw = lax.ppermute(cw, axis, forward)
        if s <= behind:
            ccw = lax.ppermute(ccw, axis, backward)
        if s < ahead:
            cw = (cw.astype(jnp.float32) + term(ahead - s).astype(jnp.float32)).astype(terms.dtype)
        else:
            total = total + cw.astype(jnp.float32)
        if s < behind:
            ccw = (ccw.astype(jnp.float32) + term(s - behind).astype(jnp.float32)).astype(terms.dtype)
        elif s == behind:
            total = total + ccw.astype(jnp.float32)
    return total


def tree_all_gather(block, axis):
    size = lax.axis_size(axis)
    assert size & (size - 1) == 0
    me = lax.axis_index(axis)
    data = block[None]
    mask = 1
    while mask < size:
        bit = (me // mask) % 2
        perm = [(j, j ^ mask) for j in range(size)]
        other = lax.ppermute(data, axis, perm)
        data = jnp.where(bit == 0, jnp.concatenate([data, other]), jnp.concatenate([other, data]))
        mask *= 2
    return data.reshape((size * block.shape[0],) + block.shape[1:])


def conv_rows(framed, kern, kbias):
    rows = framed.shape[0] - 6
    cols = framed.shape[1]
    wide = jnp.pad(framed, ((0, 0), (3, 3), (0, 0)))
    total = jnp.zeros((rows, cols, framed.shape[2]), jnp.float32) + kbias
    for i in range(kern.shape[0]):
        for j in range(kern.shape[1]):
            total = total + wide[i : i + rows, j : j + cols].astype(jnp.float32) * kern[i, j]
    return total


def back_conv(grad_pad, kern):
    rows = grad_pad.shape[0] - 6
    cols = grad_pad.shape[1]
    wide = jnp.pad(grad_pad, ((0, 0), (3, 3), (0, 0)))
    total = jnp.zeros((rows, cols, grad_pad.shape[2]), jnp.float32)
    for i in range(kern.shape[0]):
        for j in range(kern.shape[1]):
            total = (
                total
                + wide[6 - i : 6 - i + rows, 6 - j : 6 - j + cols].astype(jnp.float32) * kern[i, j]
            )
    return total


def kern_grad(framed, grad_rows):
    rows = grad_rows.shape[0]
    cols = grad_rows.shape[1]
    wide = jnp.pad(framed, ((0, 0), (3, 3), (0, 0)))
    grad_f = grad_rows.astype(jnp.float32)
    parts = []
    for i in range(7):
        for j in range(7):
            parts.append(
                jnp.sum(wide[i : i + rows, j : j + cols].astype(jnp.float32) * grad_f, axis=(0, 1))
            )
    return jnp.stack(parts).reshape(7, 7, grad_rows.shape[2])


def apply_layer_norm(activation_rows, scale_factor, offset_bias):
    centered_input = activation_rows - jnp.mean(activation_rows, axis=-1, keepdims=True)
    inverse_deviation = lax.rsqrt(
        jnp.mean(centered_input * centered_input, axis=-1, keepdims=True) + 1e-06
    )
    standardized_input = centered_input * inverse_deviation
    return (
        (standardized_input * scale_factor + offset_bias).astype(jnp.bfloat16),
        standardized_input,
        inverse_deviation,
    )


def gelu_grad(value):
    return (
        0.5 * (1.0 + jax.scipy.special.erf(value * 0.7071067811865476))
        + value * jnp.exp(-0.5 * value * value) * 0.3989422804014327
    )


def layer_norm_backward(normed_input_gradient, scale_factor, standardized_input, inverse_deviation):
    scaled_output = normed_input_gradient * scale_factor
    return (
        inverse_deviation
        * (
            scaled_output
            - jnp.mean(scaled_output, axis=-1, keepdims=True)
            - standardized_input
            * jnp.mean(scaled_output * standardized_input, axis=-1, keepdims=True)
        )
    ).astype(jnp.bfloat16)


def body(
    ring,
    frames,
    kernel,
    kernel_bias,
    layer_norm_weight,
    layer_norm_bias,
    up_weight,
    up_bias,
    grn_gamma,
    grn_beta,
    grad_out,
):
    slab = frames[0]
    chans = slab.shape[2]
    columns, slab = ring_all_gather(up_weight, "fsdp", ring, slab)
    padded = extended(slab, (("rows", 0),), 3)
    activation_rows = conv_rows(padded, kernel, kernel_bias)
    normed_output, standardized_input, inverse_deviation = apply_layer_norm(
        activation_rows, layer_norm_weight, layer_norm_bias
    )
    whole = tree_all_gather(normed_output, "rows")
    height = whole.shape[0]
    cols = whole.shape[1]
    flat = whole.reshape(-1, chans)
    pre = jnp.dot(flat, columns, preferred_element_type=jnp.float32) + up_bias
    post = jax.nn.gelu(pre, approximate=False)
    norms = jnp.sqrt(jnp.sum(post * post, axis=0) + 1e-06)
    cot_f = grad_out[0].reshape(flat.shape[0], -1).astype(jnp.float32)
    dnorm = grn_gamma * jnp.sum(cot_f * post, axis=0)
    norm_total = lax.psum(jnp.sum(norms), "rows")
    denom = norm_total / FF + 1e-06
    ratio = norms / denom
    output = (grn_gamma * (post * ratio) + grn_beta + post).astype(jnp.bfloat16)
    cross = lax.psum(jnp.sum(dnorm * norms), "rows")
    dnorms = dnorm / denom - cross / (denom * denom) / FF
    dpost = cot_f * (1.0 + grn_gamma * ratio) + post * (dnorms / norms)
    dpre = (dpost * gelu_grad(pre)).astype(jnp.bfloat16)
    w_term = lax.dot_general(
        flat, dpre, (((0,), (0,)), ((), ())), preferred_element_type=jnp.float32
    )
    n_fsdp = lax.axis_size("fsdp")
    w_bf = w_term.astype(jnp.bfloat16)
    keep = w_bf.shape[1] - (w_bf.shape[1] // 3) // 128 * 128
    up_grad = jnp.concatenate(
        [
            lax.psum_scatter(w_bf[:, :keep], "fsdp", scatter_dimension=0, tiled=True).astype(
                jnp.float32
            ),
            ring_reduce_scatter(
                w_bf[:, keep:].reshape((n_fsdp, chans // n_fsdp, -1)), "fsdp", ring
            ),
        ],
        axis=1,
    )
    dpre_rows = dpre.reshape(height, cols, -1)
    group_terms = jnp.einsum(
        "hwf,cf->hwc", dpre_rows, columns, preferred_element_type=jnp.float32
    ).astype(jnp.bfloat16)
    n_rows = lax.axis_size("rows")
    normed_input_gradient = tree_reduce_scatter(
        group_terms.reshape((n_rows, height // n_rows) + group_terms.shape[1:]), "rows"
    )
    activation_gradient = layer_norm_backward(
        normed_input_gradient, layer_norm_weight, standardized_input, inverse_deviation
    )
    grad_pad = extended(activation_gradient, (("rows", 0),), 3)
    dframe = back_conv(grad_pad, kernel).astype(jnp.bfloat16)
    kernel_local = kern_grad(padded, activation_gradient)
    kernel_total = tree_allreduce(kernel_local, ("rows", "fsdp"))
    activation = output.reshape(1, height, cols, -1)
    return (activation, dframe.reshape((1,) + dframe.shape), up_grad, kernel_total)


def solution(mesh):
    placed = (
        P("fsdp", "rows", None, None),
        P(),
        P(),
        P(),
        P(),
        P("fsdp", "rows"),
        P("rows"),
        P("rows"),
        P("rows"),
        P("fsdp", None, None, "rows"),
    )
    return jax.shard_map(
        functools.partial(body, fsdp_ring(mesh)),
        mesh=mesh,
        in_specs=placed,
        out_specs=(
            P("fsdp", None, None, "rows"),
            P("fsdp", "rows", None, None),
            P("fsdp", "rows"),
            P(),
        ),
        check_vma=False,
    )
```

```python
import functools

import jax
import jax.numpy as jnp
from jax import lax
from jax.sharding import PartitionSpec as P

FF = 6144


def extended(block, sides, width):
    for axis, dim in sides:
        count = lax.axis_size(axis)
        forward = [(i, i + 1) for i in range(count - 1)]
        backward = [(target, source) for source, target in forward]
        low = lax.ppermute(
            lax.slice_in_dim(block, block.shape[dim] - width, None, axis=dim), axis, forward
        )
        high = lax.ppermute(lax.slice_in_dim(block, 0, width, axis=dim), axis, backward)
        block = jnp.concatenate([low, block, high], axis=dim)
    return block


def _bit_steps(axes):
    steps = []
    for axis in axes:
        size = lax.axis_size(axis)
        assert size & (size - 1) == 0
        mask = 1
        while mask < size:
            steps.append((axis, mask, size))
            mask *= 2
    return steps


def tree_allreduce(value, axes):
    shape = value.shape
    flat = value.reshape(-1)
    steps = _bit_steps(axes)
    assert flat.shape[0] % (1 << len(steps)) == 0
    bits = []
    for axis, mask, size in steps:
        bit = (lax.axis_index(axis) // mask) % 2
        bits.append(bit)
        halves = flat.reshape(2, -1)
        keep = lax.dynamic_index_in_dim(halves, bit, keepdims=False)
        give = lax.dynamic_index_in_dim(halves, 1 - bit, keepdims=False)
        perm = [(j, j ^ mask) for j in range(size)]
        flat = keep + lax.ppermute(give, axis, perm)
    for (axis, mask, size), bit in reversed(list(zip(steps, bits))):
        perm = [(j, j ^ mask) for j in range(size)]
        other = lax.ppermute(flat, axis, perm)
        flat = jnp.where(bit == 0, jnp.concatenate([flat, other]), jnp.concatenate([other, flat]))
    return flat.reshape(shape)


def tree_reduce_scatter(chunks, axis):
    size = lax.axis_size(axis)
    assert chunks.shape[0] == size and size & (size - 1) == 0
    me = lax.axis_index(axis)
    data = chunks
    mask = 1
    while mask < size:
        bit = (me // mask) % 2
        pairs = data.reshape((data.shape[0] // 2, 2) + data.shape[1:])
        keep = lax.dynamic_index_in_dim(pairs, bit, axis=1, keepdims=False)
        give = lax.dynamic_index_in_dim(pairs, 1 - bit, axis=1, keepdims=False)
        perm = [(j, j ^ mask) for j in range(size)]
        data = keep.astype(jnp.float32) + lax.ppermute(give, axis, perm).astype(jnp.float32)
        mask *= 2
    return data[0]


def fsdp_ring(mesh):
    count = mesh.shape["fsdp"]
    try:
        members = [mesh.devices[j, 0] for j in range(count)]
        spots = [(d.coords[2], d.coords[1]) for d in members]
        zs = sorted({z for z, _ in spots})
        ys = sorted({y for _, y in spots})
        rows_a, cols_b = len(zs), len(ys)
        where = {(zs.index(z), ys.index(y)): j for j, (z, y) in enumerate(spots)}
        assert len(where) == count == rows_a * cols_b and rows_a % 2 == 0 and cols_b >= 2
        cells = [(a, 0) for a in range(rows_a)]
        for k, a in enumerate(range(rows_a - 1, -1, -1)):
            span = range(1, cols_b) if k % 2 == 0 else range(cols_b - 1, 0, -1)
            cells += [(a, b) for b in span]
        ring = [where[c] for c in cells]
        assert sorted(ring) == list(range(count))
    except Exception:
        ring = list(range(count))
    return ring


def ring_all_gather(block, axis, ring, held=None):
    count = len(ring)
    place = [0] * count
    for k, j in enumerate(ring):
        place[j] = k
    ring_arr = jnp.array(ring, jnp.int32)
    me = lax.axis_index(axis)
    spot = jnp.array(place, jnp.int32)[me]
    forward = [(ring[k], ring[(k + 1) % count]) for k in range(count)]
    backward = [(ring[k], ring[(k - 1) % count]) for k in range(count)]
    ahead = count // 2
    behind = count - 1 - ahead
    gathered = jnp.zeros((count,) + block.shape, block.dtype)
    gathered = lax.dynamic_update_index_in_dim(gathered, block, me, 0)
    cw = block
    ccw = block
    for s in range(1, ahead + 1):
        cw = lax.ppermute(cw, axis, forward)
        if s <= behind:
            ccw = lax.ppermute(ccw, axis, backward)
        if s == 1 and held is not None:
            cw, ccw, held = lax.optimization_barrier((cw, ccw, held))
        gathered = lax.dynamic_update_index_in_dim(gathered, cw, ring_arr[(spot - s) % count], 0)
        if s <= behind:
            gathered = lax.dynamic_update_index_in_dim(
                gathered, ccw, ring_arr[(spot + s) % count], 0
            )
    return gathered.reshape((count * block.shape[0],) + block.shape[1:]), held


def ring_reduce_scatter(terms, axis, ring):
    count = len(ring)
    place = [0] * count
    for k, j in enumerate(ring):
        place[j] = k
    ring_arr = jnp.array(ring, jnp.int32)
    me = lax.axis_index(axis)
    spot = jnp.array(place, jnp.int32)[me]
    forward = [(ring[k], ring[(k + 1) % count]) for k in range(count)]
    backward = [(ring[k], ring[(k - 1) % count]) for k in range(count)]
    ahead = count // 2
    behind = count - 1 - ahead

    def term(offset):
        return lax.dynamic_index_in_dim(terms, ring_arr[(spot + offset) % count], 0, keepdims=False)

    total = term(0).astype(jnp.float32)
    cw = term(ahead)
    ccw = term(-behind) if behind else None
    for s in range(1, ahead + 1):
        cw = lax.ppermute(cw, axis, forward)
        if s <= behind:
            ccw = lax.ppermute(ccw, axis, backward)
        if s < ahead:
            cw = (cw.astype(jnp.float32) + term(ahead - s).astype(jnp.float32)).astype(terms.dtype)
        else:
            total = total + cw.astype(jnp.float32)
        if s < behind:
            ccw = (ccw.astype(jnp.float32) + term(s - behind).astype(jnp.float32)).astype(terms.dtype)
        elif s == behind:
            total = total + ccw.astype(jnp.float32)
    return total


def tree_all_gather(block, axis):
    size = lax.axis_size(axis)
    assert size & (size - 1) == 0
    me = lax.axis_index(axis)
    data = block[None]
    mask = 1
    while mask < size:
        bit = (me // mask) % 2
        perm = [(j, j ^ mask) for j in range(size)]
        other = lax.ppermute(data, axis, perm)
        data = jnp.where(bit == 0, jnp.concatenate([data, other]), jnp.concatenate([other, data]))
        mask *= 2
    return data.reshape((size * block.shape[0],) + block.shape[1:])


def conv_rows(framed, kern, kbias):
    rows = framed.shape[0] - 6
    cols = framed.shape[1]
    wide = jnp.pad(framed, ((0, 0), (3, 3), (0, 0)))
    total = jnp.zeros((rows, cols, framed.shape[2]), jnp.float32) + kbias
    for i in range(kern.shape[0]):
        for j in range(kern.shape[1]):
            total = total + wide[i : i + rows, j : j + cols].astype(jnp.float32) * kern[i, j]
    return total


def back_conv(grad_pad, kern):
    rows = grad_pad.shape[0] - 6
    cols = grad_pad.shape[1]
    wide = jnp.pad(grad_pad, ((0, 0), (3, 3), (0, 0)))
    total = jnp.zeros((rows, cols, grad_pad.shape[2]), jnp.float32)
    for i in range(kern.shape[0]):
        for j in range(kern.shape[1]):
            total = (
                total
                + wide[6 - i : 6 - i + rows, 6 - j : 6 - j + cols].astype(jnp.float32) * kern[i, j]
            )
    return total


def kern_grad(framed, grad_rows):
    rows = grad_rows.shape[0]
    cols = grad_rows.shape[1]
    wide = jnp.pad(framed, ((0, 0), (3, 3), (0, 0)))
    grad_f = grad_rows.astype(jnp.float32)
    parts = []
    for i in range(7):
        for j in range(7):
            parts.append(
                jnp.sum(wide[i : i + rows, j : j + cols].astype(jnp.float32) * grad_f, axis=(0, 1))
            )
    return jnp.stack(parts).reshape(7, 7, grad_rows.shape[2])


def apply_layer_norm(activation_rows, scale_factor, offset_bias):
    centered_input = activation_rows - jnp.mean(activation_rows, axis=-1, keepdims=True)
    inverse_deviation = lax.rsqrt(
        jnp.mean(centered_input * centered_input, axis=-1, keepdims=True) + 1e-06
    )
    standardized_input = centered_input * inverse_deviation
    return (
        (standardized_input * scale_factor + offset_bias).astype(jnp.bfloat16),
        standardized_input,
        inverse_deviation,
    )


def gelu_grad(value):
    return (
        0.5 * (1.0 + jax.scipy.special.erf(value * 0.7071067811865476))
        + value * jnp.exp(-0.5 * value * value) * 0.3989422804014327
    )


def layer_norm_backward(normed_input_gradient, scale_factor, standardized_input, inverse_deviation):
    scaled_output = normed_input_gradient * scale_factor
    return (
        inverse_deviation
        * (
            scaled_output
            - jnp.mean(scaled_output, axis=-1, keepdims=True)
            - standardized_input
            * jnp.mean(scaled_output * standardized_input, axis=-1, keepdims=True)
        )
    ).astype(jnp.bfloat16)


def body(
    ring,
    frames,
    kernel,
    kernel_bias,
    layer_norm_weight,
    layer_norm_bias,
    up_weight,
    up_bias,
    grn_gamma,
    grn_beta,
    grad_out,
):
    slab = frames[0]
    chans = slab.shape[2]
    columns, slab = ring_all_gather(up_weight, "fsdp", ring, slab)
    padded = extended(slab, (("rows", 0),), 3)
    activation_rows = conv_rows(padded, kernel, kernel_bias)
    normed_output, standardized_input, inverse_deviation = apply_layer_norm(
        activation_rows, layer_norm_weight, layer_norm_bias
    )
    whole = tree_all_gather(normed_output, "rows")
    height = whole.shape[0]
    cols = whole.shape[1]
    flat = whole.reshape(-1, chans)
    pre = jnp.dot(flat, columns, preferred_element_type=jnp.float32) + up_bias
    post = jax.nn.gelu(pre, approximate=False)
    norms = jnp.sqrt(jnp.sum(post * post, axis=0) + 1e-06)
    cot_f = grad_out[0].reshape(flat.shape[0], -1).astype(jnp.float32)
    dnorm = grn_gamma * jnp.sum(cot_f * post, axis=0)
    norm_total = lax.psum(jnp.sum(norms), "rows")
    denom = norm_total / FF + 1e-06
    ratio = norms / denom
    output = (grn_gamma * (post * ratio) + grn_beta + post).astype(jnp.bfloat16)
    cross = lax.psum(jnp.sum(dnorm * norms), "rows")
    dnorms = dnorm / denom - cross / (denom * denom) / FF
    dpost = cot_f * (1.0 + grn_gamma * ratio) + post * (dnorms / norms)
    dpre = (dpost * gelu_grad(pre)).astype(jnp.bfloat16)
    w_term = lax.dot_general(
        flat, dpre, (((0,), (0,)), ((), ())), preferred_element_type=jnp.float32
    )
    n_fsdp = lax.axis_size("fsdp")
    up_grad = ring_reduce_scatter(
        w_term.astype(jnp.bfloat16).reshape((n_fsdp, chans // n_fsdp, -1)), "fsdp", ring
    )
    dpre_rows = dpre.reshape(height, cols, -1)
    group_terms = jnp.einsum(
        "hwf,cf->hwc", dpre_rows, columns, preferred_element_type=jnp.float32
    ).astype(jnp.bfloat16)
    n_rows = lax.axis_size("rows")
    normed_input_gradient = tree_reduce_scatter(
        group_terms.reshape((n_rows, height // n_rows) + group_terms.shape[1:]), "rows"
    )
    activation_gradient = layer_norm_backward(
        normed_input_gradient, layer_norm_weight, standardized_input, inverse_deviation
    )
    grad_pad = extended(activation_gradient, (("rows", 0),), 3)
    dframe = back_conv(grad_pad, kernel).astype(jnp.bfloat16)
    kernel_local = kern_grad(padded, activation_gradient)
    n_rows = lax.axis_size("rows")
    kernel_part = tree_reduce_scatter(kernel_local.reshape(n_rows, -1), "rows")
    kernel_total = tree_all_gather(lax.psum(kernel_part, "fsdp"), "rows").reshape(kernel_local.shape)
    activation = output.reshape(1, height, cols, -1)
    return (activation, dframe.reshape((1,) + dframe.shape), up_grad, kernel_total)


def solution(mesh):
    placed = (
        P("fsdp", "rows", None, None),
        P(),
        P(),
        P(),
        P(),
        P("fsdp", "rows"),
        P("rows"),
        P("rows"),
        P("rows"),
        P("fsdp", None, None, "rows"),
    )
    return jax.shard_map(
        functools.partial(body, fsdp_ring(mesh)),
        mesh=mesh,
        in_specs=placed,
        out_specs=(
            P("fsdp", None, None, "rows"),
            P("fsdp", "rows", None, None),
            P("fsdp", "rows"),
            P(),
        ),
        check_vma=False,
    )
```

```python
import functools

import jax
import jax.numpy as jnp
from jax import lax
from jax.sharding import PartitionSpec as P

FF = 6144


def extended(block, sides, width):
    for axis, dim in sides:
        count = lax.axis_size(axis)
        forward = [(i, i + 1) for i in range(count - 1)]
        backward = [(target, source) for source, target in forward]
        low = lax.ppermute(
            lax.slice_in_dim(block, block.shape[dim] - width, None, axis=dim), axis, forward
        )
        high = lax.ppermute(lax.slice_in_dim(block, 0, width, axis=dim), axis, backward)
        block = jnp.concatenate([low, block, high], axis=dim)
    return block


def _bit_steps(axes):
    steps = []
    for axis in axes:
        size = lax.axis_size(axis)
        assert size & (size - 1) == 0
        mask = 1
        while mask < size:
            steps.append((axis, mask, size))
            mask *= 2
    return steps


def tree_allreduce(value, axes):
    shape = value.shape
    flat = value.reshape(-1)
    steps = _bit_steps(axes)
    assert flat.shape[0] % (1 << len(steps)) == 0
    bits = []
    for axis, mask, size in steps:
        bit = (lax.axis_index(axis) // mask) % 2
        bits.append(bit)
        halves = flat.reshape(2, -1)
        keep = lax.dynamic_index_in_dim(halves, bit, keepdims=False)
        give = lax.dynamic_index_in_dim(halves, 1 - bit, keepdims=False)
        perm = [(j, j ^ mask) for j in range(size)]
        flat = keep + lax.ppermute(give, axis, perm)
    for (axis, mask, size), bit in reversed(list(zip(steps, bits))):
        perm = [(j, j ^ mask) for j in range(size)]
        other = lax.ppermute(flat, axis, perm)
        flat = jnp.where(bit == 0, jnp.concatenate([flat, other]), jnp.concatenate([other, flat]))
    return flat.reshape(shape)


def tree_reduce_scatter(chunks, axis):
    size = lax.axis_size(axis)
    assert chunks.shape[0] == size and size & (size - 1) == 0
    me = lax.axis_index(axis)
    data = chunks
    mask = 1
    while mask < size:
        bit = (me // mask) % 2
        pairs = data.reshape((data.shape[0] // 2, 2) + data.shape[1:])
        keep = lax.dynamic_index_in_dim(pairs, bit, axis=1, keepdims=False)
        give = lax.dynamic_index_in_dim(pairs, 1 - bit, axis=1, keepdims=False)
        perm = [(j, j ^ mask) for j in range(size)]
        data = keep.astype(jnp.float32) + lax.ppermute(give, axis, perm).astype(jnp.float32)
        mask *= 2
    return data[0]


def fsdp_ring(mesh):
    count = mesh.shape["fsdp"]
    try:
        members = [mesh.devices[j, 0] for j in range(count)]
        spots = [(d.coords[2], d.coords[1]) for d in members]
        zs = sorted({z for z, _ in spots})
        ys = sorted({y for _, y in spots})
        rows_a, cols_b = len(zs), len(ys)
        where = {(zs.index(z), ys.index(y)): j for j, (z, y) in enumerate(spots)}
        assert len(where) == count == rows_a * cols_b and rows_a % 2 == 0 and cols_b >= 2
        cells = [(a, 0) for a in range(rows_a)]
        for k, a in enumerate(range(rows_a - 1, -1, -1)):
            span = range(1, cols_b) if k % 2 == 0 else range(cols_b - 1, 0, -1)
            cells += [(a, b) for b in span]
        ring = [where[c] for c in cells]
        assert sorted(ring) == list(range(count))
    except Exception:
        ring = list(range(count))
    return ring


def ring_all_gather(block, axis, ring, held=None):
    count = len(ring)
    place = [0] * count
    for k, j in enumerate(ring):
        place[j] = k
    ring_arr = jnp.array(ring, jnp.int32)
    me = lax.axis_index(axis)
    spot = jnp.array(place, jnp.int32)[me]
    forward = [(ring[k], ring[(k + 1) % count]) for k in range(count)]
    backward = [(ring[k], ring[(k - 1) % count]) for k in range(count)]
    ahead = count // 2
    behind = count - 1 - ahead
    gathered = jnp.zeros((count,) + block.shape, block.dtype)
    gathered = lax.dynamic_update_index_in_dim(gathered, block, me, 0)
    cw = block
    ccw = block
    for s in range(1, ahead + 1):
        cw = lax.ppermute(cw, axis, forward)
        if s <= behind:
            ccw = lax.ppermute(ccw, axis, backward)
        if s == 1 and held is not None:
            cw, ccw, held = lax.optimization_barrier((cw, ccw, held))
        gathered = lax.dynamic_update_index_in_dim(gathered, cw, ring_arr[(spot - s) % count], 0)
        if s <= behind:
            gathered = lax.dynamic_update_index_in_dim(
                gathered, ccw, ring_arr[(spot + s) % count], 0
            )
    return gathered.reshape((count * block.shape[0],) + block.shape[1:]), held


def ring_reduce_scatter(terms, axis, ring):
    count = len(ring)
    place = [0] * count
    for k, j in enumerate(ring):
        place[j] = k
    ring_arr = jnp.array(ring, jnp.int32)
    me = lax.axis_index(axis)
    spot = jnp.array(place, jnp.int32)[me]
    forward = [(ring[k], ring[(k + 1) % count]) for k in range(count)]
    backward = [(ring[k], ring[(k - 1) % count]) for k in range(count)]
    ahead = count // 2
    behind = count - 1 - ahead

    def term(offset):
        return lax.dynamic_index_in_dim(terms, ring_arr[(spot + offset) % count], 0, keepdims=False)

    total = term(0).astype(jnp.float32)
    cw = term(ahead)
    ccw = term(-behind) if behind else None
    for s in range(1, ahead + 1):
        cw = lax.ppermute(cw, axis, forward)
        if s <= behind:
            ccw = lax.ppermute(ccw, axis, backward)
        if s < ahead:
            cw = (cw.astype(jnp.float32) + term(ahead - s).astype(jnp.float32)).astype(terms.dtype)
        else:
            total = total + cw.astype(jnp.float32)
        if s < behind:
            ccw = (ccw.astype(jnp.float32) + term(s - behind).astype(jnp.float32)).astype(terms.dtype)
        elif s == behind:
            total = total + ccw.astype(jnp.float32)
    return total


def tree_all_gather(block, axis):
    size = lax.axis_size(axis)
    assert size & (size - 1) == 0
    me = lax.axis_index(axis)
    data = block[None]
    mask = 1
    while mask < size:
        bit = (me // mask) % 2
        perm = [(j, j ^ mask) for j in range(size)]
        other = lax.ppermute(data, axis, perm)
        data = jnp.where(bit == 0, jnp.concatenate([data, other]), jnp.concatenate([other, data]))
        mask *= 2
    return data.reshape((size * block.shape[0],) + block.shape[1:])


def conv_rows(framed, kern, kbias):
    rows = framed.shape[0] - 6
    cols = framed.shape[1]
    wide = jnp.pad(framed, ((0, 0), (3, 3), (0, 0)))
    total = jnp.zeros((rows, cols, framed.shape[2]), jnp.float32) + kbias
    for i in range(kern.shape[0]):
        for j in range(kern.shape[1]):
            total = total + wide[i : i + rows, j : j + cols].astype(jnp.float32) * kern[i, j]
    return total


def back_conv(grad_pad, kern):
    rows = grad_pad.shape[0] - 6
    cols = grad_pad.shape[1]
    wide = jnp.pad(grad_pad, ((0, 0), (3, 3), (0, 0)))
    total = jnp.zeros((rows, cols, grad_pad.shape[2]), jnp.float32)
    for i in range(kern.shape[0]):
        for j in range(kern.shape[1]):
            total = (
                total
                + wide[6 - i : 6 - i + rows, 6 - j : 6 - j + cols].astype(jnp.float32) * kern[i, j]
            )
    return total


def kern_grad(framed, grad_rows):
    rows = grad_rows.shape[0]
    cols = grad_rows.shape[1]
    wide = jnp.pad(framed, ((0, 0), (3, 3), (0, 0)))
    grad_f = grad_rows.astype(jnp.float32)
    parts = []
    for i in range(7):
        for j in range(7):
            parts.append(
                jnp.sum(wide[i : i + rows, j : j + cols].astype(jnp.float32) * grad_f, axis=(0, 1))
            )
    return jnp.stack(parts).reshape(7, 7, grad_rows.shape[2])


def apply_layer_norm(activation_rows, scale_factor, offset_bias):
    centered_input = activation_rows - jnp.mean(activation_rows, axis=-1, keepdims=True)
    inverse_deviation = lax.rsqrt(
        jnp.mean(centered_input * centered_input, axis=-1, keepdims=True) + 1e-06
    )
    standardized_input = centered_input * inverse_deviation
    return (
        (standardized_input * scale_factor + offset_bias).astype(jnp.bfloat16),
        standardized_input,
        inverse_deviation,
    )


def gelu_grad(value):
    return (
        0.5 * (1.0 + jax.scipy.special.erf(value * 0.7071067811865476))
        + value * jnp.exp(-0.5 * value * value) * 0.3989422804014327
    )


def layer_norm_backward(normed_input_gradient, scale_factor, standardized_input, inverse_deviation):
    scaled_output = normed_input_gradient * scale_factor
    return (
        inverse_deviation
        * (
            scaled_output
            - jnp.mean(scaled_output, axis=-1, keepdims=True)
            - standardized_input
            * jnp.mean(scaled_output * standardized_input, axis=-1, keepdims=True)
        )
    ).astype(jnp.bfloat16)


def body(
    ring,
    frames,
    kernel,
    kernel_bias,
    layer_norm_weight,
    layer_norm_bias,
    up_weight,
    up_bias,
    grn_gamma,
    grn_beta,
    grad_out,
):
    slab = frames[0]
    chans = slab.shape[2]
    staged = jnp.where(up_weight == up_weight, up_weight, jnp.zeros_like(up_weight))
    columns, slab = ring_all_gather(staged, "fsdp", ring, slab)
    padded = extended(slab, (("rows", 0),), 3)
    activation_rows = conv_rows(padded, kernel, kernel_bias)
    normed_output, standardized_input, inverse_deviation = apply_layer_norm(
        activation_rows, layer_norm_weight, layer_norm_bias
    )
    whole = tree_all_gather(normed_output, "rows")
    height = whole.shape[0]
    cols = whole.shape[1]
    flat = whole.reshape(-1, chans)
    pre = jnp.dot(flat, columns, preferred_element_type=jnp.float32) + up_bias
    post = jax.nn.gelu(pre, approximate=False)
    norms = jnp.sqrt(jnp.sum(post * post, axis=0) + 1e-06)
    cot_f = grad_out[0].reshape(flat.shape[0], -1).astype(jnp.float32)
    dnorm = grn_gamma * jnp.sum(cot_f * post, axis=0)
    norm_total = lax.psum(jnp.sum(norms), "rows")
    denom = norm_total / FF + 1e-06
    ratio = norms / denom
    output = (grn_gamma * (post * ratio) + grn_beta + post).astype(jnp.bfloat16)
    cross = lax.psum(jnp.sum(dnorm * norms), "rows")
    dnorms = dnorm / denom - cross / (denom * denom) / FF
    dpost = cot_f * (1.0 + grn_gamma * ratio) + post * (dnorms / norms)
    dpre = (dpost * gelu_grad(pre)).astype(jnp.bfloat16)
    w_term = lax.dot_general(
        flat, dpre, (((0,), (0,)), ((), ())), preferred_element_type=jnp.float32
    )
    up_grad = lax.psum_scatter(
        w_term.astype(jnp.bfloat16), "fsdp", scatter_dimension=0, tiled=True
    ).astype(jnp.float32)
    dpre_rows = dpre.reshape(height, cols, -1)
    group_terms = jnp.einsum(
        "hwf,cf->hwc", dpre_rows, columns, preferred_element_type=jnp.float32
    ).astype(jnp.bfloat16)
    n_rows = lax.axis_size("rows")
    normed_input_gradient = tree_reduce_scatter(
        group_terms.reshape((n_rows, height // n_rows) + group_terms.shape[1:]), "rows"
    )
    activation_gradient = layer_norm_backward(
        normed_input_gradient, layer_norm_weight, standardized_input, inverse_deviation
    )
    grad_pad = extended(activation_gradient, (("rows", 0),), 3)
    dframe = back_conv(grad_pad, kernel).astype(jnp.bfloat16)
    kernel_local = kern_grad(padded, activation_gradient)
    kernel_total = tree_allreduce(kernel_local, ("rows", "fsdp"))
    activation = output.reshape(1, height, cols, -1)
    return (activation, dframe.reshape((1,) + dframe.shape), up_grad, kernel_total)


def solution(mesh):
    placed = (
        P("fsdp", "rows", None, None),
        P(),
        P(),
        P(),
        P(),
        P("fsdp", "rows"),
        P("rows"),
        P("rows"),
        P("rows"),
        P("fsdp", None, None, "rows"),
    )
    return jax.shard_map(
        functools.partial(body, fsdp_ring(mesh)),
        mesh=mesh,
        in_specs=placed,
        out_specs=(
            P("fsdp", None, None, "rows"),
            P("fsdp", "rows", None, None),
            P("fsdp", "rows"),
            P(),
        ),
        check_vma=False,
    )
```

```python
import functools

import jax
import jax.numpy as jnp
from jax import lax
from jax.sharding import PartitionSpec as P

FF = 6144


def extended(block, sides, width):
    for axis, dim in sides:
        count = lax.axis_size(axis)
        forward = [(i, i + 1) for i in range(count - 1)]
        backward = [(target, source) for source, target in forward]
        low = lax.ppermute(
            lax.slice_in_dim(block, block.shape[dim] - width, None, axis=dim), axis, forward
        )
        high = lax.ppermute(lax.slice_in_dim(block, 0, width, axis=dim), axis, backward)
        block = jnp.concatenate([low, block, high], axis=dim)
    return block


def _bit_steps(axes):
    steps = []
    for axis in axes:
        size = lax.axis_size(axis)
        assert size & (size - 1) == 0
        mask = 1
        while mask < size:
            steps.append((axis, mask, size))
            mask *= 2
    return steps


def tree_allreduce(value, axes):
    shape = value.shape
    flat = value.reshape(-1)
    steps = _bit_steps(axes)
    assert flat.shape[0] % (1 << len(steps)) == 0
    bits = []
    for axis, mask, size in steps:
        bit = (lax.axis_index(axis) // mask) % 2
        bits.append(bit)
        halves = flat.reshape(2, -1)
        keep = lax.dynamic_index_in_dim(halves, bit, keepdims=False)
        give = lax.dynamic_index_in_dim(halves, 1 - bit, keepdims=False)
        perm = [(j, j ^ mask) for j in range(size)]
        flat = keep + lax.ppermute(give, axis, perm)
    for (axis, mask, size), bit in reversed(list(zip(steps, bits))):
        perm = [(j, j ^ mask) for j in range(size)]
        other = lax.ppermute(flat, axis, perm)
        flat = jnp.where(bit == 0, jnp.concatenate([flat, other]), jnp.concatenate([other, flat]))
    return flat.reshape(shape)


def tree_reduce_scatter(chunks, axis):
    size = lax.axis_size(axis)
    assert chunks.shape[0] == size and size & (size - 1) == 0
    me = lax.axis_index(axis)
    data = chunks
    mask = 1
    while mask < size:
        bit = (me // mask) % 2
        pairs = data.reshape((data.shape[0] // 2, 2) + data.shape[1:])
        keep = lax.dynamic_index_in_dim(pairs, bit, axis=1, keepdims=False)
        give = lax.dynamic_index_in_dim(pairs, 1 - bit, axis=1, keepdims=False)
        perm = [(j, j ^ mask) for j in range(size)]
        data = keep.astype(jnp.float32) + lax.ppermute(give, axis, perm).astype(jnp.float32)
        mask *= 2
    return data[0]


def fsdp_ring(mesh):
    count = mesh.shape["fsdp"]
    try:
        members = [mesh.devices[j, 0] for j in range(count)]
        spots = [(d.coords[2], d.coords[1]) for d in members]
        zs = sorted({z for z, _ in spots})
        ys = sorted({y for _, y in spots})
        rows_a, cols_b = len(zs), len(ys)
        where = {(zs.index(z), ys.index(y)): j for j, (z, y) in enumerate(spots)}
        assert len(where) == count == rows_a * cols_b and rows_a % 2 == 0 and cols_b >= 2
        cells = [(a, 0) for a in range(rows_a)]
        for k, a in enumerate(range(rows_a - 1, -1, -1)):
            span = range(1, cols_b) if k % 2 == 0 else range(cols_b - 1, 0, -1)
            cells += [(a, b) for b in span]
        ring = [where[c] for c in cells]
        assert sorted(ring) == list(range(count))
    except Exception:
        ring = list(range(count))
    return ring


def ring_all_gather(block, axis, ring, held=None):
    count = len(ring)
    place = [0] * count
    for k, j in enumerate(ring):
        place[j] = k
    ring_arr = jnp.array(ring, jnp.int32)
    me = lax.axis_index(axis)
    spot = jnp.array(place, jnp.int32)[me]
    forward = [(ring[k], ring[(k + 1) % count]) for k in range(count)]
    backward = [(ring[k], ring[(k - 1) % count]) for k in range(count)]
    ahead = count // 2
    behind = count - 1 - ahead
    gathered = jnp.zeros((count,) + block.shape, block.dtype)
    gathered = lax.dynamic_update_index_in_dim(gathered, block, me, 0)
    cw = block
    ccw = block
    for s in range(1, ahead + 1):
        cw = lax.ppermute(cw, axis, forward)
        if s <= behind:
            ccw = lax.ppermute(ccw, axis, backward)
        if s == 1 and held is not None:
            cw, ccw, held = lax.optimization_barrier((cw, ccw, held))
        gathered = lax.dynamic_update_index_in_dim(gathered, cw, ring_arr[(spot - s) % count], 0)
        if s <= behind:
            gathered = lax.dynamic_update_index_in_dim(
                gathered, ccw, ring_arr[(spot + s) % count], 0
            )
    return gathered.reshape((count * block.shape[0],) + block.shape[1:]), held


def ring_reduce_scatter(terms, axis, ring):
    count = len(ring)
    place = [0] * count
    for k, j in enumerate(ring):
        place[j] = k
    ring_arr = jnp.array(ring, jnp.int32)
    me = lax.axis_index(axis)
    spot = jnp.array(place, jnp.int32)[me]
    forward = [(ring[k], ring[(k + 1) % count]) for k in range(count)]
    backward = [(ring[k], ring[(k - 1) % count]) for k in range(count)]
    ahead = count // 2
    behind = count - 1 - ahead

    def term(offset):
        return lax.dynamic_index_in_dim(terms, ring_arr[(spot + offset) % count], 0, keepdims=False)

    total = term(0).astype(jnp.float32)
    cw = term(ahead)
    ccw = term(-behind) if behind else None
    for s in range(1, ahead + 1):
        cw = lax.ppermute(cw, axis, forward)
        if s <= behind:
            ccw = lax.ppermute(ccw, axis, backward)
        if s < ahead:
            cw = (cw.astype(jnp.float32) + term(ahead - s).astype(jnp.float32)).astype(terms.dtype)
        else:
            total = total + cw.astype(jnp.float32)
        if s < behind:
            ccw = (ccw.astype(jnp.float32) + term(s - behind).astype(jnp.float32)).astype(terms.dtype)
        elif s == behind:
            total = total + ccw.astype(jnp.float32)
    return total


def tree_all_gather(block, axis):
    size = lax.axis_size(axis)
    assert size & (size - 1) == 0
    me = lax.axis_index(axis)
    data = block[None]
    mask = 1
    while mask < size:
        bit = (me // mask) % 2
        perm = [(j, j ^ mask) for j in range(size)]
        other = lax.ppermute(data, axis, perm)
        data = jnp.where(bit == 0, jnp.concatenate([data, other]), jnp.concatenate([other, data]))
        mask *= 2
    return data.reshape((size * block.shape[0],) + block.shape[1:])


def conv_rows(framed, kern, kbias):
    rows = framed.shape[0] - 6
    cols = framed.shape[1]
    wide = jnp.pad(framed, ((0, 0), (3, 3), (0, 0)))
    total = jnp.zeros((rows, cols, framed.shape[2]), jnp.float32) + kbias
    for i in range(kern.shape[0]):
        for j in range(kern.shape[1]):
            total = total + wide[i : i + rows, j : j + cols].astype(jnp.float32) * kern[i, j]
    return total


def back_conv(grad_pad, kern):
    rows = grad_pad.shape[0] - 6
    cols = grad_pad.shape[1]
    wide = jnp.pad(grad_pad, ((0, 0), (3, 3), (0, 0)))
    total = jnp.zeros((rows, cols, grad_pad.shape[2]), jnp.float32)
    for i in range(kern.shape[0]):
        for j in range(kern.shape[1]):
            total = (
                total
                + wide[6 - i : 6 - i + rows, 6 - j : 6 - j + cols].astype(jnp.float32) * kern[i, j]
            )
    return total


def kern_grad(framed, grad_rows):
    rows = grad_rows.shape[0]
    cols = grad_rows.shape[1]
    wide = jnp.pad(framed, ((0, 0), (3, 3), (0, 0)))
    grad_f = grad_rows.astype(jnp.float32)
    parts = []
    for i in range(7):
        for j in range(7):
            parts.append(
                jnp.sum(wide[i : i + rows, j : j + cols].astype(jnp.float32) * grad_f, axis=(0, 1))
            )
    return jnp.stack(parts).reshape(7, 7, grad_rows.shape[2])


def apply_layer_norm(activation_rows, scale_factor, offset_bias):
    centered_input = activation_rows - jnp.mean(activation_rows, axis=-1, keepdims=True)
    inverse_deviation = lax.rsqrt(
        jnp.mean(centered_input * centered_input, axis=-1, keepdims=True) + 1e-06
    )
    standardized_input = centered_input * inverse_deviation
    return (
        (standardized_input * scale_factor + offset_bias).astype(jnp.bfloat16),
        standardized_input,
        inverse_deviation,
    )


def gelu_grad(value):
    return (
        0.5 * (1.0 + jax.scipy.special.erf(value * 0.7071067811865476))
        + value * jnp.exp(-0.5 * value * value) * 0.3989422804014327
    )


def layer_norm_backward(normed_input_gradient, scale_factor, standardized_input, inverse_deviation):
    scaled_output = normed_input_gradient * scale_factor
    return (
        inverse_deviation
        * (
            scaled_output
            - jnp.mean(scaled_output, axis=-1, keepdims=True)
            - standardized_input
            * jnp.mean(scaled_output * standardized_input, axis=-1, keepdims=True)
        )
    ).astype(jnp.bfloat16)


def body(
    ring,
    frames,
    kernel,
    kernel_bias,
    layer_norm_weight,
    layer_norm_bias,
    up_weight,
    up_bias,
    grn_gamma,
    grn_beta,
    grad_out,
):
    slab = frames[0]
    chans = slab.shape[2]
    staged = jnp.where(up_weight == up_weight, up_weight, jnp.zeros_like(up_weight))
    columns, slab = ring_all_gather(staged, "fsdp", ring, slab)
    padded = extended(slab, (("rows", 0),), 3)
    activation_rows = conv_rows(padded, kernel, kernel_bias)
    normed_output, standardized_input, inverse_deviation = apply_layer_norm(
        activation_rows, layer_norm_weight, layer_norm_bias
    )
    whole = tree_all_gather(normed_output, "rows")
    height = whole.shape[0]
    cols = whole.shape[1]
    flat = whole.reshape(-1, chans)
    pre = jnp.dot(flat, columns, preferred_element_type=jnp.float32) + up_bias
    post = jax.nn.gelu(pre, approximate=False)
    norms = jnp.sqrt(jnp.sum(post * post, axis=0) + 1e-06)
    cot_f = grad_out[0].reshape(flat.shape[0], -1).astype(jnp.float32)
    dnorm = grn_gamma * jnp.sum(cot_f * post, axis=0)
    slope = gelu_grad(pre)
    slope, norm_local = lax.optimization_barrier((slope, jnp.sum(norms)))
    norm_total = lax.psum(norm_local, "rows")
    denom = norm_total / FF + 1e-06
    ratio = norms / denom
    output = (grn_gamma * (post * ratio) + grn_beta + post).astype(jnp.bfloat16)
    cross = lax.psum(jnp.sum(dnorm * norms), "rows")
    dnorms = dnorm / denom - cross / (denom * denom) / FF
    dpost = cot_f * (1.0 + grn_gamma * ratio) + post * (dnorms / norms)
    dpre = (dpost * slope).astype(jnp.bfloat16)
    w_term = lax.dot_general(
        flat, dpre, (((0,), (0,)), ((), ())), preferred_element_type=jnp.float32
    )
    up_grad = lax.psum_scatter(
        w_term.astype(jnp.bfloat16), "fsdp", scatter_dimension=0, tiled=True
    ).astype(jnp.float32)
    dpre_rows = dpre.reshape(height, cols, -1)
    group_terms = jnp.einsum(
        "hwf,cf->hwc", dpre_rows, columns, preferred_element_type=jnp.float32
    ).astype(jnp.bfloat16)
    n_rows = lax.axis_size("rows")
    normed_input_gradient = tree_reduce_scatter(
        group_terms.reshape((n_rows, height // n_rows) + group_terms.shape[1:]), "rows"
    )
    activation_gradient = layer_norm_backward(
        normed_input_gradient, layer_norm_weight, standardized_input, inverse_deviation
    )
    grad_pad = extended(activation_gradient, (("rows", 0),), 3)
    dframe = back_conv(grad_pad, kernel).astype(jnp.bfloat16)
    kernel_local = kern_grad(padded, activation_gradient)
    kernel_total = tree_allreduce(kernel_local, ("rows", "fsdp"))
    activation = output.reshape(1, height, cols, -1)
    return (activation, dframe.reshape((1,) + dframe.shape), up_grad, kernel_total)


def solution(mesh):
    placed = (
        P("fsdp", "rows", None, None),
        P(),
        P(),
        P(),
        P(),
        P("fsdp", "rows"),
        P("rows"),
        P("rows"),
        P("rows"),
        P("fsdp", None, None, "rows"),
    )
    return jax.shard_map(
        functools.partial(body, fsdp_ring(mesh)),
        mesh=mesh,
        in_specs=placed,
        out_specs=(
            P("fsdp", None, None, "rows"),
            P("fsdp", "rows", None, None),
            P("fsdp", "rows"),
            P(),
        ),
        check_vma=False,
    )
```

```python
import functools

import jax
import jax.numpy as jnp
from jax import lax
from jax.sharding import PartitionSpec as P

FF = 6144


def extended(block, sides, width):
    for axis, dim in sides:
        count = lax.axis_size(axis)
        forward = [(i, i + 1) for i in range(count - 1)]
        backward = [(target, source) for source, target in forward]
        low = lax.ppermute(
            lax.slice_in_dim(block, block.shape[dim] - width, None, axis=dim), axis, forward
        )
        high = lax.ppermute(lax.slice_in_dim(block, 0, width, axis=dim), axis, backward)
        block = jnp.concatenate([low, block, high], axis=dim)
    return block


def _bit_steps(axes):
    steps = []
    for axis in axes:
        size = lax.axis_size(axis)
        assert size & (size - 1) == 0
        mask = 1
        while mask < size:
            steps.append((axis, mask, size))
            mask *= 2
    return steps


def tree_allreduce(value, axes):
    shape = value.shape
    flat = value.reshape(-1)
    steps = _bit_steps(axes)
    assert flat.shape[0] % (1 << len(steps)) == 0
    bits = []
    for axis, mask, size in steps:
        bit = (lax.axis_index(axis) // mask) % 2
        bits.append(bit)
        halves = flat.reshape(2, -1)
        keep = lax.dynamic_index_in_dim(halves, bit, keepdims=False)
        give = lax.dynamic_index_in_dim(halves, 1 - bit, keepdims=False)
        perm = [(j, j ^ mask) for j in range(size)]
        flat = keep + lax.ppermute(give, axis, perm)
    for (axis, mask, size), bit in reversed(list(zip(steps, bits))):
        perm = [(j, j ^ mask) for j in range(size)]
        other = lax.ppermute(flat, axis, perm)
        flat = jnp.where(bit == 0, jnp.concatenate([flat, other]), jnp.concatenate([other, flat]))
    return flat.reshape(shape)


def tree_reduce_scatter(chunks, axis):
    size = lax.axis_size(axis)
    assert chunks.shape[0] == size and size & (size - 1) == 0
    me = lax.axis_index(axis)
    data = chunks
    mask = 1
    while mask < size:
        bit = (me // mask) % 2
        pairs = data.reshape((data.shape[0] // 2, 2) + data.shape[1:])
        keep = lax.dynamic_index_in_dim(pairs, bit, axis=1, keepdims=False)
        give = lax.dynamic_index_in_dim(pairs, 1 - bit, axis=1, keepdims=False)
        perm = [(j, j ^ mask) for j in range(size)]
        data = keep.astype(jnp.float32) + lax.ppermute(give, axis, perm).astype(jnp.float32)
        mask *= 2
    return data[0]


def fsdp_ring(mesh):
    count = mesh.shape["fsdp"]
    try:
        members = [mesh.devices[j, 0] for j in range(count)]
        spots = [(d.coords[2], d.coords[1]) for d in members]
        zs = sorted({z for z, _ in spots})
        ys = sorted({y for _, y in spots})
        rows_a, cols_b = len(zs), len(ys)
        where = {(zs.index(z), ys.index(y)): j for j, (z, y) in enumerate(spots)}
        assert len(where) == count == rows_a * cols_b and rows_a % 2 == 0 and cols_b >= 2
        cells = [(a, 0) for a in range(rows_a)]
        for k, a in enumerate(range(rows_a - 1, -1, -1)):
            span = range(1, cols_b) if k % 2 == 0 else range(cols_b - 1, 0, -1)
            cells += [(a, b) for b in span]
        ring = [where[c] for c in cells]
        assert sorted(ring) == list(range(count))
    except Exception:
        ring = list(range(count))
    return ring


def ring_all_gather(block, axis, ring, held=None):
    count = len(ring)
    place = [0] * count
    for k, j in enumerate(ring):
        place[j] = k
    ring_arr = jnp.array(ring, jnp.int32)
    me = lax.axis_index(axis)
    spot = jnp.array(place, jnp.int32)[me]
    forward = [(ring[k], ring[(k + 1) % count]) for k in range(count)]
    backward = [(ring[k], ring[(k - 1) % count]) for k in range(count)]
    ahead = count // 2
    behind = count - 1 - ahead
    gathered = jnp.zeros((count,) + block.shape, block.dtype)
    gathered = lax.dynamic_update_index_in_dim(gathered, block, me, 0)
    cw = block
    ccw = block
    for s in range(1, ahead + 1):
        cw = lax.ppermute(cw, axis, forward)
        if s <= behind:
            ccw = lax.ppermute(ccw, axis, backward)
        if s == 1 and held is not None:
            cw, ccw, held = lax.optimization_barrier((cw, ccw, held))
        gathered = lax.dynamic_update_index_in_dim(gathered, cw, ring_arr[(spot - s) % count], 0)
        if s <= behind:
            gathered = lax.dynamic_update_index_in_dim(
                gathered, ccw, ring_arr[(spot + s) % count], 0
            )
    return gathered.reshape((count * block.shape[0],) + block.shape[1:]), held


def ring_reduce_scatter(terms, axis, ring):
    count = len(ring)
    place = [0] * count
    for k, j in enumerate(ring):
        place[j] = k
    ring_arr = jnp.array(ring, jnp.int32)
    me = lax.axis_index(axis)
    spot = jnp.array(place, jnp.int32)[me]
    forward = [(ring[k], ring[(k + 1) % count]) for k in range(count)]
    backward = [(ring[k], ring[(k - 1) % count]) for k in range(count)]
    ahead = count // 2
    behind = count - 1 - ahead

    def term(offset):
        return lax.dynamic_index_in_dim(terms, ring_arr[(spot + offset) % count], 0, keepdims=False)

    total = term(0).astype(jnp.float32)
    cw = term(ahead)
    ccw = term(-behind) if behind else None
    for s in range(1, ahead + 1):
        cw = lax.ppermute(cw, axis, forward)
        if s <= behind:
            ccw = lax.ppermute(ccw, axis, backward)
        if s < ahead:
            cw = (cw.astype(jnp.float32) + term(ahead - s).astype(jnp.float32)).astype(terms.dtype)
        else:
            total = total + cw.astype(jnp.float32)
        if s < behind:
            ccw = (ccw.astype(jnp.float32) + term(s - behind).astype(jnp.float32)).astype(terms.dtype)
        elif s == behind:
            total = total + ccw.astype(jnp.float32)
    return total


def tree_all_gather(block, axis):
    size = lax.axis_size(axis)
    assert size & (size - 1) == 0
    me = lax.axis_index(axis)
    data = block[None]
    mask = 1
    while mask < size:
        bit = (me // mask) % 2
        perm = [(j, j ^ mask) for j in range(size)]
        other = lax.ppermute(data, axis, perm)
        data = jnp.where(bit == 0, jnp.concatenate([data, other]), jnp.concatenate([other, data]))
        mask *= 2
    return data.reshape((size * block.shape[0],) + block.shape[1:])


def conv_rows(framed, kern, kbias):
    rows = framed.shape[0] - 6
    cols = framed.shape[1]
    wide = jnp.pad(framed, ((0, 0), (3, 3), (0, 0)))
    total = jnp.zeros((rows, cols, framed.shape[2]), jnp.float32) + kbias
    for i in range(kern.shape[0]):
        for j in range(kern.shape[1]):
            total = total + wide[i : i + rows, j : j + cols].astype(jnp.float32) * kern[i, j]
    return total


def back_conv(grad_pad, kern):
    rows = grad_pad.shape[0] - 6
    cols = grad_pad.shape[1]
    wide = jnp.pad(grad_pad, ((0, 0), (3, 3), (0, 0)))
    total = jnp.zeros((rows, cols, grad_pad.shape[2]), jnp.float32)
    for i in range(kern.shape[0]):
        for j in range(kern.shape[1]):
            total = (
                total
                + wide[6 - i : 6 - i + rows, 6 - j : 6 - j + cols].astype(jnp.float32) * kern[i, j]
            )
    return total


def kern_grad(framed, grad_rows):
    rows = grad_rows.shape[0]
    cols = grad_rows.shape[1]
    wide = jnp.pad(framed, ((0, 0), (3, 3), (0, 0)))
    grad_f = grad_rows.astype(jnp.float32)
    parts = []
    for i in range(7):
        for j in range(7):
            parts.append(
                jnp.sum(wide[i : i + rows, j : j + cols].astype(jnp.float32) * grad_f, axis=(0, 1))
            )
    return jnp.stack(parts).reshape(7, 7, grad_rows.shape[2])


def apply_layer_norm(activation_rows, scale_factor, offset_bias):
    centered_input = activation_rows - jnp.mean(activation_rows, axis=-1, keepdims=True)
    inverse_deviation = lax.rsqrt(
        jnp.mean(centered_input * centered_input, axis=-1, keepdims=True) + 1e-06
    )
    standardized_input = centered_input * inverse_deviation
    return (
        (standardized_input * scale_factor + offset_bias).astype(jnp.bfloat16),
        standardized_input,
        inverse_deviation,
    )


def gelu_grad(value):
    return (
        0.5 * (1.0 + jax.scipy.special.erf(value * 0.7071067811865476))
        + value * jnp.exp(-0.5 * value * value) * 0.3989422804014327
    )


def layer_norm_backward(normed_input_gradient, scale_factor, standardized_input, inverse_deviation):
    scaled_output = normed_input_gradient * scale_factor
    return (
        inverse_deviation
        * (
            scaled_output
            - jnp.mean(scaled_output, axis=-1, keepdims=True)
            - standardized_input
            * jnp.mean(scaled_output * standardized_input, axis=-1, keepdims=True)
        )
    ).astype(jnp.bfloat16)


def body(
    ring,
    frames,
    kernel,
    kernel_bias,
    layer_norm_weight,
    layer_norm_bias,
    up_weight,
    up_bias,
    grn_gamma,
    grn_beta,
    grad_out,
):
    slab = frames[0]
    chans = slab.shape[2]
    staged = jnp.where(up_weight == up_weight, up_weight, jnp.zeros_like(up_weight))
    columns, slab = ring_all_gather(staged, "fsdp", ring, slab)
    padded = extended(slab, (("rows", 0),), 3)
    activation_rows = conv_rows(padded, kernel, kernel_bias)
    normed_output, standardized_input, inverse_deviation = apply_layer_norm(
        activation_rows, layer_norm_weight, layer_norm_bias
    )
    whole = tree_all_gather(normed_output, "rows")
    height = whole.shape[0]
    cols = whole.shape[1]
    flat = whole.reshape(-1, chans)
    pre = jnp.dot(flat, columns, preferred_element_type=jnp.float32) + up_bias
    post = jax.nn.gelu(pre, approximate=False)
    norms = jnp.sqrt(jnp.sum(post * post, axis=0) + 1e-06)
    cot_f = grad_out[0].reshape(flat.shape[0], -1).astype(jnp.float32)
    dnorm = grn_gamma * jnp.sum(cot_f * post, axis=0)
    norm_total = lax.psum(jnp.sum(norms), "rows")
    denom = norm_total / FF + 1e-06
    ratio = norms / denom
    output = (grn_gamma * (post * ratio) + grn_beta + post).astype(jnp.bfloat16)
    cross = lax.psum(jnp.sum(dnorm * norms), "rows")
    dnorms = dnorm / denom - cross / (denom * denom) / FF
    dpost = cot_f * (1.0 + grn_gamma * ratio) + post * (dnorms / norms)
    dpre = (dpost * gelu_grad(pre)).astype(jnp.bfloat16)
    w_term = lax.dot_general(
        flat, dpre, (((0,), (0,)), ((), ())), preferred_element_type=jnp.float32
    )
    n_fsdp = lax.axis_size("fsdp")
    up_grad = ring_reduce_scatter(
        w_term.astype(jnp.bfloat16).reshape((n_fsdp, chans // n_fsdp, -1)), "fsdp", ring
    )
    dpre_rows = dpre.reshape(height, cols, -1)
    group_terms = jnp.einsum(
        "hwf,cf->hwc", dpre_rows, columns, preferred_element_type=jnp.float32
    ).astype(jnp.bfloat16)
    n_rows = lax.axis_size("rows")
    normed_input_gradient = tree_reduce_scatter(
        group_terms.reshape((n_rows, height // n_rows) + group_terms.shape[1:]), "rows"
    )
    activation_gradient = layer_norm_backward(
        normed_input_gradient, layer_norm_weight, standardized_input, inverse_deviation
    )
    grad_pad = extended(activation_gradient, (("rows", 0),), 3)
    dframe = back_conv(grad_pad, kernel).astype(jnp.bfloat16)
    kernel_local = kern_grad(padded, activation_gradient)
    kernel_total = tree_allreduce(kernel_local, ("rows", "fsdp"))
    activation = output.reshape(1, height, cols, -1)
    return (activation, dframe.reshape((1,) + dframe.shape), up_grad, kernel_total)


def solution(mesh):
    placed = (
        P("fsdp", "rows", None, None),
        P(),
        P(),
        P(),
        P(),
        P("fsdp", "rows"),
        P("rows"),
        P("rows"),
        P("rows"),
        P("fsdp", None, None, "rows"),
    )
    return jax.shard_map(
        functools.partial(body, fsdp_ring(mesh)),
        mesh=mesh,
        in_specs=placed,
        out_specs=(
            P("fsdp", None, None, "rows"),
            P("fsdp", "rows", None, None),
            P("fsdp", "rows"),
            P(),
        ),
        check_vma=False,
    )
```

```python
import functools

import jax
import jax.numpy as jnp
from jax import lax
from jax.sharding import PartitionSpec as P

FF = 6144


def extended(block, sides, width):
    for axis, dim in sides:
        count = lax.axis_size(axis)
        forward = [(i, i + 1) for i in range(count - 1)]
        backward = [(target, source) for source, target in forward]
        low = lax.ppermute(
            lax.slice_in_dim(block, block.shape[dim] - width, None, axis=dim), axis, forward
        )
        high = lax.ppermute(lax.slice_in_dim(block, 0, width, axis=dim), axis, backward)
        block = jnp.concatenate([low, block, high], axis=dim)
    return block


def _bit_steps(axes):
    steps = []
    for axis in axes:
        size = lax.axis_size(axis)
        assert size & (size - 1) == 0
        mask = 1
        while mask < size:
            steps.append((axis, mask, size))
            mask *= 2
    return steps


def tree_allreduce(value, axes):
    shape = value.shape
    flat = value.reshape(-1)
    steps = _bit_steps(axes)
    assert flat.shape[0] % (1 << len(steps)) == 0
    bits = []
    for axis, mask, size in steps:
        bit = (lax.axis_index(axis) // mask) % 2
        bits.append(bit)
        halves = flat.reshape(2, -1)
        keep = lax.dynamic_index_in_dim(halves, bit, keepdims=False)
        give = lax.dynamic_index_in_dim(halves, 1 - bit, keepdims=False)
        perm = [(j, j ^ mask) for j in range(size)]
        flat = keep + lax.ppermute(give, axis, perm)
    for (axis, mask, size), bit in reversed(list(zip(steps, bits))):
        perm = [(j, j ^ mask) for j in range(size)]
        other = lax.ppermute(flat, axis, perm)
        flat = jnp.where(bit == 0, jnp.concatenate([flat, other]), jnp.concatenate([other, flat]))
    return flat.reshape(shape)


def tree_reduce_scatter(chunks, axis):
    size = lax.axis_size(axis)
    assert chunks.shape[0] == size and size & (size - 1) == 0
    me = lax.axis_index(axis)
    data = chunks
    mask = 1
    while mask < size:
        bit = (me // mask) % 2
        pairs = data.reshape((data.shape[0] // 2, 2) + data.shape[1:])
        keep = lax.dynamic_index_in_dim(pairs, bit, axis=1, keepdims=False)
        give = lax.dynamic_index_in_dim(pairs, 1 - bit, axis=1, keepdims=False)
        perm = [(j, j ^ mask) for j in range(size)]
        data = keep.astype(jnp.float32) + lax.ppermute(give, axis, perm).astype(jnp.float32)
        mask *= 2
    return data[0]


def fsdp_ring(mesh):
    count = mesh.shape["fsdp"]
    try:
        members = [mesh.devices[j, 0] for j in range(count)]
        spots = [(d.coords[2], d.coords[1]) for d in members]
        zs = sorted({z for z, _ in spots})
        ys = sorted({y for _, y in spots})
        rows_a, cols_b = len(zs), len(ys)
        where = {(zs.index(z), ys.index(y)): j for j, (z, y) in enumerate(spots)}
        assert len(where) == count == rows_a * cols_b and rows_a % 2 == 0 and cols_b >= 2
        cells = [(a, 0) for a in range(rows_a)]
        for k, a in enumerate(range(rows_a - 1, -1, -1)):
            span = range(1, cols_b) if k % 2 == 0 else range(cols_b - 1, 0, -1)
            cells += [(a, b) for b in span]
        ring = [where[c] for c in cells]
        assert sorted(ring) == list(range(count))
    except Exception:
        ring = list(range(count))
    return ring


def ring_all_gather(block, axis, ring, held=None):
    count = len(ring)
    place = [0] * count
    for k, j in enumerate(ring):
        place[j] = k
    ring_arr = jnp.array(ring, jnp.int32)
    me = lax.axis_index(axis)
    spot = jnp.array(place, jnp.int32)[me]
    forward = [(ring[k], ring[(k + 1) % count]) for k in range(count)]
    backward = [(ring[k], ring[(k - 1) % count]) for k in range(count)]
    ahead = count // 2
    behind = count - 1 - ahead
    gathered = jnp.zeros((count,) + block.shape, block.dtype)
    gathered = lax.dynamic_update_index_in_dim(gathered, block, me, 0)
    cw = block
    ccw = block
    for s in range(1, ahead + 1):
        cw = lax.ppermute(cw, axis, forward)
        if s <= behind:
            ccw = lax.ppermute(ccw, axis, backward)
        if s == 1 and held is not None:
            cw, ccw, held = lax.optimization_barrier((cw, ccw, held))
        gathered = lax.dynamic_update_index_in_dim(gathered, cw, ring_arr[(spot - s) % count], 0)
        if s <= behind:
            gathered = lax.dynamic_update_index_in_dim(
                gathered, ccw, ring_arr[(spot + s) % count], 0
            )
    return gathered.reshape((count * block.shape[0],) + block.shape[1:]), held


def ring_reduce_scatter(terms, axis, ring, held=None):
    count = len(ring)
    place = [0] * count
    for k, j in enumerate(ring):
        place[j] = k
    ring_arr = jnp.array(ring, jnp.int32)
    me = lax.axis_index(axis)
    spot = jnp.array(place, jnp.int32)[me]
    forward = [(ring[k], ring[(k + 1) % count]) for k in range(count)]
    backward = [(ring[k], ring[(k - 1) % count]) for k in range(count)]
    ahead = count // 2
    behind = count - 1 - ahead

    def term(offset):
        return lax.dynamic_index_in_dim(terms, ring_arr[(spot + offset) % count], 0, keepdims=False)

    total = term(0).astype(jnp.float32)
    cw = term(ahead)
    ccw = term(-behind) if behind else None
    for s in range(1, ahead + 1):
        cw = lax.ppermute(cw, axis, forward)
        if s <= behind:
            ccw = lax.ppermute(ccw, axis, backward)
        if s == ahead - 1 and held is not None:
            cw, ccw, held = lax.optimization_barrier((cw, ccw, held))
        if s < ahead:
            cw = (cw.astype(jnp.float32) + term(ahead - s).astype(jnp.float32)).astype(terms.dtype)
        else:
            total = total + cw.astype(jnp.float32)
        if s < behind:
            ccw = (ccw.astype(jnp.float32) + term(s - behind).astype(jnp.float32)).astype(terms.dtype)
        elif s == behind:
            total = total + ccw.astype(jnp.float32)
    return total, held


def tree_all_gather(block, axis):
    size = lax.axis_size(axis)
    assert size & (size - 1) == 0
    me = lax.axis_index(axis)
    data = block[None]
    mask = 1
    while mask < size:
        bit = (me // mask) % 2
        perm = [(j, j ^ mask) for j in range(size)]
        other = lax.ppermute(data, axis, perm)
        data = jnp.where(bit == 0, jnp.concatenate([data, other]), jnp.concatenate([other, data]))
        mask *= 2
    return data.reshape((size * block.shape[0],) + block.shape[1:])


def conv_rows(framed, kern, kbias):
    rows = framed.shape[0] - 6
    cols = framed.shape[1]
    wide = jnp.pad(framed, ((0, 0), (3, 3), (0, 0)))
    total = jnp.zeros((rows, cols, framed.shape[2]), jnp.float32) + kbias
    for i in range(kern.shape[0]):
        for j in range(kern.shape[1]):
            total = total + wide[i : i + rows, j : j + cols].astype(jnp.float32) * kern[i, j]
    return total


def back_conv(grad_pad, kern):
    rows = grad_pad.shape[0] - 6
    cols = grad_pad.shape[1]
    wide = jnp.pad(grad_pad, ((0, 0), (3, 3), (0, 0)))
    total = jnp.zeros((rows, cols, grad_pad.shape[2]), jnp.float32)
    for i in range(kern.shape[0]):
        for j in range(kern.shape[1]):
            total = (
                total
                + wide[6 - i : 6 - i + rows, 6 - j : 6 - j + cols].astype(jnp.float32) * kern[i, j]
            )
    return total


def kern_grad(framed, grad_rows):
    rows = grad_rows.shape[0]
    cols = grad_rows.shape[1]
    wide = jnp.pad(framed, ((0, 0), (3, 3), (0, 0)))
    grad_f = grad_rows.astype(jnp.float32)
    parts = []
    for i in range(7):
        for j in range(7):
            parts.append(
                jnp.sum(wide[i : i + rows, j : j + cols].astype(jnp.float32) * grad_f, axis=(0, 1))
            )
    return jnp.stack(parts).reshape(7, 7, grad_rows.shape[2])


def apply_layer_norm(activation_rows, scale_factor, offset_bias):
    centered_input = activation_rows - jnp.mean(activation_rows, axis=-1, keepdims=True)
    inverse_deviation = lax.rsqrt(
        jnp.mean(centered_input * centered_input, axis=-1, keepdims=True) + 1e-06
    )
    standardized_input = centered_input * inverse_deviation
    return (
        (standardized_input * scale_factor + offset_bias).astype(jnp.bfloat16),
        standardized_input,
        inverse_deviation,
    )


def gelu_grad(value):
    return (
        0.5 * (1.0 + jax.scipy.special.erf(value * 0.7071067811865476))
        + value * jnp.exp(-0.5 * value * value) * 0.3989422804014327
    )


def layer_norm_backward(normed_input_gradient, scale_factor, standardized_input, inverse_deviation):
    scaled_output = normed_input_gradient * scale_factor
    return (
        inverse_deviation
        * (
            scaled_output
            - jnp.mean(scaled_output, axis=-1, keepdims=True)
            - standardized_input
            * jnp.mean(scaled_output * standardized_input, axis=-1, keepdims=True)
        )
    ).astype(jnp.bfloat16)


def body(
    ring,
    frames,
    kernel,
    kernel_bias,
    layer_norm_weight,
    layer_norm_bias,
    up_weight,
    up_bias,
    grn_gamma,
    grn_beta,
    grad_out,
):
    slab = frames[0]
    chans = slab.shape[2]
    staged = jnp.where(up_weight == up_weight, up_weight, jnp.zeros_like(up_weight))
    columns, slab = ring_all_gather(staged, "fsdp", ring, slab)
    padded = extended(slab, (("rows", 0),), 3)
    activation_rows = conv_rows(padded, kernel, kernel_bias)
    normed_output, standardized_input, inverse_deviation = apply_layer_norm(
        activation_rows, layer_norm_weight, layer_norm_bias
    )
    whole = tree_all_gather(normed_output, "rows")
    height = whole.shape[0]
    cols = whole.shape[1]
    flat = whole.reshape(-1, chans)
    pre = jnp.dot(flat, columns, preferred_element_type=jnp.float32) + up_bias
    post = jax.nn.gelu(pre, approximate=False)
    norms = jnp.sqrt(jnp.sum(post * post, axis=0) + 1e-06)
    cot_f = grad_out[0].reshape(flat.shape[0], -1).astype(jnp.float32)
    dnorm = grn_gamma * jnp.sum(cot_f * post, axis=0)
    norm_total = lax.psum(jnp.sum(norms), "rows")
    denom = norm_total / FF + 1e-06
    ratio = norms / denom
    output = (grn_gamma * (post * ratio) + grn_beta + post).astype(jnp.bfloat16)
    cross = lax.psum(jnp.sum(dnorm * norms), "rows")
    dnorms = dnorm / denom - cross / (denom * denom) / FF
    dpost = cot_f * (1.0 + grn_gamma * ratio) + post * (dnorms / norms)
    dpre = (dpost * gelu_grad(pre)).astype(jnp.bfloat16)
    w_term = lax.dot_general(
        flat, dpre, (((0,), (0,)), ((), ())), preferred_element_type=jnp.float32
    )
    n_fsdp = lax.axis_size("fsdp")
    w_parts = w_term.astype(jnp.bfloat16).reshape((n_fsdp, chans // n_fsdp, -1))
    dpre_rows = dpre.reshape(height, cols, -1)
    group_terms = jnp.einsum(
        "hwf,cf->hwc", dpre_rows, columns, preferred_element_type=jnp.float32
    ).astype(jnp.bfloat16)
    n_rows = lax.axis_size("rows")
    normed_input_gradient = tree_reduce_scatter(
        group_terms.reshape((n_rows, height // n_rows) + group_terms.shape[1:]), "rows"
    )
    activation_gradient = layer_norm_backward(
        normed_input_gradient, layer_norm_weight, standardized_input, inverse_deviation
    )
    grad_pad = extended(activation_gradient, (("rows", 0),), 3)
    dframe = back_conv(grad_pad, kernel).astype(jnp.bfloat16)
    kernel_local = kern_grad(padded, activation_gradient)
    up_grad, kernel_local = ring_reduce_scatter(w_parts, "fsdp", ring, kernel_local)
    kernel_total = tree_allreduce(kernel_local, ("rows", "fsdp"))
    activation = output.reshape(1, height, cols, -1)
    return (activation, dframe.reshape((1,) + dframe.shape), up_grad, kernel_total)


def solution(mesh):
    placed = (
        P("fsdp", "rows", None, None),
        P(),
        P(),
        P(),
        P(),
        P("fsdp", "rows"),
        P("rows"),
        P("rows"),
        P("rows"),
        P("fsdp", None, None, "rows"),
    )
    return jax.shard_map(
        functools.partial(body, fsdp_ring(mesh)),
        mesh=mesh,
        in_specs=placed,
        out_specs=(
            P("fsdp", None, None, "rows"),
            P("fsdp", "rows", None, None),
            P("fsdp", "rows"),
            P(),
        ),
        check_vma=False,
    )
```

```python
import functools

import jax
import jax.numpy as jnp
from jax import lax
from jax.sharding import PartitionSpec as P

FF = 6144


def extended(block, sides, width):
    for axis, dim in sides:
        count = lax.axis_size(axis)
        forward = [(i, i + 1) for i in range(count - 1)]
        backward = [(target, source) for source, target in forward]
        low = lax.ppermute(
            lax.slice_in_dim(block, block.shape[dim] - width, None, axis=dim), axis, forward
        )
        high = lax.ppermute(lax.slice_in_dim(block, 0, width, axis=dim), axis, backward)
        block = jnp.concatenate([low, block, high], axis=dim)
    return block


def _bit_steps(axes):
    steps = []
    for axis in axes:
        size = lax.axis_size(axis)
        assert size & (size - 1) == 0
        mask = 1
        while mask < size:
            steps.append((axis, mask, size))
            mask *= 2
    return steps


def tree_allreduce(value, axes):
    shape = value.shape
    flat = value.reshape(-1)
    steps = _bit_steps(axes)
    assert flat.shape[0] % (1 << len(steps)) == 0
    bits = []
    for axis, mask, size in steps:
        bit = (lax.axis_index(axis) // mask) % 2
        bits.append(bit)
        halves = flat.reshape(2, -1)
        keep = lax.dynamic_index_in_dim(halves, bit, keepdims=False)
        give = lax.dynamic_index_in_dim(halves, 1 - bit, keepdims=False)
        perm = [(j, j ^ mask) for j in range(size)]
        flat = keep + lax.ppermute(give, axis, perm)
    for (axis, mask, size), bit in reversed(list(zip(steps, bits))):
        perm = [(j, j ^ mask) for j in range(size)]
        other = lax.ppermute(flat, axis, perm)
        flat = jnp.where(bit == 0, jnp.concatenate([flat, other]), jnp.concatenate([other, flat]))
    return flat.reshape(shape)


def tree_reduce_scatter(chunks, axis):
    size = lax.axis_size(axis)
    assert chunks.shape[0] == size and size & (size - 1) == 0
    me = lax.axis_index(axis)
    data = chunks
    mask = 1
    while mask < size:
        bit = (me // mask) % 2
        pairs = data.reshape((data.shape[0] // 2, 2) + data.shape[1:])
        keep = lax.dynamic_index_in_dim(pairs, bit, axis=1, keepdims=False)
        give = lax.dynamic_index_in_dim(pairs, 1 - bit, axis=1, keepdims=False)
        perm = [(j, j ^ mask) for j in range(size)]
        data = keep.astype(jnp.float32) + lax.ppermute(give, axis, perm).astype(jnp.float32)
        mask *= 2
    return data[0]


def fsdp_ring(mesh):
    count = mesh.shape["fsdp"]
    try:
        members = [mesh.devices[j, 0] for j in range(count)]
        spots = [(d.coords[2], d.coords[1]) for d in members]
        zs = sorted({z for z, _ in spots})
        ys = sorted({y for _, y in spots})
        rows_a, cols_b = len(zs), len(ys)
        where = {(zs.index(z), ys.index(y)): j for j, (z, y) in enumerate(spots)}
        assert len(where) == count == rows_a * cols_b and rows_a % 2 == 0 and cols_b >= 2
        cells = [(a, 0) for a in range(rows_a)]
        for k, a in enumerate(range(rows_a - 1, -1, -1)):
            span = range(1, cols_b) if k % 2 == 0 else range(cols_b - 1, 0, -1)
            cells += [(a, b) for b in span]
        ring = [where[c] for c in cells]
        assert sorted(ring) == list(range(count))
    except Exception:
        ring = list(range(count))
    return ring


def ring_all_gather(block, axis, ring, held=None):
    count = len(ring)
    place = [0] * count
    for k, j in enumerate(ring):
        place[j] = k
    ring_arr = jnp.array(ring, jnp.int32)
    me = lax.axis_index(axis)
    spot = jnp.array(place, jnp.int32)[me]
    forward = [(ring[k], ring[(k + 1) % count]) for k in range(count)]
    backward = [(ring[k], ring[(k - 1) % count]) for k in range(count)]
    ahead = count // 2
    behind = count - 1 - ahead
    gathered = jnp.zeros((count,) + block.shape, block.dtype)
    gathered = lax.dynamic_update_index_in_dim(gathered, block, me, 0)
    cw = block
    ccw = block
    split = count % 2 == 0 and count > 2
    for s in range(1, ahead + 1):
        if split and s == ahead:
            half = block.shape[-1] // 2
            cw = jnp.concatenate(
                [
                    lax.ppermute(cw[..., :half], axis, forward),
                    lax.ppermute(ccw[..., half:], axis, backward),
                ],
                axis=-1,
            )
            gathered = lax.dynamic_update_index_in_dim(
                gathered, cw, ring_arr[(spot - s) % count], 0
            )
            break
        cw = lax.ppermute(cw, axis, forward)
        if s <= behind:
            ccw = lax.ppermute(ccw, axis, backward)
        if s == 1 and held is not None:
            cw, ccw, held = lax.optimization_barrier((cw, ccw, held))
        gathered = lax.dynamic_update_index_in_dim(gathered, cw, ring_arr[(spot - s) % count], 0)
        if s <= behind:
            gathered = lax.dynamic_update_index_in_dim(
                gathered, ccw, ring_arr[(spot + s) % count], 0
            )
    return gathered.reshape((count * block.shape[0],) + block.shape[1:]), held


def ring_reduce_scatter(terms, axis, ring):
    count = len(ring)
    place = [0] * count
    for k, j in enumerate(ring):
        place[j] = k
    ring_arr = jnp.array(ring, jnp.int32)
    me = lax.axis_index(axis)
    spot = jnp.array(place, jnp.int32)[me]
    forward = [(ring[k], ring[(k + 1) % count]) for k in range(count)]
    backward = [(ring[k], ring[(k - 1) % count]) for k in range(count)]
    ahead = count // 2
    behind = count - 1 - ahead

    def term(offset):
        return lax.dynamic_index_in_dim(terms, ring_arr[(spot + offset) % count], 0, keepdims=False)

    total = term(0).astype(jnp.float32)
    cw = term(ahead)
    ccw = term(-behind) if behind else None
    for s in range(1, ahead + 1):
        cw = lax.ppermute(cw, axis, forward)
        if s <= behind:
            ccw = lax.ppermute(ccw, axis, backward)
        if s < ahead:
            cw = (cw.astype(jnp.float32) + term(ahead - s).astype(jnp.float32)).astype(terms.dtype)
        else:
            total = total + cw.astype(jnp.float32)
        if s < behind:
            ccw = (ccw.astype(jnp.float32) + term(s - behind).astype(jnp.float32)).astype(terms.dtype)
        elif s == behind:
            total = total + ccw.astype(jnp.float32)
    return total


def tree_all_gather(block, axis):
    size = lax.axis_size(axis)
    assert size & (size - 1) == 0
    me = lax.axis_index(axis)
    data = block[None]
    mask = 1
    while mask < size:
        bit = (me // mask) % 2
        perm = [(j, j ^ mask) for j in range(size)]
        other = lax.ppermute(data, axis, perm)
        data = jnp.where(bit == 0, jnp.concatenate([data, other]), jnp.concatenate([other, data]))
        mask *= 2
    return data.reshape((size * block.shape[0],) + block.shape[1:])


def conv_rows(framed, kern, kbias):
    rows = framed.shape[0] - 6
    cols = framed.shape[1]
    wide = jnp.pad(framed, ((0, 0), (3, 3), (0, 0)))
    total = jnp.zeros((rows, cols, framed.shape[2]), jnp.float32) + kbias
    for i in range(kern.shape[0]):
        for j in range(kern.shape[1]):
            total = total + wide[i : i + rows, j : j + cols].astype(jnp.float32) * kern[i, j]
    return total


def back_conv(grad_pad, kern):
    rows = grad_pad.shape[0] - 6
    cols = grad_pad.shape[1]
    wide = jnp.pad(grad_pad, ((0, 0), (3, 3), (0, 0)))
    total = jnp.zeros((rows, cols, grad_pad.shape[2]), jnp.float32)
    for i in range(kern.shape[0]):
        for j in range(kern.shape[1]):
            total = (
                total
                + wide[6 - i : 6 - i + rows, 6 - j : 6 - j + cols].astype(jnp.float32) * kern[i, j]
            )
    return total


def kern_grad(framed, grad_rows):
    rows = grad_rows.shape[0]
    cols = grad_rows.shape[1]
    wide = jnp.pad(framed, ((0, 0), (3, 3), (0, 0)))
    grad_f = grad_rows.astype(jnp.float32)
    parts = []
    for i in range(7):
        for j in range(7):
            parts.append(
                jnp.sum(wide[i : i + rows, j : j + cols].astype(jnp.float32) * grad_f, axis=(0, 1))
            )
    return jnp.stack(parts).reshape(7, 7, grad_rows.shape[2])


def apply_layer_norm(activation_rows, scale_factor, offset_bias):
    centered_input = activation_rows - jnp.mean(activation_rows, axis=-1, keepdims=True)
    inverse_deviation = lax.rsqrt(
        jnp.mean(centered_input * centered_input, axis=-1, keepdims=True) + 1e-06
    )
    standardized_input = centered_input * inverse_deviation
    return (
        (standardized_input * scale_factor + offset_bias).astype(jnp.bfloat16),
        standardized_input,
        inverse_deviation,
    )


def gelu_grad(value):
    return (
        0.5 * (1.0 + jax.scipy.special.erf(value * 0.7071067811865476))
        + value * jnp.exp(-0.5 * value * value) * 0.3989422804014327
    )


def layer_norm_backward(normed_input_gradient, scale_factor, standardized_input, inverse_deviation):
    scaled_output = normed_input_gradient * scale_factor
    return (
        inverse_deviation
        * (
            scaled_output
            - jnp.mean(scaled_output, axis=-1, keepdims=True)
            - standardized_input
            * jnp.mean(scaled_output * standardized_input, axis=-1, keepdims=True)
        )
    ).astype(jnp.bfloat16)


def body(
    ring,
    frames,
    kernel,
    kernel_bias,
    layer_norm_weight,
    layer_norm_bias,
    up_weight,
    up_bias,
    grn_gamma,
    grn_beta,
    grad_out,
):
    slab = frames[0]
    chans = slab.shape[2]
    staged = jnp.where(up_weight == up_weight, up_weight, jnp.zeros_like(up_weight))
    columns, slab = ring_all_gather(staged, "fsdp", ring, slab)
    padded = extended(slab, (("rows", 0),), 3)
    activation_rows = conv_rows(padded, kernel, kernel_bias)
    normed_output, standardized_input, inverse_deviation = apply_layer_norm(
        activation_rows, layer_norm_weight, layer_norm_bias
    )
    whole = tree_all_gather(normed_output, "rows")
    height = whole.shape[0]
    cols = whole.shape[1]
    flat = whole.reshape(-1, chans)
    pre = jnp.dot(flat, columns, preferred_element_type=jnp.float32) + up_bias
    post = jax.nn.gelu(pre, approximate=False)
    norms = jnp.sqrt(jnp.sum(post * post, axis=0) + 1e-06)
    cot_f = grad_out[0].reshape(flat.shape[0], -1).astype(jnp.float32)
    dnorm = grn_gamma * jnp.sum(cot_f * post, axis=0)
    norm_total = lax.psum(jnp.sum(norms), "rows")
    denom = norm_total / FF + 1e-06
    ratio = norms / denom
    output = (grn_gamma * (post * ratio) + grn_beta + post).astype(jnp.bfloat16)
    cross = lax.psum(jnp.sum(dnorm * norms), "rows")
    dnorms = dnorm / denom - cross / (denom * denom) / FF
    dpost = cot_f * (1.0 + grn_gamma * ratio) + post * (dnorms / norms)
    dpre = (dpost * gelu_grad(pre)).astype(jnp.bfloat16)
    w_term = lax.dot_general(
        flat, dpre, (((0,), (0,)), ((), ())), preferred_element_type=jnp.float32
    )
    up_grad = lax.psum_scatter(
        w_term.astype(jnp.bfloat16), "fsdp", scatter_dimension=0, tiled=True
    ).astype(jnp.float32)
    dpre_rows = dpre.reshape(height, cols, -1)
    group_terms = jnp.einsum(
        "hwf,cf->hwc", dpre_rows, columns, preferred_element_type=jnp.float32
    ).astype(jnp.bfloat16)
    n_rows = lax.axis_size("rows")
    normed_input_gradient = tree_reduce_scatter(
        group_terms.reshape((n_rows, height // n_rows) + group_terms.shape[1:]), "rows"
    )
    activation_gradient = layer_norm_backward(
        normed_input_gradient, layer_norm_weight, standardized_input, inverse_deviation
    )
    grad_pad = extended(activation_gradient, (("rows", 0),), 3)
    dframe = back_conv(grad_pad, kernel).astype(jnp.bfloat16)
    kernel_local = kern_grad(padded, activation_gradient)
    kernel_total = tree_allreduce(kernel_local, ("rows", "fsdp"))
    activation = output.reshape(1, height, cols, -1)
    return (activation, dframe.reshape((1,) + dframe.shape), up_grad, kernel_total)


def solution(mesh):
    placed = (
        P("fsdp", "rows", None, None),
        P(),
        P(),
        P(),
        P(),
        P("fsdp", "rows"),
        P("rows"),
        P("rows"),
        P("rows"),
        P("fsdp", None, None, "rows"),
    )
    return jax.shard_map(
        functools.partial(body, fsdp_ring(mesh)),
        mesh=mesh,
        in_specs=placed,
        out_specs=(
            P("fsdp", None, None, "rows"),
            P("fsdp", "rows", None, None),
            P("fsdp", "rows"),
            P(),
        ),
        check_vma=False,
    )
```

```python
import functools

import jax
import jax.numpy as jnp
from jax import lax
from jax.sharding import PartitionSpec as P

FF = 6144


def extended(block, sides, width):
    for axis, dim in sides:
        count = lax.axis_size(axis)
        forward = [(i, i + 1) for i in range(count - 1)]
        backward = [(target, source) for source, target in forward]
        low = lax.ppermute(
            lax.slice_in_dim(block, block.shape[dim] - width, None, axis=dim), axis, forward
        )
        high = lax.ppermute(lax.slice_in_dim(block, 0, width, axis=dim), axis, backward)
        block = jnp.concatenate([low, block, high], axis=dim)
    return block


def _bit_steps(axes):
    steps = []
    for axis in axes:
        size = lax.axis_size(axis)
        assert size & (size - 1) == 0
        mask = 1
        while mask < size:
            steps.append((axis, mask, size))
            mask *= 2
    return steps


def tree_allreduce(value, axes):
    shape = value.shape
    flat = value.reshape(-1)
    steps = _bit_steps(axes)
    assert flat.shape[0] % (1 << len(steps)) == 0
    bits = []
    for axis, mask, size in steps:
        bit = (lax.axis_index(axis) // mask) % 2
        bits.append(bit)
        halves = flat.reshape(2, -1)
        keep = lax.dynamic_index_in_dim(halves, bit, keepdims=False)
        give = lax.dynamic_index_in_dim(halves, 1 - bit, keepdims=False)
        perm = [(j, j ^ mask) for j in range(size)]
        flat = keep + lax.ppermute(give, axis, perm)
    for (axis, mask, size), bit in reversed(list(zip(steps, bits))):
        perm = [(j, j ^ mask) for j in range(size)]
        other = lax.ppermute(flat, axis, perm)
        flat = jnp.where(bit == 0, jnp.concatenate([flat, other]), jnp.concatenate([other, flat]))
    return flat.reshape(shape)


def tree_reduce_scatter(chunks, axis):
    size = lax.axis_size(axis)
    assert chunks.shape[0] == size and size & (size - 1) == 0
    me = lax.axis_index(axis)
    data = chunks
    mask = 1
    while mask < size:
        bit = (me // mask) % 2
        pairs = data.reshape((data.shape[0] // 2, 2) + data.shape[1:])
        keep = lax.dynamic_index_in_dim(pairs, bit, axis=1, keepdims=False)
        give = lax.dynamic_index_in_dim(pairs, 1 - bit, axis=1, keepdims=False)
        perm = [(j, j ^ mask) for j in range(size)]
        data = keep.astype(jnp.float32) + lax.ppermute(give, axis, perm).astype(jnp.float32)
        mask *= 2
    return data[0]


def fsdp_ring(mesh):
    count = mesh.shape["fsdp"]
    try:
        members = [mesh.devices[j, 0] for j in range(count)]
        spots = [(d.coords[2], d.coords[1]) for d in members]
        zs = sorted({z for z, _ in spots})
        ys = sorted({y for _, y in spots})
        rows_a, cols_b = len(zs), len(ys)
        where = {(zs.index(z), ys.index(y)): j for j, (z, y) in enumerate(spots)}
        assert len(where) == count == rows_a * cols_b and rows_a % 2 == 0 and cols_b >= 2
        cells = [(a, 0) for a in range(rows_a)]
        for k, a in enumerate(range(rows_a - 1, -1, -1)):
            span = range(1, cols_b) if k % 2 == 0 else range(cols_b - 1, 0, -1)
            cells += [(a, b) for b in span]
        ring = [where[c] for c in cells]
        assert sorted(ring) == list(range(count))
    except Exception:
        ring = list(range(count))
    return ring


def ring_all_gather(block, axis, ring, held=None):
    count = len(ring)
    place = [0] * count
    for k, j in enumerate(ring):
        place[j] = k
    ring_arr = jnp.array(ring, jnp.int32)
    me = lax.axis_index(axis)
    spot = jnp.array(place, jnp.int32)[me]
    forward = [(ring[k], ring[(k + 1) % count]) for k in range(count)]
    backward = [(ring[k], ring[(k - 1) % count]) for k in range(count)]
    ahead = count // 2
    behind = count - 1 - ahead
    gathered = jnp.zeros((count,) + block.shape, block.dtype)
    gathered = lax.dynamic_update_index_in_dim(gathered, block, me, 0)
    cw = block
    ccw = block
    split = count % 2 == 0 and count > 2
    for s in range(1, ahead + 1):
        if split and s == ahead:
            half = block.shape[-1] // 2
            cw = jnp.concatenate(
                [
                    lax.ppermute(cw[..., :half], axis, forward),
                    lax.ppermute(ccw[..., half:], axis, backward),
                ],
                axis=-1,
            )
            gathered = lax.dynamic_update_index_in_dim(
                gathered, cw, ring_arr[(spot - s) % count], 0
            )
            break
        if split and s == 1:
            half = block.shape[-1] // 2
            cw = jnp.concatenate(
                [lax.ppermute(cw[..., :half], axis, forward), lax.ppermute(cw[..., half:], axis, forward)],
                axis=-1,
            )
            ccw = jnp.concatenate(
                [lax.ppermute(ccw[..., :half], axis, backward), lax.ppermute(ccw[..., half:], axis, backward)],
                axis=-1,
            )
        else:
            cw = lax.ppermute(cw, axis, forward)
            if s <= behind:
                ccw = lax.ppermute(ccw, axis, backward)
        if s == 1 and held is not None:
            cw, ccw, held = lax.optimization_barrier((cw, ccw, held))
        gathered = lax.dynamic_update_index_in_dim(gathered, cw, ring_arr[(spot - s) % count], 0)
        if s <= behind:
            gathered = lax.dynamic_update_index_in_dim(
                gathered, ccw, ring_arr[(spot + s) % count], 0
            )
    return gathered.reshape((count * block.shape[0],) + block.shape[1:]), held


def ring_reduce_scatter(terms, axis, ring):
    count = len(ring)
    place = [0] * count
    for k, j in enumerate(ring):
        place[j] = k
    ring_arr = jnp.array(ring, jnp.int32)
    me = lax.axis_index(axis)
    spot = jnp.array(place, jnp.int32)[me]
    forward = [(ring[k], ring[(k + 1) % count]) for k in range(count)]
    backward = [(ring[k], ring[(k - 1) % count]) for k in range(count)]
    ahead = count // 2
    behind = count - 1 - ahead

    def term(offset):
        return lax.dynamic_index_in_dim(terms, ring_arr[(spot + offset) % count], 0, keepdims=False)

    total = term(0).astype(jnp.float32)
    cw = term(ahead)
    ccw = term(-behind) if behind else None
    for s in range(1, ahead + 1):
        cw = lax.ppermute(cw, axis, forward)
        if s <= behind:
            ccw = lax.ppermute(ccw, axis, backward)
        if s < ahead:
            cw = (cw.astype(jnp.float32) + term(ahead - s).astype(jnp.float32)).astype(terms.dtype)
        else:
            total = total + cw.astype(jnp.float32)
        if s < behind:
            ccw = (ccw.astype(jnp.float32) + term(s - behind).astype(jnp.float32)).astype(terms.dtype)
        elif s == behind:
            total = total + ccw.astype(jnp.float32)
    return total


def tree_all_gather(block, axis):
    size = lax.axis_size(axis)
    assert size & (size - 1) == 0
    me = lax.axis_index(axis)
    data = block[None]
    mask = 1
    while mask < size:
        bit = (me // mask) % 2
        perm = [(j, j ^ mask) for j in range(size)]
        other = lax.ppermute(data, axis, perm)
        data = jnp.where(bit == 0, jnp.concatenate([data, other]), jnp.concatenate([other, data]))
        mask *= 2
    return data.reshape((size * block.shape[0],) + block.shape[1:])


def conv_rows(framed, kern, kbias):
    rows = framed.shape[0] - 6
    cols = framed.shape[1]
    wide = jnp.pad(framed, ((0, 0), (3, 3), (0, 0)))
    total = jnp.zeros((rows, cols, framed.shape[2]), jnp.float32) + kbias
    for i in range(kern.shape[0]):
        for j in range(kern.shape[1]):
            total = total + wide[i : i + rows, j : j + cols].astype(jnp.float32) * kern[i, j]
    return total


def back_conv(grad_pad, kern):
    rows = grad_pad.shape[0] - 6
    cols = grad_pad.shape[1]
    wide = jnp.pad(grad_pad, ((0, 0), (3, 3), (0, 0)))
    total = jnp.zeros((rows, cols, grad_pad.shape[2]), jnp.float32)
    for i in range(kern.shape[0]):
        for j in range(kern.shape[1]):
            total = (
                total
                + wide[6 - i : 6 - i + rows, 6 - j : 6 - j + cols].astype(jnp.float32) * kern[i, j]
            )
    return total


def kern_grad(framed, grad_rows):
    rows = grad_rows.shape[0]
    cols = grad_rows.shape[1]
    wide = jnp.pad(framed, ((0, 0), (3, 3), (0, 0)))
    grad_f = grad_rows.astype(jnp.float32)
    parts = []
    for i in range(7):
        for j in range(7):
            parts.append(
                jnp.sum(wide[i : i + rows, j : j + cols].astype(jnp.float32) * grad_f, axis=(0, 1))
            )
    return jnp.stack(parts).reshape(7, 7, grad_rows.shape[2])


def apply_layer_norm(activation_rows, scale_factor, offset_bias):
    centered_input = activation_rows - jnp.mean(activation_rows, axis=-1, keepdims=True)
    inverse_deviation = lax.rsqrt(
        jnp.mean(centered_input * centered_input, axis=-1, keepdims=True) + 1e-06
    )
    standardized_input = centered_input * inverse_deviation
    return (
        (standardized_input * scale_factor + offset_bias).astype(jnp.bfloat16),
        standardized_input,
        inverse_deviation,
    )


def gelu_grad(value):
    return (
        0.5 * (1.0 + jax.scipy.special.erf(value * 0.7071067811865476))
        + value * jnp.exp(-0.5 * value * value) * 0.3989422804014327
    )


def layer_norm_backward(normed_input_gradient, scale_factor, standardized_input, inverse_deviation):
    scaled_output = normed_input_gradient * scale_factor
    return (
        inverse_deviation
        * (
            scaled_output
            - jnp.mean(scaled_output, axis=-1, keepdims=True)
            - standardized_input
            * jnp.mean(scaled_output * standardized_input, axis=-1, keepdims=True)
        )
    ).astype(jnp.bfloat16)


def body(
    ring,
    frames,
    kernel,
    kernel_bias,
    layer_norm_weight,
    layer_norm_bias,
    up_weight,
    up_bias,
    grn_gamma,
    grn_beta,
    grad_out,
):
    slab = frames[0]
    chans = slab.shape[2]
    staged = jnp.where(up_weight == up_weight, up_weight, jnp.zeros_like(up_weight))
    columns, slab = ring_all_gather(staged, "fsdp", ring, slab)
    padded = extended(slab, (("rows", 0),), 3)
    activation_rows = conv_rows(padded, kernel, kernel_bias)
    normed_output, standardized_input, inverse_deviation = apply_layer_norm(
        activation_rows, layer_norm_weight, layer_norm_bias
    )
    whole = tree_all_gather(normed_output, "rows")
    height = whole.shape[0]
    cols = whole.shape[1]
    flat = whole.reshape(-1, chans)
    pre = jnp.dot(flat, columns, preferred_element_type=jnp.float32) + up_bias
    post = jax.nn.gelu(pre, approximate=False)
    norms = jnp.sqrt(jnp.sum(post * post, axis=0) + 1e-06)
    cot_f = grad_out[0].reshape(flat.shape[0], -1).astype(jnp.float32)
    dnorm = grn_gamma * jnp.sum(cot_f * post, axis=0)
    norm_total = lax.psum(jnp.sum(norms), "rows")
    denom = norm_total / FF + 1e-06
    ratio = norms / denom
    output = (grn_gamma * (post * ratio) + grn_beta + post).astype(jnp.bfloat16)
    cross = lax.psum(jnp.sum(dnorm * norms), "rows")
    dnorms = dnorm / denom - cross / (denom * denom) / FF
    dpost = cot_f * (1.0 + grn_gamma * ratio) + post * (dnorms / norms)
    dpre = (dpost * gelu_grad(pre)).astype(jnp.bfloat16)
    w_term = lax.dot_general(
        flat, dpre, (((0,), (0,)), ((), ())), preferred_element_type=jnp.float32
    )
    up_grad = lax.psum_scatter(
        w_term.astype(jnp.bfloat16), "fsdp", scatter_dimension=0, tiled=True
    ).astype(jnp.float32)
    dpre_rows = dpre.reshape(height, cols, -1)
    group_terms = jnp.einsum(
        "hwf,cf->hwc", dpre_rows, columns, preferred_element_type=jnp.float32
    ).astype(jnp.bfloat16)
    n_rows = lax.axis_size("rows")
    normed_input_gradient = tree_reduce_scatter(
        group_terms.reshape((n_rows, height // n_rows) + group_terms.shape[1:]), "rows"
    )
    activation_gradient = layer_norm_backward(
        normed_input_gradient, layer_norm_weight, standardized_input, inverse_deviation
    )
    grad_pad = extended(activation_gradient, (("rows", 0),), 3)
    dframe = back_conv(grad_pad, kernel).astype(jnp.bfloat16)
    kernel_local = kern_grad(padded, activation_gradient)
    kernel_total = tree_allreduce(kernel_local, ("rows", "fsdp"))
    activation = output.reshape(1, height, cols, -1)
    return (activation, dframe.reshape((1,) + dframe.shape), up_grad, kernel_total)


def solution(mesh):
    placed = (
        P("fsdp", "rows", None, None),
        P(),
        P(),
        P(),
        P(),
        P("fsdp", "rows"),
        P("rows"),
        P("rows"),
        P("rows"),
        P("fsdp", None, None, "rows"),
    )
    return jax.shard_map(
        functools.partial(body, fsdp_ring(mesh)),
        mesh=mesh,
        in_specs=placed,
        out_specs=(
            P("fsdp", None, None, "rows"),
            P("fsdp", "rows", None, None),
            P("fsdp", "rows"),
            P(),
        ),
        check_vma=False,
    )
```

```python
import functools

import jax
import jax.numpy as jnp
from jax import lax
from jax.sharding import PartitionSpec as P

FF = 6144


def extended(block, sides, width):
    for axis, dim in sides:
        count = lax.axis_size(axis)
        forward = [(i, i + 1) for i in range(count - 1)]
        backward = [(target, source) for source, target in forward]
        low = lax.ppermute(
            lax.slice_in_dim(block, block.shape[dim] - width, None, axis=dim), axis, forward
        )
        high = lax.ppermute(lax.slice_in_dim(block, 0, width, axis=dim), axis, backward)
        block = jnp.concatenate([low, block, high], axis=dim)
    return block


def _bit_steps(axes):
    steps = []
    for axis in axes:
        size = lax.axis_size(axis)
        assert size & (size - 1) == 0
        mask = 1
        while mask < size:
            steps.append((axis, mask, size))
            mask *= 2
    return steps


def tree_allreduce(value, axes):
    shape = value.shape
    flat = value.reshape(-1)
    steps = _bit_steps(axes)
    assert flat.shape[0] % (1 << len(steps)) == 0
    bits = []
    for axis, mask, size in steps:
        bit = (lax.axis_index(axis) // mask) % 2
        bits.append(bit)
        halves = flat.reshape(2, -1)
        keep = lax.dynamic_index_in_dim(halves, bit, keepdims=False)
        give = lax.dynamic_index_in_dim(halves, 1 - bit, keepdims=False)
        perm = [(j, j ^ mask) for j in range(size)]
        flat = keep + lax.ppermute(give, axis, perm)
    for (axis, mask, size), bit in reversed(list(zip(steps, bits))):
        perm = [(j, j ^ mask) for j in range(size)]
        other = lax.ppermute(flat, axis, perm)
        flat = jnp.where(bit == 0, jnp.concatenate([flat, other]), jnp.concatenate([other, flat]))
    return flat.reshape(shape)


def tree_reduce_scatter(chunks, axis):
    size = lax.axis_size(axis)
    assert chunks.shape[0] == size and size & (size - 1) == 0
    me = lax.axis_index(axis)
    data = chunks
    mask = 1
    while mask < size:
        bit = (me // mask) % 2
        pairs = data.reshape((data.shape[0] // 2, 2) + data.shape[1:])
        keep = lax.dynamic_index_in_dim(pairs, bit, axis=1, keepdims=False)
        give = lax.dynamic_index_in_dim(pairs, 1 - bit, axis=1, keepdims=False)
        perm = [(j, j ^ mask) for j in range(size)]
        data = keep.astype(jnp.float32) + lax.ppermute(give, axis, perm).astype(jnp.float32)
        mask *= 2
    return data[0]


def fsdp_ring(mesh):
    count = mesh.shape["fsdp"]
    try:
        members = [mesh.devices[j, 0] for j in range(count)]
        spots = [(d.coords[2], d.coords[1]) for d in members]
        zs = sorted({z for z, _ in spots})
        ys = sorted({y for _, y in spots})
        rows_a, cols_b = len(zs), len(ys)
        where = {(zs.index(z), ys.index(y)): j for j, (z, y) in enumerate(spots)}
        assert len(where) == count == rows_a * cols_b and rows_a % 2 == 0 and cols_b >= 2
        cells = [(a, 0) for a in range(rows_a)]
        for k, a in enumerate(range(rows_a - 1, -1, -1)):
            span = range(1, cols_b) if k % 2 == 0 else range(cols_b - 1, 0, -1)
            cells += [(a, b) for b in span]
        ring = [where[c] for c in cells]
        assert sorted(ring) == list(range(count))
    except Exception:
        ring = list(range(count))
    return ring


def ring_all_gather(block, axis, ring, held=None):
    count = len(ring)
    place = [0] * count
    for k, j in enumerate(ring):
        place[j] = k
    ring_arr = jnp.array(ring, jnp.int32)
    me = lax.axis_index(axis)
    spot = jnp.array(place, jnp.int32)[me]
    forward = [(ring[k], ring[(k + 1) % count]) for k in range(count)]
    backward = [(ring[k], ring[(k - 1) % count]) for k in range(count)]
    ahead = count // 2
    behind = count - 1 - ahead
    gathered = jnp.zeros((count,) + block.shape, block.dtype)
    gathered = lax.dynamic_update_index_in_dim(gathered, block, me, 0)
    cw = block
    ccw = block
    split = count % 2 == 0 and count > 2
    for s in range(1, ahead + 1):
        if split and s == ahead:
            half = block.shape[-1] // 2
            cw = jnp.concatenate(
                [
                    lax.ppermute(cw[..., :half], axis, forward),
                    lax.ppermute(ccw[..., half:], axis, backward),
                ],
                axis=-1,
            )
            gathered = lax.dynamic_update_index_in_dim(
                gathered, cw, ring_arr[(spot - s) % count], 0
            )
            break
        cw = lax.ppermute(cw, axis, forward)
        if s <= behind:
            ccw = lax.ppermute(ccw, axis, backward)
        if s == 1 and held is not None:
            cw, ccw, held = lax.optimization_barrier((cw, ccw, held))
        gathered = lax.dynamic_update_index_in_dim(gathered, cw, ring_arr[(spot - s) % count], 0)
        if s <= behind:
            gathered = lax.dynamic_update_index_in_dim(
                gathered, ccw, ring_arr[(spot + s) % count], 0
            )
    return gathered.reshape((count * block.shape[0],) + block.shape[1:]), held


def ring_reduce_scatter(terms, axis, ring):
    count = len(ring)
    place = [0] * count
    for k, j in enumerate(ring):
        place[j] = k
    ring_arr = jnp.array(ring, jnp.int32)
    me = lax.axis_index(axis)
    spot = jnp.array(place, jnp.int32)[me]
    forward = [(ring[k], ring[(k + 1) % count]) for k in range(count)]
    backward = [(ring[k], ring[(k - 1) % count]) for k in range(count)]
    ahead = count // 2
    behind = count - 1 - ahead

    def term(offset):
        return lax.dynamic_index_in_dim(terms, ring_arr[(spot + offset) % count], 0, keepdims=False)

    total = term(0).astype(jnp.float32)
    cw = term(ahead)
    ccw = term(-behind) if behind else None
    for s in range(1, ahead + 1):
        cw = lax.ppermute(cw, axis, forward)
        if s <= behind:
            ccw = lax.ppermute(ccw, axis, backward)
        if s < ahead:
            cw = (cw.astype(jnp.float32) + term(ahead - s).astype(jnp.float32)).astype(terms.dtype)
        else:
            total = total + cw.astype(jnp.float32)
        if s < behind:
            ccw = (ccw.astype(jnp.float32) + term(s - behind).astype(jnp.float32)).astype(terms.dtype)
        elif s == behind:
            total = total + ccw.astype(jnp.float32)
    return total


def tree_all_gather(block, axis):
    size = lax.axis_size(axis)
    assert size & (size - 1) == 0
    me = lax.axis_index(axis)
    data = block[None]
    mask = 1
    while mask < size:
        bit = (me // mask) % 2
        perm = [(j, j ^ mask) for j in range(size)]
        other = lax.ppermute(data, axis, perm)
        data = jnp.where(bit == 0, jnp.concatenate([data, other]), jnp.concatenate([other, data]))
        mask *= 2
    return data.reshape((size * block.shape[0],) + block.shape[1:])


def doubling_sum(value, axis):
    size = lax.axis_size(axis)
    assert size & (size - 1) == 0
    mask = 1
    while mask < size:
        value = value + lax.ppermute(value, axis, [(j, j ^ mask) for j in range(size)])
        mask *= 2
    return value


def conv_rows(framed, kern, kbias):
    rows = framed.shape[0] - 6
    cols = framed.shape[1]
    wide = jnp.pad(framed, ((0, 0), (3, 3), (0, 0)))
    total = jnp.zeros((rows, cols, framed.shape[2]), jnp.float32) + kbias
    for i in range(kern.shape[0]):
        for j in range(kern.shape[1]):
            total = total + wide[i : i + rows, j : j + cols].astype(jnp.float32) * kern[i, j]
    return total


def back_conv(grad_pad, kern):
    rows = grad_pad.shape[0] - 6
    cols = grad_pad.shape[1]
    wide = jnp.pad(grad_pad, ((0, 0), (3, 3), (0, 0)))
    total = jnp.zeros((rows, cols, grad_pad.shape[2]), jnp.float32)
    for i in range(kern.shape[0]):
        for j in range(kern.shape[1]):
            total = (
                total
                + wide[6 - i : 6 - i + rows, 6 - j : 6 - j + cols].astype(jnp.float32) * kern[i, j]
            )
    return total


def kern_grad(framed, grad_rows):
    rows = grad_rows.shape[0]
    cols = grad_rows.shape[1]
    wide = jnp.pad(framed, ((0, 0), (3, 3), (0, 0)))
    grad_f = grad_rows.astype(jnp.float32)
    parts = []
    for i in range(7):
        for j in range(7):
            parts.append(
                jnp.sum(wide[i : i + rows, j : j + cols].astype(jnp.float32) * grad_f, axis=(0, 1))
            )
    return jnp.stack(parts).reshape(7, 7, grad_rows.shape[2])


def apply_layer_norm(activation_rows, scale_factor, offset_bias):
    centered_input = activation_rows - jnp.mean(activation_rows, axis=-1, keepdims=True)
    inverse_deviation = lax.rsqrt(
        jnp.mean(centered_input * centered_input, axis=-1, keepdims=True) + 1e-06
    )
    standardized_input = centered_input * inverse_deviation
    return (
        (standardized_input * scale_factor + offset_bias).astype(jnp.bfloat16),
        standardized_input,
        inverse_deviation,
    )


def gelu_grad(value):
    return (
        0.5 * (1.0 + jax.scipy.special.erf(value * 0.7071067811865476))
        + value * jnp.exp(-0.5 * value * value) * 0.3989422804014327
    )


def layer_norm_backward(normed_input_gradient, scale_factor, standardized_input, inverse_deviation):
    scaled_output = normed_input_gradient * scale_factor
    return (
        inverse_deviation
        * (
            scaled_output
            - jnp.mean(scaled_output, axis=-1, keepdims=True)
            - standardized_input
            * jnp.mean(scaled_output * standardized_input, axis=-1, keepdims=True)
        )
    ).astype(jnp.bfloat16)


def body(
    ring,
    frames,
    kernel,
    kernel_bias,
    layer_norm_weight,
    layer_norm_bias,
    up_weight,
    up_bias,
    grn_gamma,
    grn_beta,
    grad_out,
):
    slab = frames[0]
    chans = slab.shape[2]
    staged = jnp.where(up_weight == up_weight, up_weight, jnp.zeros_like(up_weight))
    columns, slab = ring_all_gather(staged, "fsdp", ring, slab)
    padded = extended(slab, (("rows", 0),), 3)
    activation_rows = conv_rows(padded, kernel, kernel_bias)
    normed_output, standardized_input, inverse_deviation = apply_layer_norm(
        activation_rows, layer_norm_weight, layer_norm_bias
    )
    whole = tree_all_gather(normed_output, "rows")
    height = whole.shape[0]
    cols = whole.shape[1]
    flat = whole.reshape(-1, chans)
    pre = jnp.dot(flat, columns, preferred_element_type=jnp.float32) + up_bias
    post = jax.nn.gelu(pre, approximate=False)
    norms = jnp.sqrt(jnp.sum(post * post, axis=0) + 1e-06)
    cot_f = grad_out[0].reshape(flat.shape[0], -1).astype(jnp.float32)
    dnorm = grn_gamma * jnp.sum(cot_f * post, axis=0)
    totals = doubling_sum(jnp.stack([jnp.sum(norms), jnp.sum(dnorm * norms)]), "rows")
    norm_total = totals[0]
    denom = norm_total / FF + 1e-06
    ratio = norms / denom
    output = (grn_gamma * (post * ratio) + grn_beta + post).astype(jnp.bfloat16)
    cross = totals[1]
    dnorms = dnorm / denom - cross / (denom * denom) / FF
    dpost = cot_f * (1.0 + grn_gamma * ratio) + post * (dnorms / norms)
    dpre = (dpost * gelu_grad(pre)).astype(jnp.bfloat16)
    w_term = lax.dot_general(
        flat, dpre, (((0,), (0,)), ((), ())), preferred_element_type=jnp.float32
    )
    up_grad = lax.psum_scatter(
        w_term.astype(jnp.bfloat16), "fsdp", scatter_dimension=0, tiled=True
    ).astype(jnp.float32)
    dpre_rows = dpre.reshape(height, cols, -1)
    group_terms = jnp.einsum(
        "hwf,cf->hwc", dpre_rows, columns, preferred_element_type=jnp.float32
    ).astype(jnp.bfloat16)
    n_rows = lax.axis_size("rows")
    normed_input_gradient = tree_reduce_scatter(
        group_terms.reshape((n_rows, height // n_rows) + group_terms.shape[1:]), "rows"
    )
    activation_gradient = layer_norm_backward(
        normed_input_gradient, layer_norm_weight, standardized_input, inverse_deviation
    )
    grad_pad = extended(activation_gradient, (("rows", 0),), 3)
    dframe = back_conv(grad_pad, kernel).astype(jnp.bfloat16)
    kernel_local = kern_grad(padded, activation_gradient)
    kernel_total = tree_allreduce(kernel_local, ("rows", "fsdp"))
    activation = output.reshape(1, height, cols, -1)
    return (activation, dframe.reshape((1,) + dframe.shape), up_grad, kernel_total)


def solution(mesh):
    placed = (
        P("fsdp", "rows", None, None),
        P(),
        P(),
        P(),
        P(),
        P("fsdp", "rows"),
        P("rows"),
        P("rows"),
        P("rows"),
        P("fsdp", None, None, "rows"),
    )
    return jax.shard_map(
        functools.partial(body, fsdp_ring(mesh)),
        mesh=mesh,
        in_specs=placed,
        out_specs=(
            P("fsdp", None, None, "rows"),
            P("fsdp", "rows", None, None),
            P("fsdp", "rows"),
            P(),
        ),
        check_vma=False,
    )
```

```python
import functools

import jax
import jax.numpy as jnp
from jax import lax
from jax.sharding import PartitionSpec as P

FF = 6144


def extended(block, sides, width):
    for axis, dim in sides:
        count = lax.axis_size(axis)
        forward = [(i, i + 1) for i in range(count - 1)]
        backward = [(target, source) for source, target in forward]
        low = lax.ppermute(
            lax.slice_in_dim(block, block.shape[dim] - width, None, axis=dim), axis, forward
        )
        high = lax.ppermute(lax.slice_in_dim(block, 0, width, axis=dim), axis, backward)
        block = jnp.concatenate([low, block, high], axis=dim)
    return block


def _bit_steps(axes):
    steps = []
    for axis in axes:
        size = lax.axis_size(axis)
        assert size & (size - 1) == 0
        mask = 1
        while mask < size:
            steps.append((axis, mask, size))
            mask *= 2
    return steps


def tree_allreduce(value, axes):
    shape = value.shape
    flat = value.reshape(-1)
    steps = _bit_steps(axes)
    assert flat.shape[0] % (1 << len(steps)) == 0
    bits = []
    for axis, mask, size in steps:
        bit = (lax.axis_index(axis) // mask) % 2
        bits.append(bit)
        halves = flat.reshape(2, -1)
        keep = lax.dynamic_index_in_dim(halves, bit, keepdims=False)
        give = lax.dynamic_index_in_dim(halves, 1 - bit, keepdims=False)
        perm = [(j, j ^ mask) for j in range(size)]
        flat = keep + lax.ppermute(give, axis, perm)
    for (axis, mask, size), bit in reversed(list(zip(steps, bits))):
        perm = [(j, j ^ mask) for j in range(size)]
        other = lax.ppermute(flat, axis, perm)
        flat = jnp.where(bit == 0, jnp.concatenate([flat, other]), jnp.concatenate([other, flat]))
    return flat.reshape(shape)


def tree_reduce_scatter(chunks, axis):
    size = lax.axis_size(axis)
    assert chunks.shape[0] == size and size & (size - 1) == 0
    me = lax.axis_index(axis)
    data = chunks
    mask = 1
    while mask < size:
        bit = (me // mask) % 2
        pairs = data.reshape((data.shape[0] // 2, 2) + data.shape[1:])
        keep = lax.dynamic_index_in_dim(pairs, bit, axis=1, keepdims=False)
        give = lax.dynamic_index_in_dim(pairs, 1 - bit, axis=1, keepdims=False)
        perm = [(j, j ^ mask) for j in range(size)]
        data = keep.astype(jnp.float32) + lax.ppermute(give, axis, perm).astype(jnp.float32)
        mask *= 2
    return data[0]


def fsdp_ring(mesh):
    count = mesh.shape["fsdp"]
    try:
        members = [mesh.devices[j, 0] for j in range(count)]
        spots = [(d.coords[2], d.coords[1]) for d in members]
        zs = sorted({z for z, _ in spots})
        ys = sorted({y for _, y in spots})
        rows_a, cols_b = len(zs), len(ys)
        where = {(zs.index(z), ys.index(y)): j for j, (z, y) in enumerate(spots)}
        assert len(where) == count == rows_a * cols_b and rows_a % 2 == 0 and cols_b >= 2
        cells = [(a, 0) for a in range(rows_a)]
        for k, a in enumerate(range(rows_a - 1, -1, -1)):
            span = range(1, cols_b) if k % 2 == 0 else range(cols_b - 1, 0, -1)
            cells += [(a, b) for b in span]
        ring = [where[c] for c in cells]
        assert sorted(ring) == list(range(count))
    except Exception:
        ring = list(range(count))
    return ring


def ring_all_gather(block, axis, ring, held=None):
    count = len(ring)
    place = [0] * count
    for k, j in enumerate(ring):
        place[j] = k
    ring_arr = jnp.array(ring, jnp.int32)
    me = lax.axis_index(axis)
    spot = jnp.array(place, jnp.int32)[me]
    forward = [(ring[k], ring[(k + 1) % count]) for k in range(count)]
    backward = [(ring[k], ring[(k - 1) % count]) for k in range(count)]
    ahead = count // 2
    behind = count - 1 - ahead
    gathered = jnp.zeros((count,) + block.shape, block.dtype)
    gathered = lax.dynamic_update_index_in_dim(gathered, block, me, 0)
    cw = block
    ccw = block
    split = count % 2 == 0 and count > 2
    for s in range(1, ahead + 1):
        if split and s == ahead:
            half = block.shape[-1] // 2
            cw = jnp.concatenate(
                [
                    lax.ppermute(cw[..., :half], axis, forward),
                    lax.ppermute(ccw[..., half:], axis, backward),
                ],
                axis=-1,
            )
            gathered = lax.dynamic_update_index_in_dim(
                gathered, cw, ring_arr[(spot - s) % count], 0
            )
            break
        cw = lax.ppermute(cw, axis, forward)
        if s <= behind:
            ccw = lax.ppermute(ccw, axis, backward)
        if s == 1 and held is not None:
            cw, ccw, held = lax.optimization_barrier((cw, ccw, held))
        gathered = lax.dynamic_update_index_in_dim(gathered, cw, ring_arr[(spot - s) % count], 0)
        if s <= behind:
            gathered = lax.dynamic_update_index_in_dim(
                gathered, ccw, ring_arr[(spot + s) % count], 0
            )
    return gathered.reshape((count * block.shape[0],) + block.shape[1:]), held


def ring_reduce_scatter(terms, axis, ring):
    count = len(ring)
    place = [0] * count
    for k, j in enumerate(ring):
        place[j] = k
    ring_arr = jnp.array(ring, jnp.int32)
    me = lax.axis_index(axis)
    spot = jnp.array(place, jnp.int32)[me]
    forward = [(ring[k], ring[(k + 1) % count]) for k in range(count)]
    backward = [(ring[k], ring[(k - 1) % count]) for k in range(count)]
    ahead = count // 2
    behind = count - 1 - ahead

    def term(offset):
        return lax.dynamic_index_in_dim(terms, ring_arr[(spot + offset) % count], 0, keepdims=False)

    total = term(0).astype(jnp.float32)
    cw = term(ahead)
    ccw = term(-behind) if behind else None
    for s in range(1, ahead + 1):
        cw = lax.ppermute(cw, axis, forward)
        if s <= behind:
            ccw = lax.ppermute(ccw, axis, backward)
        if s < ahead:
            cw = (cw.astype(jnp.float32) + term(ahead - s).astype(jnp.float32)).astype(terms.dtype)
        else:
            total = total + cw.astype(jnp.float32)
        if s < behind:
            ccw = (ccw.astype(jnp.float32) + term(s - behind).astype(jnp.float32)).astype(terms.dtype)
        elif s == behind:
            total = total + ccw.astype(jnp.float32)
    return total


def tree_all_gather(block, axis):
    size = lax.axis_size(axis)
    assert size & (size - 1) == 0
    me = lax.axis_index(axis)
    data = block[None]
    mask = size // 2
    bits = 0
    while mask >= 1:
        bit = (me // mask) % 2
        perm = [(j, j ^ mask) for j in range(size)]
        other = lax.ppermute(data, axis, perm)
        data = jnp.where(bit == 0, jnp.concatenate([data, other]), jnp.concatenate([other, data]))
        mask //= 2
        bits += 1
    data = data.reshape((2,) * bits + block.shape)
    data = jnp.transpose(data, tuple(reversed(range(bits))) + tuple(range(bits, data.ndim)))
    return data.reshape((size * block.shape[0],) + block.shape[1:])


def conv_rows(framed, kern, kbias):
    rows = framed.shape[0] - 6
    cols = framed.shape[1]
    wide = jnp.pad(framed, ((0, 0), (3, 3), (0, 0)))
    total = jnp.zeros((rows, cols, framed.shape[2]), jnp.float32) + kbias
    for i in range(kern.shape[0]):
        for j in range(kern.shape[1]):
            total = total + wide[i : i + rows, j : j + cols].astype(jnp.float32) * kern[i, j]
    return total


def back_conv(grad_pad, kern):
    rows = grad_pad.shape[0] - 6
    cols = grad_pad.shape[1]
    wide = jnp.pad(grad_pad, ((0, 0), (3, 3), (0, 0)))
    total = jnp.zeros((rows, cols, grad_pad.shape[2]), jnp.float32)
    for i in range(kern.shape[0]):
        for j in range(kern.shape[1]):
            total = (
                total
                + wide[6 - i : 6 - i + rows, 6 - j : 6 - j + cols].astype(jnp.float32) * kern[i, j]
            )
    return total


def kern_grad(framed, grad_rows):
    rows = grad_rows.shape[0]
    cols = grad_rows.shape[1]
    wide = jnp.pad(framed, ((0, 0), (3, 3), (0, 0)))
    grad_f = grad_rows.astype(jnp.float32)
    parts = []
    for i in range(7):
        for j in range(7):
            parts.append(
                jnp.sum(wide[i : i + rows, j : j + cols].astype(jnp.float32) * grad_f, axis=(0, 1))
            )
    return jnp.stack(parts).reshape(7, 7, grad_rows.shape[2])


def apply_layer_norm(activation_rows, scale_factor, offset_bias):
    centered_input = activation_rows - jnp.mean(activation_rows, axis=-1, keepdims=True)
    inverse_deviation = lax.rsqrt(
        jnp.mean(centered_input * centered_input, axis=-1, keepdims=True) + 1e-06
    )
    standardized_input = centered_input * inverse_deviation
    return (
        (standardized_input * scale_factor + offset_bias).astype(jnp.bfloat16),
        standardized_input,
        inverse_deviation,
    )


def gelu_grad(value):
    return (
        0.5 * (1.0 + jax.scipy.special.erf(value * 0.7071067811865476))
        + value * jnp.exp(-0.5 * value * value) * 0.3989422804014327
    )


def layer_norm_backward(normed_input_gradient, scale_factor, standardized_input, inverse_deviation):
    scaled_output = normed_input_gradient * scale_factor
    return (
        inverse_deviation
        * (
            scaled_output
            - jnp.mean(scaled_output, axis=-1, keepdims=True)
            - standardized_input
            * jnp.mean(scaled_output * standardized_input, axis=-1, keepdims=True)
        )
    ).astype(jnp.bfloat16)


def body(
    ring,
    frames,
    kernel,
    kernel_bias,
    layer_norm_weight,
    layer_norm_bias,
    up_weight,
    up_bias,
    grn_gamma,
    grn_beta,
    grad_out,
):
    slab = frames[0]
    chans = slab.shape[2]
    staged = jnp.where(up_weight == up_weight, up_weight, jnp.zeros_like(up_weight))
    columns, slab = ring_all_gather(staged, "fsdp", ring, slab)
    padded = extended(slab, (("rows", 0),), 3)
    activation_rows = conv_rows(padded, kernel, kernel_bias)
    normed_output, standardized_input, inverse_deviation = apply_layer_norm(
        activation_rows, layer_norm_weight, layer_norm_bias
    )
    whole = tree_all_gather(normed_output, "rows")
    height = whole.shape[0]
    cols = whole.shape[1]
    flat = whole.reshape(-1, chans)
    pre = jnp.dot(flat, columns, preferred_element_type=jnp.float32) + up_bias
    post = jax.nn.gelu(pre, approximate=False)
    norms = jnp.sqrt(jnp.sum(post * post, axis=0) + 1e-06)
    cot_f = grad_out[0].reshape(flat.shape[0], -1).astype(jnp.float32)
    dnorm = grn_gamma * jnp.sum(cot_f * post, axis=0)
    norm_total = lax.psum(jnp.sum(norms), "rows")
    denom = norm_total / FF + 1e-06
    ratio = norms / denom
    output = (grn_gamma * (post * ratio) + grn_beta + post).astype(jnp.bfloat16)
    cross = lax.psum(jnp.sum(dnorm * norms), "rows")
    dnorms = dnorm / denom - cross / (denom * denom) / FF
    dpost = cot_f * (1.0 + grn_gamma * ratio) + post * (dnorms / norms)
    dpre = (dpost * gelu_grad(pre)).astype(jnp.bfloat16)
    w_term = lax.dot_general(
        flat, dpre, (((0,), (0,)), ((), ())), preferred_element_type=jnp.float32
    )
    up_grad = lax.psum_scatter(
        w_term.astype(jnp.bfloat16), "fsdp", scatter_dimension=0, tiled=True
    ).astype(jnp.float32)
    dpre_rows = dpre.reshape(height, cols, -1)
    group_terms = jnp.einsum(
        "hwf,cf->hwc", dpre_rows, columns, preferred_element_type=jnp.float32
    ).astype(jnp.bfloat16)
    n_rows = lax.axis_size("rows")
    normed_input_gradient = tree_reduce_scatter(
        group_terms.reshape((n_rows, height // n_rows) + group_terms.shape[1:]), "rows"
    )
    activation_gradient = layer_norm_backward(
        normed_input_gradient, layer_norm_weight, standardized_input, inverse_deviation
    )
    grad_pad = extended(activation_gradient, (("rows", 0),), 3)
    dframe = back_conv(grad_pad, kernel).astype(jnp.bfloat16)
    kernel_local = kern_grad(padded, activation_gradient)
    kernel_total = tree_allreduce(kernel_local, ("rows", "fsdp"))
    activation = output.reshape(1, height, cols, -1)
    return (activation, dframe.reshape((1,) + dframe.shape), up_grad, kernel_total)


def solution(mesh):
    placed = (
        P("fsdp", "rows", None, None),
        P(),
        P(),
        P(),
        P(),
        P("fsdp", "rows"),
        P("rows"),
        P("rows"),
        P("rows"),
        P("fsdp", None, None, "rows"),
    )
    return jax.shard_map(
        functools.partial(body, fsdp_ring(mesh)),
        mesh=mesh,
        in_specs=placed,
        out_specs=(
            P("fsdp", None, None, "rows"),
            P("fsdp", "rows", None, None),
            P("fsdp", "rows"),
            P(),
        ),
        check_vma=False,
    )
```

```python
import functools

import jax
import jax.numpy as jnp
from jax import lax
from jax.sharding import PartitionSpec as P

FF = 6144


def extended(block, sides, width):
    for axis, dim in sides:
        count = lax.axis_size(axis)
        forward = [(i, i + 1) for i in range(count - 1)]
        backward = [(target, source) for source, target in forward]
        low = lax.ppermute(
            lax.slice_in_dim(block, block.shape[dim] - width, None, axis=dim), axis, forward
        )
        high = lax.ppermute(lax.slice_in_dim(block, 0, width, axis=dim), axis, backward)
        block = jnp.concatenate([low, block, high], axis=dim)
    return block


def _bit_steps(axes):
    steps = []
    for axis in axes:
        size = lax.axis_size(axis)
        assert size & (size - 1) == 0
        mask = 1
        while mask < size:
            steps.append((axis, mask, size))
            mask *= 2
    return steps


def tree_allreduce(value, axes):
    shape = value.shape
    flat = value.reshape(-1)
    steps = _bit_steps(axes)
    assert flat.shape[0] % (1 << len(steps)) == 0
    bits = []
    for axis, mask, size in steps:
        bit = (lax.axis_index(axis) // mask) % 2
        bits.append(bit)
        halves = flat.reshape(2, -1)
        keep = lax.dynamic_index_in_dim(halves, bit, keepdims=False)
        give = lax.dynamic_index_in_dim(halves, 1 - bit, keepdims=False)
        perm = [(j, j ^ mask) for j in range(size)]
        flat = keep + lax.ppermute(give, axis, perm)
    for (axis, mask, size), bit in reversed(list(zip(steps, bits))):
        perm = [(j, j ^ mask) for j in range(size)]
        other = lax.ppermute(flat, axis, perm)
        flat = jnp.where(bit == 0, jnp.concatenate([flat, other]), jnp.concatenate([other, flat]))
    return flat.reshape(shape)


def tree_reduce_scatter(chunks, axis):
    size = lax.axis_size(axis)
    assert chunks.shape[0] == size and size & (size - 1) == 0
    me = lax.axis_index(axis)
    data = chunks
    mask = 1
    while mask < size:
        bit = (me // mask) % 2
        pairs = data.reshape((data.shape[0] // 2, 2) + data.shape[1:])
        keep = lax.dynamic_index_in_dim(pairs, bit, axis=1, keepdims=False)
        give = lax.dynamic_index_in_dim(pairs, 1 - bit, axis=1, keepdims=False)
        perm = [(j, j ^ mask) for j in range(size)]
        data = keep.astype(jnp.float32) + lax.ppermute(give, axis, perm).astype(jnp.float32)
        mask *= 2
    return data[0]


def fsdp_ring(mesh):
    count = mesh.shape["fsdp"]
    try:
        members = [mesh.devices[j, 0] for j in range(count)]
        spots = [(d.coords[2], d.coords[1]) for d in members]
        zs = sorted({z for z, _ in spots})
        ys = sorted({y for _, y in spots})
        rows_a, cols_b = len(zs), len(ys)
        where = {(zs.index(z), ys.index(y)): j for j, (z, y) in enumerate(spots)}
        assert len(where) == count == rows_a * cols_b and rows_a % 2 == 0 and cols_b >= 2
        cells = [(a, 0) for a in range(rows_a)]
        for k, a in enumerate(range(rows_a - 1, -1, -1)):
            span = range(1, cols_b) if k % 2 == 0 else range(cols_b - 1, 0, -1)
            cells += [(a, b) for b in span]
        ring = [where[c] for c in cells]
        assert sorted(ring) == list(range(count))
    except Exception:
        ring = list(range(count))
    return ring


def ring_all_gather(block, axis, ring, held=None):
    count = len(ring)
    place = [0] * count
    for k, j in enumerate(ring):
        place[j] = k
    ring_arr = jnp.array(ring, jnp.int32)
    me = lax.axis_index(axis)
    spot = jnp.array(place, jnp.int32)[me]
    forward = [(ring[k], ring[(k + 1) % count]) for k in range(count)]
    backward = [(ring[k], ring[(k - 1) % count]) for k in range(count)]
    ahead = count // 2
    behind = count - 1 - ahead
    gathered = jnp.zeros((count,) + block.shape, block.dtype)
    gathered = lax.dynamic_update_index_in_dim(gathered, block, me, 0)
    cw = block
    ccw = block
    split = count % 2 == 0 and count > 2
    for s in range(1, ahead + 1):
        if split and s == ahead:
            half = block.shape[-1] // 2
            cw = jnp.concatenate(
                [
                    lax.ppermute(cw[..., :half], axis, forward),
                    lax.ppermute(ccw[..., half:], axis, backward),
                ],
                axis=-1,
            )
            gathered = lax.dynamic_update_index_in_dim(
                gathered, cw, ring_arr[(spot - s) % count], 0
            )
            break
        cw = lax.ppermute(cw, axis, forward)
        if s <= behind:
            ccw = lax.ppermute(ccw, axis, backward)
        if s == 1 and held is not None:
            cw, ccw, held = lax.optimization_barrier((cw, ccw, held))
        gathered = lax.dynamic_update_index_in_dim(gathered, cw, ring_arr[(spot - s) % count], 0)
        if s <= behind:
            gathered = lax.dynamic_update_index_in_dim(
                gathered, ccw, ring_arr[(spot + s) % count], 0
            )
    return gathered.reshape((count * block.shape[0],) + block.shape[1:]), held


def ring_reduce_scatter(terms, axis, ring):
    count = len(ring)
    place = [0] * count
    for k, j in enumerate(ring):
        place[j] = k
    ring_arr = jnp.array(ring, jnp.int32)
    me = lax.axis_index(axis)
    spot = jnp.array(place, jnp.int32)[me]
    forward = [(ring[k], ring[(k + 1) % count]) for k in range(count)]
    backward = [(ring[k], ring[(k - 1) % count]) for k in range(count)]
    ahead = count // 2
    behind = count - 1 - ahead

    def term(offset):
        return lax.dynamic_index_in_dim(terms, ring_arr[(spot + offset) % count], 0, keepdims=False)

    total = term(0).astype(jnp.float32)
    cw = term(ahead)
    ccw = term(-behind) if behind else None
    for s in range(1, ahead + 1):
        cw = lax.ppermute(cw, axis, forward)
        if s <= behind:
            ccw = lax.ppermute(ccw, axis, backward)
        if s < ahead:
            cw = (cw.astype(jnp.float32) + term(ahead - s).astype(jnp.float32)).astype(terms.dtype)
        else:
            total = total + cw.astype(jnp.float32)
        if s < behind:
            ccw = (ccw.astype(jnp.float32) + term(s - behind).astype(jnp.float32)).astype(terms.dtype)
        elif s == behind:
            total = total + ccw.astype(jnp.float32)
    return total


def tree_all_gather(block, axis):
    size = lax.axis_size(axis)
    assert size & (size - 1) == 0
    me = lax.axis_index(axis)
    data = block[None]
    mask = 1
    while mask < size:
        bit = (me // mask) % 2
        perm = [(j, j ^ mask) for j in range(size)]
        other = lax.ppermute(data, axis, perm)
        data = jnp.where(bit == 0, jnp.concatenate([data, other]), jnp.concatenate([other, data]))
        mask *= 2
    return data.reshape((size * block.shape[0],) + block.shape[1:])


def conv_rows(framed, kern, kbias):
    rows = framed.shape[0] - 6
    cols = framed.shape[1]
    wide = jnp.pad(framed, ((0, 0), (3, 3), (0, 0)))
    total = jnp.zeros((rows, cols, framed.shape[2]), jnp.float32) + kbias
    for i in range(kern.shape[0]):
        for j in range(kern.shape[1]):
            total = total + wide[i : i + rows, j : j + cols].astype(jnp.float32) * kern[i, j]
    return total


def back_conv(grad_pad, kern):
    rows = grad_pad.shape[0] - 6
    cols = grad_pad.shape[1]
    wide = jnp.pad(grad_pad, ((0, 0), (3, 3), (0, 0)))
    total = jnp.zeros((rows, cols, grad_pad.shape[2]), jnp.float32)
    for i in range(kern.shape[0]):
        for j in range(kern.shape[1]):
            total = (
                total
                + wide[6 - i : 6 - i + rows, 6 - j : 6 - j + cols].astype(jnp.float32) * kern[i, j]
            )
    return total


def kern_grad(framed, grad_rows):
    rows = grad_rows.shape[0]
    cols = grad_rows.shape[1]
    wide = jnp.pad(framed, ((0, 0), (3, 3), (0, 0)))
    grad_f = grad_rows.astype(jnp.float32)
    parts = []
    for i in range(7):
        for j in range(7):
            parts.append(
                jnp.sum(wide[i : i + rows, j : j + cols].astype(jnp.float32) * grad_f, axis=(0, 1))
            )
    return jnp.stack(parts).reshape(7, 7, grad_rows.shape[2])


def apply_layer_norm(activation_rows, scale_factor, offset_bias):
    centered_input = activation_rows - jnp.mean(activation_rows, axis=-1, keepdims=True)
    inverse_deviation = lax.rsqrt(
        jnp.mean(centered_input * centered_input, axis=-1, keepdims=True) + 1e-06
    )
    standardized_input = centered_input * inverse_deviation
    return (
        (standardized_input * scale_factor + offset_bias).astype(jnp.bfloat16),
        standardized_input,
        inverse_deviation,
    )


def gelu_grad(value):
    return (
        0.5 * (1.0 + jax.scipy.special.erf(value * 0.7071067811865476))
        + value * jnp.exp(-0.5 * value * value) * 0.3989422804014327
    )


def layer_norm_backward(normed_input_gradient, scale_factor, standardized_input, inverse_deviation):
    scaled_output = normed_input_gradient * scale_factor
    return (
        inverse_deviation
        * (
            scaled_output
            - jnp.mean(scaled_output, axis=-1, keepdims=True)
            - standardized_input
            * jnp.mean(scaled_output * standardized_input, axis=-1, keepdims=True)
        )
    ).astype(jnp.bfloat16)


def body(
    ring,
    frames,
    kernel,
    kernel_bias,
    layer_norm_weight,
    layer_norm_bias,
    up_weight,
    up_bias,
    grn_gamma,
    grn_beta,
    grad_out,
):
    slab = frames[0]
    chans = slab.shape[2]
    staged = jnp.where(up_weight == up_weight, up_weight, jnp.zeros_like(up_weight))
    columns, _ = ring_all_gather(staged, "fsdp", ring)
    padded = extended(slab, (("rows", 0),), 3)
    activation_rows = conv_rows(padded, kernel, kernel_bias)
    normed_output, standardized_input, inverse_deviation = apply_layer_norm(
        activation_rows, layer_norm_weight, layer_norm_bias
    )
    whole = tree_all_gather(normed_output, "rows")
    height = whole.shape[0]
    cols = whole.shape[1]
    flat = whole.reshape(-1, chans)
    pre = jnp.dot(flat, columns, preferred_element_type=jnp.float32) + up_bias
    post = jax.nn.gelu(pre, approximate=False)
    norms = jnp.sqrt(jnp.sum(post * post, axis=0) + 1e-06)
    cot_f = grad_out[0].reshape(flat.shape[0], -1).astype(jnp.float32)
    dnorm = grn_gamma * jnp.sum(cot_f * post, axis=0)
    norm_total = lax.psum(jnp.sum(norms), "rows")
    denom = norm_total / FF + 1e-06
    ratio = norms / denom
    output = (grn_gamma * (post * ratio) + grn_beta + post).astype(jnp.bfloat16)
    cross = lax.psum(jnp.sum(dnorm * norms), "rows")
    dnorms = dnorm / denom - cross / (denom * denom) / FF
    dpost = cot_f * (1.0 + grn_gamma * ratio) + post * (dnorms / norms)
    dpre = (dpost * gelu_grad(pre)).astype(jnp.bfloat16)
    w_term = lax.dot_general(
        flat, dpre, (((0,), (0,)), ((), ())), preferred_element_type=jnp.float32
    )
    up_grad = lax.psum_scatter(
        w_term.astype(jnp.bfloat16), "fsdp", scatter_dimension=0, tiled=True
    ).astype(jnp.float32)
    dpre_rows = dpre.reshape(height, cols, -1)
    group_terms = jnp.einsum(
        "hwf,cf->hwc", dpre_rows, columns, preferred_element_type=jnp.float32
    ).astype(jnp.bfloat16)
    n_rows = lax.axis_size("rows")
    normed_input_gradient = tree_reduce_scatter(
        group_terms.reshape((n_rows, height // n_rows) + group_terms.shape[1:]), "rows"
    )
    activation_gradient = layer_norm_backward(
        normed_input_gradient, layer_norm_weight, standardized_input, inverse_deviation
    )
    grad_pad = extended(activation_gradient, (("rows", 0),), 3)
    dframe = back_conv(grad_pad, kernel).astype(jnp.bfloat16)
    kernel_local = kern_grad(padded, activation_gradient)
    kernel_total = tree_allreduce(kernel_local, ("rows", "fsdp"))
    activation = output.reshape(1, height, cols, -1)
    return (activation, dframe.reshape((1,) + dframe.shape), up_grad, kernel_total)


def solution(mesh):
    placed = (
        P("fsdp", "rows", None, None),
        P(),
        P(),
        P(),
        P(),
        P("fsdp", "rows"),
        P("rows"),
        P("rows"),
        P("rows"),
        P("fsdp", None, None, "rows"),
    )
    return jax.shard_map(
        functools.partial(body, fsdp_ring(mesh)),
        mesh=mesh,
        in_specs=placed,
        out_specs=(
            P("fsdp", None, None, "rows"),
            P("fsdp", "rows", None, None),
            P("fsdp", "rows"),
            P(),
        ),
        check_vma=False,
    )
```

```python
import functools

import jax
import jax.numpy as jnp
from jax import lax
from jax.sharding import PartitionSpec as P

FF = 6144


def extended(block, sides, width):
    for axis, dim in sides:
        count = lax.axis_size(axis)
        forward = [(i, i + 1) for i in range(count - 1)]
        backward = [(target, source) for source, target in forward]
        low = lax.ppermute(
            lax.slice_in_dim(block, block.shape[dim] - width, None, axis=dim), axis, forward
        )
        high = lax.ppermute(lax.slice_in_dim(block, 0, width, axis=dim), axis, backward)
        block = jnp.concatenate([low, block, high], axis=dim)
    return block


def _bit_steps(axes):
    steps = []
    for axis in axes:
        size = lax.axis_size(axis)
        assert size & (size - 1) == 0
        mask = 1
        while mask < size:
            steps.append((axis, mask, size))
            mask *= 2
    return steps


def tree_allreduce(value, axes):
    shape = value.shape
    flat = value.reshape(-1)
    steps = _bit_steps(axes)
    assert flat.shape[0] % (1 << len(steps)) == 0
    bits = []
    for axis, mask, size in steps:
        bit = (lax.axis_index(axis) // mask) % 2
        bits.append(bit)
        halves = flat.reshape(2, -1)
        keep = lax.dynamic_index_in_dim(halves, bit, keepdims=False)
        give = lax.dynamic_index_in_dim(halves, 1 - bit, keepdims=False)
        perm = [(j, j ^ mask) for j in range(size)]
        flat = keep + lax.ppermute(give, axis, perm)
    for (axis, mask, size), bit in reversed(list(zip(steps, bits))):
        perm = [(j, j ^ mask) for j in range(size)]
        other = lax.ppermute(flat, axis, perm)
        flat = jnp.where(bit == 0, jnp.concatenate([flat, other]), jnp.concatenate([other, flat]))
    return flat.reshape(shape)


def tree_reduce_scatter(chunks, axis):
    size = lax.axis_size(axis)
    assert chunks.shape[0] == size and size & (size - 1) == 0
    me = lax.axis_index(axis)
    data = chunks
    mask = 1
    while mask < size:
        bit = (me // mask) % 2
        pairs = data.reshape((data.shape[0] // 2, 2) + data.shape[1:])
        keep = lax.dynamic_index_in_dim(pairs, bit, axis=1, keepdims=False)
        give = lax.dynamic_index_in_dim(pairs, 1 - bit, axis=1, keepdims=False)
        perm = [(j, j ^ mask) for j in range(size)]
        data = keep.astype(jnp.float32) + lax.ppermute(give, axis, perm).astype(jnp.float32)
        mask *= 2
    return data[0]


def fsdp_ring(mesh):
    count = mesh.shape["fsdp"]
    try:
        members = [mesh.devices[j, 0] for j in range(count)]
        spots = [(d.coords[2], d.coords[1]) for d in members]
        zs = sorted({z for z, _ in spots})
        ys = sorted({y for _, y in spots})
        rows_a, cols_b = len(zs), len(ys)
        where = {(zs.index(z), ys.index(y)): j for j, (z, y) in enumerate(spots)}
        assert len(where) == count == rows_a * cols_b and rows_a % 2 == 0 and cols_b >= 2
        cells = [(a, 0) for a in range(rows_a)]
        for k, a in enumerate(range(rows_a - 1, -1, -1)):
            span = range(1, cols_b) if k % 2 == 0 else range(cols_b - 1, 0, -1)
            cells += [(a, b) for b in span]
        ring = [where[c] for c in cells]
        assert sorted(ring) == list(range(count))
    except Exception:
        ring = list(range(count))
    return ring


def ring_all_gather(block, axis, ring, held=None):
    count = len(ring)
    place = [0] * count
    for k, j in enumerate(ring):
        place[j] = k
    ring_arr = jnp.array(ring, jnp.int32)
    me = lax.axis_index(axis)
    spot = jnp.array(place, jnp.int32)[me]
    forward = [(ring[k], ring[(k + 1) % count]) for k in range(count)]
    backward = [(ring[k], ring[(k - 1) % count]) for k in range(count)]
    ahead = count // 2
    behind = count - 1 - ahead
    gathered = jnp.zeros((count,) + block.shape, block.dtype)
    gathered = lax.dynamic_update_index_in_dim(gathered, block, me, 0)
    cw = block
    ccw = block
    split = count % 2 == 0 and count > 2
    for s in range(1, ahead + 1):
        if split and s == ahead:
            half = block.shape[-1] // 2
            cw = jnp.concatenate(
                [
                    lax.ppermute(cw[..., :half], axis, forward),
                    lax.ppermute(ccw[..., half:], axis, backward),
                ],
                axis=-1,
            )
            gathered = lax.dynamic_update_index_in_dim(
                gathered, cw, ring_arr[(spot - s) % count], 0
            )
            break
        cw = lax.ppermute(cw, axis, forward)
        if s <= behind:
            ccw = lax.ppermute(ccw, axis, backward)
        if s == 1 and held is not None:
            cw, held = lax.optimization_barrier((cw, held))
        gathered = lax.dynamic_update_index_in_dim(gathered, cw, ring_arr[(spot - s) % count], 0)
        if s <= behind:
            gathered = lax.dynamic_update_index_in_dim(
                gathered, ccw, ring_arr[(spot + s) % count], 0
            )
    return gathered.reshape((count * block.shape[0],) + block.shape[1:]), held


def ring_reduce_scatter(terms, axis, ring):
    count = len(ring)
    place = [0] * count
    for k, j in enumerate(ring):
        place[j] = k
    ring_arr = jnp.array(ring, jnp.int32)
    me = lax.axis_index(axis)
    spot = jnp.array(place, jnp.int32)[me]
    forward = [(ring[k], ring[(k + 1) % count]) for k in range(count)]
    backward = [(ring[k], ring[(k - 1) % count]) for k in range(count)]
    ahead = count // 2
    behind = count - 1 - ahead

    def term(offset):
        return lax.dynamic_index_in_dim(terms, ring_arr[(spot + offset) % count], 0, keepdims=False)

    total = term(0).astype(jnp.float32)
    cw = term(ahead)
    ccw = term(-behind) if behind else None
    for s in range(1, ahead + 1):
        cw = lax.ppermute(cw, axis, forward)
        if s <= behind:
            ccw = lax.ppermute(ccw, axis, backward)
        if s < ahead:
            cw = (cw.astype(jnp.float32) + term(ahead - s).astype(jnp.float32)).astype(terms.dtype)
        else:
            total = total + cw.astype(jnp.float32)
        if s < behind:
            ccw = (ccw.astype(jnp.float32) + term(s - behind).astype(jnp.float32)).astype(terms.dtype)
        elif s == behind:
            total = total + ccw.astype(jnp.float32)
    return total


def tree_all_gather(block, axis):
    size = lax.axis_size(axis)
    assert size & (size - 1) == 0
    me = lax.axis_index(axis)
    data = block[None]
    mask = 1
    while mask < size:
        bit = (me // mask) % 2
        perm = [(j, j ^ mask) for j in range(size)]
        other = lax.ppermute(data, axis, perm)
        data = jnp.where(bit == 0, jnp.concatenate([data, other]), jnp.concatenate([other, data]))
        mask *= 2
    return data.reshape((size * block.shape[0],) + block.shape[1:])


def conv_rows(framed, kern, kbias):
    rows = framed.shape[0] - 6
    cols = framed.shape[1]
    wide = jnp.pad(framed, ((0, 0), (3, 3), (0, 0)))
    total = jnp.zeros((rows, cols, framed.shape[2]), jnp.float32) + kbias
    for i in range(kern.shape[0]):
        for j in range(kern.shape[1]):
            total = total + wide[i : i + rows, j : j + cols].astype(jnp.float32) * kern[i, j]
    return total


def back_conv(grad_pad, kern):
    rows = grad_pad.shape[0] - 6
    cols = grad_pad.shape[1]
    wide = jnp.pad(grad_pad, ((0, 0), (3, 3), (0, 0)))
    total = jnp.zeros((rows, cols, grad_pad.shape[2]), jnp.float32)
    for i in range(kern.shape[0]):
        for j in range(kern.shape[1]):
            total = (
                total
                + wide[6 - i : 6 - i + rows, 6 - j : 6 - j + cols].astype(jnp.float32) * kern[i, j]
            )
    return total


def kern_grad(framed, grad_rows):
    rows = grad_rows.shape[0]
    cols = grad_rows.shape[1]
    wide = jnp.pad(framed, ((0, 0), (3, 3), (0, 0)))
    grad_f = grad_rows.astype(jnp.float32)
    parts = []
    for i in range(7):
        for j in range(7):
            parts.append(
                jnp.sum(wide[i : i + rows, j : j + cols].astype(jnp.float32) * grad_f, axis=(0, 1))
            )
    return jnp.stack(parts).reshape(7, 7, grad_rows.shape[2])


def apply_layer_norm(activation_rows, scale_factor, offset_bias):
    centered_input = activation_rows - jnp.mean(activation_rows, axis=-1, keepdims=True)
    inverse_deviation = lax.rsqrt(
        jnp.mean(centered_input * centered_input, axis=-1, keepdims=True) + 1e-06
    )
    standardized_input = centered_input * inverse_deviation
    return (
        (standardized_input * scale_factor + offset_bias).astype(jnp.bfloat16),
        standardized_input,
        inverse_deviation,
    )


def gelu_grad(value):
    return (
        0.5 * (1.0 + jax.scipy.special.erf(value * 0.7071067811865476))
        + value * jnp.exp(-0.5 * value * value) * 0.3989422804014327
    )


def layer_norm_backward(normed_input_gradient, scale_factor, standardized_input, inverse_deviation):
    scaled_output = normed_input_gradient * scale_factor
    return (
        inverse_deviation
        * (
            scaled_output
            - jnp.mean(scaled_output, axis=-1, keepdims=True)
            - standardized_input
            * jnp.mean(scaled_output * standardized_input, axis=-1, keepdims=True)
        )
    ).astype(jnp.bfloat16)


def body(
    ring,
    frames,
    kernel,
    kernel_bias,
    layer_norm_weight,
    layer_norm_bias,
    up_weight,
    up_bias,
    grn_gamma,
    grn_beta,
    grad_out,
):
    slab = frames[0]
    chans = slab.shape[2]
    staged = jnp.where(up_weight == up_weight, up_weight, jnp.zeros_like(up_weight))
    columns, slab = ring_all_gather(staged, "fsdp", ring, slab)
    padded = extended(slab, (("rows", 0),), 3)
    activation_rows = conv_rows(padded, kernel, kernel_bias)
    normed_output, standardized_input, inverse_deviation = apply_layer_norm(
        activation_rows, layer_norm_weight, layer_norm_bias
    )
    whole = tree_all_gather(normed_output, "rows")
    height = whole.shape[0]
    cols = whole.shape[1]
    flat = whole.reshape(-1, chans)
    pre = jnp.dot(flat, columns, preferred_element_type=jnp.float32) + up_bias
    post = jax.nn.gelu(pre, approximate=False)
    norms = jnp.sqrt(jnp.sum(post * post, axis=0) + 1e-06)
    cot_f = grad_out[0].reshape(flat.shape[0], -1).astype(jnp.float32)
    dnorm = grn_gamma * jnp.sum(cot_f * post, axis=0)
    norm_total = lax.psum(jnp.sum(norms), "rows")
    denom = norm_total / FF + 1e-06
    ratio = norms / denom
    output = (grn_gamma * (post * ratio) + grn_beta + post).astype(jnp.bfloat16)
    cross = lax.psum(jnp.sum(dnorm * norms), "rows")
    dnorms = dnorm / denom - cross / (denom * denom) / FF
    dpost = cot_f * (1.0 + grn_gamma * ratio) + post * (dnorms / norms)
    dpre = (dpost * gelu_grad(pre)).astype(jnp.bfloat16)
    w_term = lax.dot_general(
        flat, dpre, (((0,), (0,)), ((), ())), preferred_element_type=jnp.float32
    )
    up_grad = lax.psum_scatter(
        w_term.astype(jnp.bfloat16), "fsdp", scatter_dimension=0, tiled=True
    ).astype(jnp.float32)
    dpre_rows = dpre.reshape(height, cols, -1)
    group_terms = jnp.einsum(
        "hwf,cf->hwc", dpre_rows, columns, preferred_element_type=jnp.float32
    ).astype(jnp.bfloat16)
    n_rows = lax.axis_size("rows")
    normed_input_gradient = tree_reduce_scatter(
        group_terms.reshape((n_rows, height // n_rows) + group_terms.shape[1:]), "rows"
    )
    activation_gradient = layer_norm_backward(
        normed_input_gradient, layer_norm_weight, standardized_input, inverse_deviation
    )
    grad_pad = extended(activation_gradient, (("rows", 0),), 3)
    dframe = back_conv(grad_pad, kernel).astype(jnp.bfloat16)
    kernel_local = kern_grad(padded, activation_gradient)
    kernel_total = tree_allreduce(kernel_local, ("rows", "fsdp"))
    activation = output.reshape(1, height, cols, -1)
    return (activation, dframe.reshape((1,) + dframe.shape), up_grad, kernel_total)


def solution(mesh):
    placed = (
        P("fsdp", "rows", None, None),
        P(),
        P(),
        P(),
        P(),
        P("fsdp", "rows"),
        P("rows"),
        P("rows"),
        P("rows"),
        P("fsdp", None, None, "rows"),
    )
    return jax.shard_map(
        functools.partial(body, fsdp_ring(mesh)),
        mesh=mesh,
        in_specs=placed,
        out_specs=(
            P("fsdp", None, None, "rows"),
            P("fsdp", "rows", None, None),
            P("fsdp", "rows"),
            P(),
        ),
        check_vma=False,
    )
```
